32 devices in a mesh: row: 8 (over z, y), col: 4 (over x, core).
Axes of the slice: x: 2, y: 2, z: 4, core: 2. Of those that a mesh axis runs over, the one named last changes fastest.
Arguments:
- tokens: bfloat16 [1024, 4096], P('row'), may hold values from -6 to 6
- in_weight: bfloat16 [4096, 8192], P('row', 'col'), may hold values from -0.09375 to 0.09375
- gate_branch: bfloat16 [1024, 8192], P('row', 'col'), may hold values from -6 to 6
- conv_weight: float32 [4, 8192], P(None, 'col'), may hold values from -3 to 3
- out_weight: bfloat16 [8192, 4096], P('col'), may hold values from -0.0625 to 0.0625
- target: bfloat16 [1024, 4096], P('row'), may hold values from -6 to 6
- lang_ids: int32 [1024], P('row'), may hold values from 0 to 31
- lang_weight: float32 [32], replicated, may hold values from 0.25 to 4
- doc_pos: int32 [1024], P('row'), may hold values from 0 to 127, as said below
Outputs:
- block_out: bfloat16 [1024, 4096], P('row', 'col')
- grad_tokens: bfloat16 [1024, 4096], P('row', 'col')
- grad_gate: bfloat16 [1024, 8192], P('row', 'col')
The draws below stay inside these ranges and needn't reach their ends.
Inputs may be any that keep to these rules, and one draw needn't show every extreme that they name: doc_pos is 0 at the first token and at every document's first token, and otherwise one more than the previous token's; no document is longer than 128 tokens and one is exactly 128 tokens long; apart from token 0, no document begins within the first 4 tokens of an aligned block of 128 tokens.
All inputs are finite; a program needn't handle non-finite values.
Results may differ from the reference program's by a relative error of at most 0.022.
Values may be sent and summed in bfloat16 or wider, within the bound.
No kernel may reach another device: no remote copies, remote signals or barrier semaphores. Data moves between devices by JAX's collectives and lax.ppermute only.
A program may use at most 128 MiB of HBM per device.

```python
import math
import jax
import jax.numpy as jnp
from jax import lax

D = 4096
INNER = 8192
CONV = 4
LANGS = 32
DOC_SPAN = 128
TOK_ROW = 128
TOKENS = 1024
N_COL = 4


def draw_doc_pos(key, part):
    places = jnp.arange(TOKENS, dtype=jnp.int32)
    phase = jax.random.randint(jax.random.fold_in(key, 1), (), CONV, DOC_SPAN).astype(jnp.int32)
    relative = places - phase
    after = relative >= 0
    forced = jnp.logical_and(after, jnp.remainder(jnp.maximum(relative, 0), DOC_SPAN) == 0)
    random_starts = jax.random.randint(jax.random.fold_in(key, 2), (TOKENS,), 0, max(DOC_SPAN // 4, 2)) == 0
    random_starts = jnp.logical_and(random_starts, jnp.remainder(places, TOK_ROW) >= CONV)
    inside_full = jnp.logical_and(after, relative < DOC_SPAN)
    random_starts = jnp.logical_and(random_starts, jnp.logical_not(inside_full))
    starts = jnp.logical_or(jnp.logical_or(forced, random_starts), places == 0)
    marked = jnp.where(starts, places, jnp.zeros_like(places))
    latest = lax.cummax(marked, axis=0)
    return (places - latest).astype(jnp.int32)


def touch_ends(result, key, least, largest):
    longest = result.shape.index(max(result.shape))
    spots = []
    for shift in (0, 1):
        where = [jax.random.randint(jax.random.fold_in(key, axis), (), 0, length) for axis, length in enumerate(result.shape)]
        where[longest] = (where[longest] + shift) % result.shape[longest]
        spots.append(tuple(where))
    return result.at[spots[0]].set(least).at[spots[1]].set(largest)


def block_scale(own_key, extent, split, least, largest):
    factor_of, own = 1.0, jax.random.fold_in(own_key, 6)
    for dim, parts in split:
        draws = jnp.exp(jax.random.uniform(jax.random.fold_in(own, dim), (parts,), jnp.float32, least / len(split), largest / len(split)))
        factor_of = factor_of * jnp.repeat(draws, extent[dim] // parts).reshape([-1 if axis == dim else 1 for axis in range(len(extent))])
    return factor_of


def gaussian(rng, shape, scale, bound, split=(), kind=jnp.bfloat16):
    entries = jax.random.normal(rng, shape, jnp.float32) * scale
    if len(split) > 0:
        entries = block_scale(rng, shape, split, -0.22, 0.18) * entries
    return jnp.clip(entries, min=-bound, max=bound).astype(kind)


def setup_inputs(seed: int = 0) -> dict:
    streams_of = jax.random.split(jax.random.key(seed), 10)
    tokens = gaussian(streams_of[0], (TOKENS, D), 1.0, 6.0, ((0, 8),))
    in_weight = gaussian(streams_of[1], (D, INNER), D ** -0.5, 0.09375, ((0, 8), (1, 4)))
    gate_branch = gaussian(streams_of[2], (TOKENS, INNER), 1.0, 6.0, ((0, 8), (1, 4)))
    conv_weight = gaussian(streams_of[3], (CONV, INNER), 0.6, 3.0, ((1, 4),), jnp.float32)
    out_weight = gaussian(streams_of[4], (INNER, D), INNER ** -0.5, 0.0625, ((0, 4),))
    target = gaussian(streams_of[5], (TOKENS, D), 1.0, 6.0, ((0, 8),))
    lang_ids = touch_ends(jax.random.randint(streams_of[6], (TOKENS,), 0, LANGS), jax.random.fold_in(streams_of[6], 1), 0, LANGS - 1).astype(jnp.int32)
    lang_weight = jnp.clip(jnp.exp(jax.random.uniform(streams_of[7], (LANGS,), jnp.float32, math.log(0.25), math.log(4.0))), 0.25, 4.0)
    doc_pos = draw_doc_pos(jax.random.fold_in(streams_of[9], 71), 0)
    return {"tokens": tokens, "in_weight": in_weight, "gate_branch": gate_branch, "conv_weight": conv_weight, "out_weight": out_weight, "target": target, "lang_ids": lang_ids, "lang_weight": lang_weight, "doc_pos": doc_pos}


def silu_grad(argument):
    sigmoid_v = jax.nn.sigmoid(argument)
    return sigmoid_v * (1.0 + argument * (1.0 - sigmoid_v))

def reference(tokens, in_weight, gate_branch, conv_weight, out_weight, target, lang_ids, lang_weight, doc_pos):
    inner_x = jnp.dot(tokens, in_weight, preferred_element_type=jnp.float32).astype(jnp.bfloat16)
    inner_f = inner_x.astype(jnp.float32)
    row_count = inner_f.shape[0]
    inner_width = inner_f.shape[1]
    conv_sum = jnp.zeros((row_count, inner_width), jnp.float32)
    for offset in range(CONV):
        keep_mask = (doc_pos >= offset).astype(jnp.float32)[:, None]
        if offset == 0:
            shifted = inner_f
        else:
            shifted = jnp.concatenate([jnp.zeros((offset, inner_width), jnp.float32), inner_f[:row_count - offset]], axis=0)
        conv_sum = conv_sum + conv_weight[offset][None, :] * shifted * keep_mask
    gate_value = gate_branch.astype(jnp.float32)
    gate_act = jax.nn.silu(gate_value)
    conv_act = jax.nn.silu(conv_sum)
    mixed = (conv_act * gate_act).astype(jnp.bfloat16)
    block_cols = INNER // N_COL
    out_total = jnp.zeros((row_count, D), jnp.float32)
    for block in range(N_COL):
        piece = jnp.dot(mixed[:, block * block_cols:(block + 1) * block_cols], out_weight[block * block_cols:(block + 1) * block_cols], preferred_element_type=jnp.float32)
        piece = lax.optimization_barrier(piece.astype(jnp.bfloat16))
        out_total = out_total + piece.astype(jnp.float32)
    block_out = out_total.astype(jnp.bfloat16)
    token_weight = lang_weight[lang_ids][:, None]
    residual_grad = (token_weight * (out_total - target.astype(jnp.float32))).astype(jnp.bfloat16)
    grad_mixed = lax.dot_general(residual_grad, out_weight, (((1,), (1,)), ((), ())), preferred_element_type=jnp.float32)
    grad_conv = grad_mixed * gate_act * silu_grad(conv_sum)
    grad_gate = (grad_mixed * conv_act * silu_grad(gate_value)).astype(jnp.bfloat16)
    grad_acc = jnp.zeros((row_count, inner_width), jnp.float32)
    for offset in range(CONV):
        masked = conv_weight[offset][None, :] * grad_conv * (doc_pos >= offset).astype(jnp.float32)[:, None]
        if offset == 0:
            grad_acc = grad_acc + masked
        else:
            grad_acc = grad_acc + jnp.concatenate([masked[offset:], jnp.zeros((offset, inner_width), jnp.float32)], axis=0)
    grad_x = grad_acc.astype(jnp.bfloat16)
    grad_total = jnp.zeros((row_count, D), jnp.float32)
    for block in range(N_COL):
        piece = lax.dot_general(grad_x[:, block * block_cols:(block + 1) * block_cols], in_weight[:, block * block_cols:(block + 1) * block_cols], (((1,), (1,)), ((), ())), preferred_element_type=jnp.float32)
        piece = lax.optimization_barrier(piece.astype(jnp.bfloat16))
        grad_total = grad_total + piece.astype(jnp.float32)
    return (block_out, grad_total.astype(jnp.bfloat16), grad_gate)
```

```python
import jax
import jax.numpy as jnp
from jax import lax
from jax.sharding import PartitionSpec as P

CONV = 4
LANGS = 32


def passed_along(value, axis, steps):
    count = lax.axis_size(axis)
    first, last = (max(0, -steps), min(count, count - steps))
    return lax.ppermute(value, axis, [(source, source + steps) for source in range(first, last)])


def silu_grad(argument):
    sigmoid_v = jax.nn.sigmoid(argument)
    return sigmoid_v * (1.0 + argument * (1.0 - sigmoid_v))


def shards(
    tokens, in_weight, gate_branch, conv_weight, out_weight, target, lang_ids, lang_weight, doc_pos
):
    row_count = tokens.shape[0]
    inner_width = gate_branch.shape[1]
    margin = CONV - 1
    moves_tokens = row_count * lax.axis_size("row") < tokens.shape[1]
    if moves_tokens:
        token_cols = lax.all_to_all(tokens, "row", 1, 0, tiled=True)
        part_x = jnp.dot(token_cols, in_weight, preferred_element_type=jnp.float32)
        inner_x = lax.psum_scatter(part_x.astype(jnp.bfloat16), "row", scatter_dimension=0, tiled=True)
    else:
        full_in = lax.all_gather(in_weight, "row", axis=0, tiled=True)
        inner_x = jnp.dot(tokens, full_in, preferred_element_type=jnp.float32).astype(jnp.bfloat16)
    from_prev = passed_along(inner_x[row_count - margin :], "row", 1)
    extended = jnp.concatenate([from_prev, inner_x], axis=0).astype(jnp.float32)
    conv_sum = jnp.zeros((row_count, inner_width), jnp.float32)
    for offset in range(CONV):
        keep_mask = (doc_pos >= offset).astype(jnp.float32)[:, None]
        conv_sum = (
            conv_sum
            + conv_weight[offset][None, :]
            * extended[margin - offset : margin - offset + row_count]
            * keep_mask
        )
    gate_value = gate_branch.astype(jnp.float32)
    gate_act = jax.nn.silu(gate_value)
    conv_act = jax.nn.silu(conv_sum)
    mixed = (conv_act * gate_act).astype(jnp.bfloat16)
    partial_value = jnp.dot(mixed, out_weight, preferred_element_type=jnp.float32)
    columns = tokens.shape[1] // lax.axis_size("col")
    col_start = lax.axis_index("col") * columns
    lang_table = (lang_ids[:, None] == jnp.arange(LANGS, dtype=jnp.int32)[None, :]).astype(
        jnp.float32
    )
    token_weight = jnp.sum(lang_table * lang_weight[None, :], axis=1)[:, None]
    out_total = lax.psum(partial_value.astype(jnp.bfloat16), "col").astype(jnp.float32)
    out_block = lax.dynamic_slice_in_dim(out_total, col_start, columns, 1)
    residual_grad = (token_weight * (out_total - target.astype(jnp.float32))).astype(jnp.bfloat16)
    grad_mixed = lax.dot_general(
        residual_grad, out_weight, (((1,), (1,)), ((), ())), preferred_element_type=jnp.float32
    )
    grad_conv = grad_mixed * gate_act * silu_grad(conv_sum)
    grad_gate = (grad_mixed * conv_act * silu_grad(gate_value)).astype(jnp.bfloat16)
    local_grad = conv_weight[0][None, :] * grad_conv
    spill_over = jnp.zeros((margin, inner_width), jnp.float32)
    for offset in range(1, CONV):
        masked = (
            conv_weight[offset][None, :]
            * grad_conv
            * (doc_pos >= offset).astype(jnp.float32)[:, None]
        )
        local_grad = local_grad + jnp.concatenate(
            [masked[offset:], jnp.zeros((offset, inner_width), jnp.float32)], axis=0
        )
        spill_over = spill_over + jnp.concatenate(
            [jnp.zeros((margin - offset, inner_width), jnp.float32), masked[:offset]], axis=0
        )
    from_next = passed_along(spill_over, "row", -1)
    grad_x = (
        local_grad
        + jnp.concatenate(
            [jnp.zeros((row_count - margin, inner_width), jnp.float32), from_next], axis=0
        )
    ).astype(jnp.bfloat16)
    if moves_tokens:
        grad_x_all = lax.all_gather(grad_x, "row", axis=0, tiled=True)
        grad_cols = lax.dot_general(
            grad_x_all, in_weight, (((1,), (1,)), ((), ())), preferred_element_type=jnp.float32
        )
        partial_grad = lax.all_to_all(grad_cols.astype(jnp.bfloat16), "row", 0, 1, tiled=True)
    else:
        partial_grad = lax.dot_general(
            grad_x, full_in, (((1,), (1,)), ((), ())), preferred_element_type=jnp.float32
        )
    grad_tokens = lax.psum_scatter(
        partial_grad.astype(jnp.bfloat16), "col", scatter_dimension=1, tiled=True
    )
    return (out_block.astype(jnp.bfloat16), grad_tokens, grad_gate)


def solution(mesh):
    in_specs = (
        P("row", None),
        P("row", "col"),
        P("row", "col"),
        P(None, "col"),
        P("col", None),
        P("row", None),
        P("row"),
        P(),
        P("row"),
    )
    out_specs = (P("row", "col"), P("row", "col"), P("row", "col"))
    return jax.shard_map(shards, mesh=mesh, in_specs=in_specs, out_specs=out_specs, check_vma=False)
```

```python
import jax
import jax.numpy as jnp
from jax import lax
from jax.sharding import PartitionSpec as P

CONV = 4
LANGS = 32


def passed_along(value, axis, steps):
    count = lax.axis_size(axis)
    first, last = (max(0, -steps), min(count, count - steps))
    return lax.ppermute(value, axis, [(source, source + steps) for source in range(first, last)])


def fetched_columns(tokens):
    n_row, n_col = lax.axis_size("row"), lax.axis_size("col")
    width = tokens.shape[1] // n_row
    if n_col % 2:
        return lax.all_to_all(tokens, "row", 1, 0, tiled=True)
    core = lax.axis_index("col") % 2
    halves = tokens.reshape(tokens.shape[0], n_row, 2, width // 2)
    mine = jnp.take(halves, core, axis=2).reshape(tokens.shape[0], n_row * (width // 2))
    mine = lax.all_to_all(mine, "row", 1, 0, tiled=True)
    other = lax.ppermute(mine, "col", [(c, c ^ 1) for c in range(n_col)])
    return jnp.where(
        core == 0, jnp.concatenate([mine, other], axis=1), jnp.concatenate([other, mine], axis=1)
    )


def placed_blocks(grad_sum, row_count):
    n_row, n_col = lax.axis_size("row"), lax.axis_size("col")
    share = n_row // n_col
    row, col = lax.axis_index("row"), lax.axis_index("col")
    pieces = []
    for j in range(share):
        got = []
        for k in range(share):
            pairs = [
                (r * n_col + c, (c * share + k) * n_col + r // share)
                for r in range(n_row)
                if r % share == j
                for c in range(n_col)
            ]
            got.append(lax.ppermute(grad_sum[k * row_count : (k + 1) * row_count], ("row", "col"), pairs))
        piece = got[0]
        for k in range(1, share):
            piece = jnp.where(row % share == k, got[k], piece)
        pieces.append(piece)
    return jnp.concatenate(pieces, axis=1)


def silu_grad(argument):
    sigmoid_v = jax.nn.sigmoid(argument)
    return sigmoid_v * (1.0 + argument * (1.0 - sigmoid_v))


def shards(
    tokens, in_weight, gate_branch, conv_weight, out_weight, target, lang_ids, lang_weight, doc_pos
):
    row_count = tokens.shape[0]
    inner_width = gate_branch.shape[1]
    margin = CONV - 1
    moves_tokens = (
        row_count * lax.axis_size("row") < tokens.shape[1]
        and lax.axis_size("row") % lax.axis_size("col") == 0
    )
    if moves_tokens:
        token_cols = fetched_columns(tokens)
        part_x = jnp.dot(token_cols, in_weight, preferred_element_type=jnp.float32)
        inner_x = lax.psum_scatter(part_x.astype(jnp.bfloat16), "row", scatter_dimension=0, tiled=True)
    else:
        full_in = lax.all_gather(in_weight, "row", axis=0, tiled=True)
        inner_x = jnp.dot(tokens, full_in, preferred_element_type=jnp.float32).astype(jnp.bfloat16)
    from_prev = passed_along(inner_x[row_count - margin :], "row", 1)
    extended = jnp.concatenate([from_prev, inner_x], axis=0).astype(jnp.float32)
    conv_sum = jnp.zeros((row_count, inner_width), jnp.float32)
    for offset in range(CONV):
        keep_mask = (doc_pos >= offset).astype(jnp.float32)[:, None]
        conv_sum = (
            conv_sum
            + conv_weight[offset][None, :]
            * extended[margin - offset : margin - offset + row_count]
            * keep_mask
        )
    gate_value = gate_branch.astype(jnp.float32)
    gate_act = jax.nn.silu(gate_value)
    conv_act = jax.nn.silu(conv_sum)
    mixed = (conv_act * gate_act).astype(jnp.bfloat16)
    partial_value = jnp.dot(mixed, out_weight, preferred_element_type=jnp.float32)
    columns = tokens.shape[1] // lax.axis_size("col")
    col_start = lax.axis_index("col") * columns
    lang_table = (lang_ids[:, None] == jnp.arange(LANGS, dtype=jnp.int32)[None, :]).astype(
        jnp.float32
    )
    token_weight = jnp.sum(lang_table * lang_weight[None, :], axis=1)[:, None]
    out_total = lax.psum(partial_value.astype(jnp.bfloat16), "col").astype(jnp.float32)
    out_block = lax.dynamic_slice_in_dim(out_total, col_start, columns, 1)
    residual_grad = (token_weight * (out_total - target.astype(jnp.float32))).astype(jnp.bfloat16)
    grad_mixed = lax.dot_general(
        residual_grad, out_weight, (((1,), (1,)), ((), ())), preferred_element_type=jnp.float32
    )
    grad_conv = grad_mixed * gate_act * silu_grad(conv_sum)
    grad_gate = (grad_mixed * conv_act * silu_grad(gate_value)).astype(jnp.bfloat16)
    local_grad = conv_weight[0][None, :] * grad_conv
    spill_over = jnp.zeros((margin, inner_width), jnp.float32)
    for offset in range(1, CONV):
        masked = (
            conv_weight[offset][None, :]
            * grad_conv
            * (doc_pos >= offset).astype(jnp.float32)[:, None]
        )
        local_grad = local_grad + jnp.concatenate(
            [masked[offset:], jnp.zeros((offset, inner_width), jnp.float32)], axis=0
        )
        spill_over = spill_over + jnp.concatenate(
            [jnp.zeros((margin - offset, inner_width), jnp.float32), masked[:offset]], axis=0
        )
    from_next = passed_along(spill_over, "row", -1)
    grad_x = (
        local_grad
        + jnp.concatenate(
            [jnp.zeros((row_count - margin, inner_width), jnp.float32), from_next], axis=0
        )
    ).astype(jnp.bfloat16)
    if moves_tokens:
        grad_x_all = lax.all_gather(grad_x, "row", axis=0, tiled=True)
        grad_cols = lax.dot_general(
            grad_x_all, in_weight, (((1,), (1,)), ((), ())), preferred_element_type=jnp.float32
        )
        grad_sum = lax.psum_scatter(
            grad_cols.astype(jnp.bfloat16), "col", scatter_dimension=0, tiled=True
        )
        grad_tokens = placed_blocks(grad_sum, row_count)
    else:
        partial_grad = lax.dot_general(
            grad_x, full_in, (((1,), (1,)), ((), ())), preferred_element_type=jnp.float32
        )
        grad_tokens = lax.psum_scatter(
            partial_grad.astype(jnp.bfloat16), "col", scatter_dimension=1, tiled=True
        )
    return (out_block.astype(jnp.bfloat16), grad_tokens, grad_gate)


def solution(mesh):
    in_specs = (
        P("row", None),
        P("row", "col"),
        P("row", "col"),
        P(None, "col"),
        P("col", None),
        P("row", None),
        P("row"),
        P(),
        P("row"),
    )
    out_specs = (P("row", "col"), P("row", "col"), P("row", "col"))
    return jax.shard_map(shards, mesh=mesh, in_specs=in_specs, out_specs=out_specs, check_vma=False)
```

```python
import jax
import jax.numpy as jnp
from jax import lax
from jax.sharding import PartitionSpec as P

CONV = 4
LANGS = 32


def passed_along(value, axis, steps):
    count = lax.axis_size(axis)
    first, last = (max(0, -steps), min(count, count - steps))
    return lax.ppermute(value, axis, [(source, source + steps) for source in range(first, last)])


def fetched_columns(tokens):
    n_row, n_col = lax.axis_size("row"), lax.axis_size("col")
    width = tokens.shape[1] // n_row
    if n_col % 2:
        return lax.all_to_all(tokens, "row", 1, 0, tiled=True)
    core = lax.axis_index("col") % 2
    halves = tokens.reshape(tokens.shape[0], n_row, 2, width // 2)
    mine = jnp.take(halves, core, axis=2).reshape(tokens.shape[0], n_row * (width // 2))
    mine = lax.all_to_all(mine, "row", 1, 0, tiled=True)
    other = lax.ppermute(mine, "col", [(c, c ^ 1) for c in range(n_col)])
    return jnp.where(
        core == 0, jnp.concatenate([mine, other], axis=1), jnp.concatenate([other, mine], axis=1)
    )


def placed_blocks(grad_sum, row_count):
    n_row, n_col = lax.axis_size("row"), lax.axis_size("col")
    share = n_row // n_col
    row, col = lax.axis_index("row"), lax.axis_index("col")
    pieces = []
    for j in range(share):
        got = []
        for k in range(share):
            pairs = [
                (r * n_col + c, (c * share + k) * n_col + r // share)
                for r in range(n_row)
                if r % share == j
                for c in range(n_col)
            ]
            got.append(lax.ppermute(grad_sum[k * row_count : (k + 1) * row_count], ("row", "col"), pairs))
        piece = got[0]
        for k in range(1, share):
            piece = jnp.where(row % share == k, got[k], piece)
        pieces.append(piece)
    return jnp.concatenate(pieces, axis=1)


def ring_order(count):
    if count % 2:
        return list(range(count))
    return list(range(0, count, 2)) + list(range(count - 1, 0, -2))


def ring_gather(value, axis):
    count = lax.axis_size(axis)
    order = ring_order(count)
    place = jnp.array([order.index(i) for i in range(count)], jnp.int32)[lax.axis_index(axis)]
    ahead = [(order[i], order[(i + 1) % count]) for i in range(count)]
    behind = [(order[(i + 1) % count], order[i]) for i in range(count)]
    half = value.shape[1] // 2
    sent_a, sent_b = value[:, :half], value[:, half:]
    got_a, got_b = [sent_a], [sent_b]
    for _ in range(1, count):
        sent_a = lax.ppermute(sent_a, axis, ahead)
        sent_b = lax.ppermute(sent_b, axis, behind)
        got_a.append(sent_a)
        got_b.append(sent_b)
    steps = jnp.arange(count)
    order_arr = jnp.array(order, jnp.int32)
    from_a = jnp.argsort(order_arr[(place - steps) % count])
    from_b = jnp.argsort(order_arr[(place + steps) % count])
    gathered_a = jnp.take(jnp.stack(got_a), from_a, axis=0)
    gathered_b = jnp.take(jnp.stack(got_b), from_b, axis=0)
    return jnp.concatenate([gathered_a, gathered_b], axis=2).reshape(
        count * value.shape[0], value.shape[1]
    )


def silu_grad(argument):
    sigmoid_v = jax.nn.sigmoid(argument)
    return sigmoid_v * (1.0 + argument * (1.0 - sigmoid_v))


def shards(
    tokens, in_weight, gate_branch, conv_weight, out_weight, target, lang_ids, lang_weight, doc_pos
):
    row_count = tokens.shape[0]
    inner_width = gate_branch.shape[1]
    margin = CONV - 1
    moves_tokens = (
        row_count * lax.axis_size("row") < tokens.shape[1]
        and lax.axis_size("row") % lax.axis_size("col") == 0
    )
    if moves_tokens:
        token_cols = fetched_columns(tokens)
        part_x = jnp.dot(token_cols, in_weight, preferred_element_type=jnp.float32)
        inner_x = lax.psum_scatter(part_x.astype(jnp.bfloat16), "row", scatter_dimension=0, tiled=True)
    else:
        full_in = lax.all_gather(in_weight, "row", axis=0, tiled=True)
        inner_x = jnp.dot(tokens, full_in, preferred_element_type=jnp.float32).astype(jnp.bfloat16)
    from_prev = passed_along(inner_x[row_count - margin :], "row", 1)
    extended = jnp.concatenate([from_prev, inner_x], axis=0).astype(jnp.float32)
    conv_sum = jnp.zeros((row_count, inner_width), jnp.float32)
    for offset in range(CONV):
        keep_mask = (doc_pos >= offset).astype(jnp.float32)[:, None]
        conv_sum = (
            conv_sum
            + conv_weight[offset][None, :]
            * extended[margin - offset : margin - offset + row_count]
            * keep_mask
        )
    gate_value = gate_branch.astype(jnp.float32)
    gate_act = jax.nn.silu(gate_value)
    conv_act = jax.nn.silu(conv_sum)
    mixed = (conv_act * gate_act).astype(jnp.bfloat16)
    partial_value = jnp.dot(mixed, out_weight, preferred_element_type=jnp.float32)
    columns = tokens.shape[1] // lax.axis_size("col")
    col_start = lax.axis_index("col") * columns
    lang_table = (lang_ids[:, None] == jnp.arange(LANGS, dtype=jnp.int32)[None, :]).astype(
        jnp.float32
    )
    token_weight = jnp.sum(lang_table * lang_weight[None, :], axis=1)[:, None]
    out_total = lax.psum(partial_value.astype(jnp.bfloat16), "col").astype(jnp.float32)
    out_block = lax.dynamic_slice_in_dim(out_total, col_start, columns, 1)
    residual_grad = (token_weight * (out_total - target.astype(jnp.float32))).astype(jnp.bfloat16)
    grad_mixed = lax.dot_general(
        residual_grad, out_weight, (((1,), (1,)), ((), ())), preferred_element_type=jnp.float32
    )
    grad_conv = grad_mixed * gate_act * silu_grad(conv_sum)
    grad_gate = (grad_mixed * conv_act * silu_grad(gate_value)).astype(jnp.bfloat16)
    local_grad = conv_weight[0][None, :] * grad_conv
    spill_over = jnp.zeros((margin, inner_width), jnp.float32)
    for offset in range(1, CONV):
        masked = (
            conv_weight[offset][None, :]
            * grad_conv
            * (doc_pos >= offset).astype(jnp.float32)[:, None]
        )
        local_grad = local_grad + jnp.concatenate(
            [masked[offset:], jnp.zeros((offset, inner_width), jnp.float32)], axis=0
        )
        spill_over = spill_over + jnp.concatenate(
            [jnp.zeros((margin - offset, inner_width), jnp.float32), masked[:offset]], axis=0
        )
    from_next = passed_along(spill_over, "row", -1)
    grad_x = (
        local_grad
        + jnp.concatenate(
            [jnp.zeros((row_count - margin, inner_width), jnp.float32), from_next], axis=0
        )
    ).astype(jnp.bfloat16)
    if moves_tokens:
        grad_x_all = ring_gather(grad_x, "row")
        grad_cols = lax.dot_general(
            grad_x_all, in_weight, (((1,), (1,)), ((), ())), preferred_element_type=jnp.float32
        )
        grad_sum = lax.psum_scatter(
            grad_cols.astype(jnp.bfloat16), "col", scatter_dimension=0, tiled=True
        )
        grad_tokens = placed_blocks(grad_sum, row_count)
    else:
        partial_grad = lax.dot_general(
            grad_x, full_in, (((1,), (1,)), ((), ())), preferred_element_type=jnp.float32
        )
        grad_tokens = lax.psum_scatter(
            partial_grad.astype(jnp.bfloat16), "col", scatter_dimension=1, tiled=True
        )
    return (out_block.astype(jnp.bfloat16), grad_tokens, grad_gate)


def solution(mesh):
    in_specs = (
        P("row", None),
        P("row", "col"),
        P("row", "col"),
        P(None, "col"),
        P("col", None),
        P("row", None),
        P("row"),
        P(),
        P("row"),
    )
    out_specs = (P("row", "col"), P("row", "col"), P("row", "col"))
    return jax.shard_map(shards, mesh=mesh, in_specs=in_specs, out_specs=out_specs, check_vma=False)
```

```python
import jax
import jax.numpy as jnp
from jax import lax
from jax.sharding import PartitionSpec as P

CONV = 4
LANGS = 32


def passed_along(value, axis, steps):
    count = lax.axis_size(axis)
    first, last = (max(0, -steps), min(count, count - steps))
    return lax.ppermute(value, axis, [(source, source + steps) for source in range(first, last)])


def fetched_columns(tokens):
    n_row, n_col = lax.axis_size("row"), lax.axis_size("col")
    width = tokens.shape[1] // n_row
    if n_col % 2:
        return lax.all_to_all(tokens, "row", 1, 0, tiled=True)
    core = lax.axis_index("col") % 2
    halves = tokens.reshape(tokens.shape[0], n_row, 2, width // 2)
    mine = jnp.take(halves, core, axis=2).reshape(tokens.shape[0], n_row * (width // 2))
    mine = lax.all_to_all(mine, "row", 1, 0, tiled=True)
    other = lax.ppermute(mine, "col", [(c, c ^ 1) for c in range(n_col)])
    return jnp.where(
        core == 0, jnp.concatenate([mine, other], axis=1), jnp.concatenate([other, mine], axis=1)
    )


def placed_blocks(grad_sum, row_count):
    n_row, n_col = lax.axis_size("row"), lax.axis_size("col")
    share = n_row // n_col
    row, col = lax.axis_index("row"), lax.axis_index("col")
    pieces = []
    for j in range(share):
        got = []
        for k in range(share):
            pairs = [
                (r * n_col + c, (c * share + k) * n_col + r // share)
                for r in range(n_row)
                if r % share == j
                for c in range(n_col)
            ]
            got.append(lax.ppermute(grad_sum[k * row_count : (k + 1) * row_count], ("row", "col"), pairs))
        piece = got[0]
        for k in range(1, share):
            piece = jnp.where(row % share == k, got[k], piece)
        pieces.append(piece)
    return jnp.concatenate(pieces, axis=1)


def ring_order(count):
    if count % 2:
        return list(range(count))
    return list(range(0, count, 2)) + list(range(count - 1, 0, -2))


def ring_place(axis):
    count = lax.axis_size(axis)
    order = ring_order(count)
    place = jnp.array([order.index(i) for i in range(count)], jnp.int32)[lax.axis_index(axis)]
    ahead = [(order[i], order[(i + 1) % count]) for i in range(count)]
    behind = [(order[(i + 1) % count], order[i]) for i in range(count)]
    return count, jnp.array(order, jnp.int32), place, ahead, behind


def ring_gather(value, axis):
    count, order, place, ahead, behind = ring_place(axis)
    half = value.shape[1] // 2
    sent_a, sent_b = value[:, :half], value[:, half:]
    got_a, got_b = [sent_a], [sent_b]
    for _ in range(1, count):
        sent_a = lax.ppermute(sent_a, axis, ahead)
        sent_b = lax.ppermute(sent_b, axis, behind)
        got_a.append(sent_a)
        got_b.append(sent_b)
    got_b = [got_b[(count - s) % count] for s in range(count)]
    sources = order[(place - jnp.arange(count)) % count]
    return jnp.stack(got_a), jnp.stack(got_b), sources


def ring_reduce_scatter(token_cols, weight, axis):
    count, order, place, ahead, behind = ring_place(axis)
    rows = token_cols.shape[0] // count
    blocks = token_cols.reshape(count, rows, token_cols.shape[1])
    half = weight.shape[1] // 2
    steps = jnp.arange(count)
    first = jnp.take(blocks, order[(place - 1 - steps) % count], axis=0).reshape(token_cols.shape)
    second = jnp.take(blocks, order[(place + 1 + steps) % count], axis=0).reshape(token_cols.shape)
    own_a = jnp.dot(first, weight[:, :half], preferred_element_type=jnp.float32)
    own_b = jnp.dot(second, weight[:, half:], preferred_element_type=jnp.float32)
    own_a = own_a.reshape(count, rows, half)
    own_b = own_b.reshape(count, rows, weight.shape[1] - half)
    sum_a, sum_b = own_a[0].astype(jnp.bfloat16), own_b[0].astype(jnp.bfloat16)
    for s in range(1, count):
        sum_a = lax.ppermute(sum_a, axis, ahead)
        sum_b = lax.ppermute(sum_b, axis, behind)
        sum_a = (sum_a.astype(jnp.float32) + own_a[s]).astype(jnp.bfloat16)
        sum_b = (sum_b.astype(jnp.float32) + own_b[s]).astype(jnp.bfloat16)
    return jnp.concatenate([sum_a, sum_b], axis=1)

def silu_grad(argument):
    sigmoid_v = jax.nn.sigmoid(argument)
    return sigmoid_v * (1.0 + argument * (1.0 - sigmoid_v))


def shards(
    tokens, in_weight, gate_branch, conv_weight, out_weight, target, lang_ids, lang_weight, doc_pos
):
    row_count = tokens.shape[0]
    inner_width = gate_branch.shape[1]
    margin = CONV - 1
    moves_tokens = (
        row_count * lax.axis_size("row") < tokens.shape[1]
        and lax.axis_size("row") % lax.axis_size("col") == 0
    )
    if moves_tokens:
        inner_x = ring_reduce_scatter(fetched_columns(tokens), in_weight, "row")
    else:
        full_in = lax.all_gather(in_weight, "row", axis=0, tiled=True)
        inner_x = jnp.dot(tokens, full_in, preferred_element_type=jnp.float32).astype(jnp.bfloat16)
    from_prev = passed_along(inner_x[row_count - margin :], "row", 1)
    extended = jnp.concatenate([from_prev, inner_x], axis=0).astype(jnp.float32)
    conv_sum = jnp.zeros((row_count, inner_width), jnp.float32)
    for offset in range(CONV):
        keep_mask = (doc_pos >= offset).astype(jnp.float32)[:, None]
        conv_sum = (
            conv_sum
            + conv_weight[offset][None, :]
            * extended[margin - offset : margin - offset + row_count]
            * keep_mask
        )
    gate_value = gate_branch.astype(jnp.float32)
    gate_act = jax.nn.silu(gate_value)
    conv_act = jax.nn.silu(conv_sum)
    mixed = (conv_act * gate_act).astype(jnp.bfloat16)
    partial_value = jnp.dot(mixed, out_weight, preferred_element_type=jnp.float32)
    columns = tokens.shape[1] // lax.axis_size("col")
    col_start = lax.axis_index("col") * columns
    lang_table = (lang_ids[:, None] == jnp.arange(LANGS, dtype=jnp.int32)[None, :]).astype(
        jnp.float32
    )
    token_weight = jnp.sum(lang_table * lang_weight[None, :], axis=1)[:, None]
    out_total = lax.psum(partial_value.astype(jnp.bfloat16), "col").astype(jnp.float32)
    out_block = lax.dynamic_slice_in_dim(out_total, col_start, columns, 1)
    residual_grad = (token_weight * (out_total - target.astype(jnp.float32))).astype(jnp.bfloat16)
    grad_mixed = lax.dot_general(
        residual_grad, out_weight, (((1,), (1,)), ((), ())), preferred_element_type=jnp.float32
    )
    grad_conv = grad_mixed * gate_act * silu_grad(conv_sum)
    grad_gate = (grad_mixed * conv_act * silu_grad(gate_value)).astype(jnp.bfloat16)
    local_grad = conv_weight[0][None, :] * grad_conv
    spill_over = jnp.zeros((margin, inner_width), jnp.float32)
    for offset in range(1, CONV):
        masked = (
            conv_weight[offset][None, :]
            * grad_conv
            * (doc_pos >= offset).astype(jnp.float32)[:, None]
        )
        local_grad = local_grad + jnp.concatenate(
            [masked[offset:], jnp.zeros((offset, inner_width), jnp.float32)], axis=0
        )
        spill_over = spill_over + jnp.concatenate(
            [jnp.zeros((margin - offset, inner_width), jnp.float32), masked[:offset]], axis=0
        )
    from_next = passed_along(spill_over, "row", -1)
    grad_x = (
        local_grad
        + jnp.concatenate(
            [jnp.zeros((row_count - margin, inner_width), jnp.float32), from_next], axis=0
        )
    ).astype(jnp.bfloat16)
    if moves_tokens:
        got_a, got_b, sources = ring_gather(grad_x, "row")
        half = grad_x.shape[1] // 2
        contract = (((2,), (1,)), ((), ()))
        grad_cols = lax.dot_general(
            got_a, in_weight[:, :half], contract, preferred_element_type=jnp.float32
        ) + lax.dot_general(got_b, in_weight[:, half:], contract, preferred_element_type=jnp.float32)
        grad_cols = jnp.take(grad_cols.astype(jnp.bfloat16), jnp.argsort(sources), axis=0)
        grad_sum = lax.psum_scatter(
            grad_cols.reshape(-1, grad_cols.shape[2]), "col", scatter_dimension=0, tiled=True
        )
        grad_tokens = placed_blocks(grad_sum, row_count)
    else:
        partial_grad = lax.dot_general(
            grad_x, full_in, (((1,), (1,)), ((), ())), preferred_element_type=jnp.float32
        )
        grad_tokens = lax.psum_scatter(
            partial_grad.astype(jnp.bfloat16), "col", scatter_dimension=1, tiled=True
        )
    return (out_block.astype(jnp.bfloat16), grad_tokens, grad_gate)


def solution(mesh):
    in_specs = (
        P("row", None),
        P("row", "col"),
        P("row", "col"),
        P(None, "col"),
        P("col", None),
        P("row", None),
        P("row"),
        P(),
        P("row"),
    )
    out_specs = (P("row", "col"), P("row", "col"), P("row", "col"))
    return jax.shard_map(shards, mesh=mesh, in_specs=in_specs, out_specs=out_specs, check_vma=False)
```

```python
import jax
import jax.numpy as jnp
from jax import lax
from jax.sharding import PartitionSpec as P

CONV = 4
LANGS = 32


def passed_along(value, axis, steps):
    count = lax.axis_size(axis)
    first, last = (max(0, -steps), min(count, count - steps))
    return lax.ppermute(value, axis, [(source, source + steps) for source in range(first, last)])


def fetched_columns(tokens):
    n_row, n_col = lax.axis_size("row"), lax.axis_size("col")
    width = tokens.shape[1] // n_row
    if n_col % 2:
        return lax.all_to_all(tokens, "row", 1, 0, tiled=True)
    core = lax.axis_index("col") % 2
    halves = tokens.reshape(tokens.shape[0], n_row, 2, width // 2)
    mine = jnp.take(halves, core, axis=2).reshape(tokens.shape[0], n_row * (width // 2))
    mine = lax.all_to_all(mine, "row", 1, 0, tiled=True)
    other = lax.ppermute(mine, "col", [(c, c ^ 1) for c in range(n_col)])
    return jnp.where(
        core == 0, jnp.concatenate([mine, other], axis=1), jnp.concatenate([other, mine], axis=1)
    )


def placed_blocks(grad_sum, row_count):
    n_row, n_col = lax.axis_size("row"), lax.axis_size("col")
    share = n_row // n_col
    row, col = lax.axis_index("row"), lax.axis_index("col")
    pieces = []
    for j in range(share):
        got = []
        for k in range(share):
            pairs = [
                (r * n_col + c, (c * share + k) * n_col + r // share)
                for r in range(n_row)
                if r % share == j
                for c in range(n_col)
            ]
            got.append(lax.ppermute(grad_sum[k * row_count : (k + 1) * row_count], ("row", "col"), pairs))
        piece = got[0]
        for k in range(1, share):
            piece = jnp.where(row % share == k, got[k], piece)
        pieces.append(piece)
    return jnp.concatenate(pieces, axis=1)


def ring_order(count):
    if count % 2:
        return list(range(count))
    return list(range(0, count, 2)) + list(range(count - 1, 0, -2))


def ring_place(axis):
    count = lax.axis_size(axis)
    order = ring_order(count)
    place = jnp.array([order.index(i) for i in range(count)], jnp.int32)[lax.axis_index(axis)]
    ahead = [(order[i], order[(i + 1) % count]) for i in range(count)]
    behind = [(order[(i + 1) % count], order[i]) for i in range(count)]
    return count, jnp.array(order, jnp.int32), place, ahead, behind


def ring_gather(value, axis):
    count, order, place, ahead, behind = ring_place(axis)
    half = value.shape[1] // 2
    sent_a, sent_b = value[:, :half], value[:, half:]
    got_a, got_b = [sent_a], [sent_b]
    for _ in range(1, count):
        sent_a = lax.ppermute(sent_a, axis, ahead)
        sent_b = lax.ppermute(sent_b, axis, behind)
        got_a.append(sent_a)
        got_b.append(sent_b)
    got_b = [got_b[(count - s) % count] for s in range(count)]
    sources = order[(place - jnp.arange(count)) % count]
    return jnp.stack(got_a), jnp.stack(got_b), sources


def ring_reduce_scatter(token_cols, weight, axis):
    count, order, place, ahead, behind = ring_place(axis)
    rows = token_cols.shape[0] // count
    blocks = token_cols.reshape(count, rows, token_cols.shape[1])
    half = weight.shape[1] // 2
    steps = jnp.arange(count)
    first = jnp.take(blocks, order[(place - 1 - steps) % count], axis=0).reshape(token_cols.shape)
    second = jnp.take(blocks, order[(place + 1 + steps) % count], axis=0).reshape(token_cols.shape)
    own_a = jnp.dot(first, weight[:, :half], preferred_element_type=jnp.float32)
    own_b = jnp.dot(second, weight[:, half:], preferred_element_type=jnp.float32)
    own_a = own_a.reshape(count, rows, half)
    own_b = own_b.reshape(count, rows, weight.shape[1] - half)
    sum_a, sum_b = own_a[0].astype(jnp.bfloat16), own_b[0].astype(jnp.bfloat16)
    for s in range(1, count):
        sum_a = lax.ppermute(sum_a, axis, ahead)
        sum_b = lax.ppermute(sum_b, axis, behind)
        sum_a = (sum_a.astype(jnp.float32) + own_a[s]).astype(jnp.bfloat16)
        sum_b = (sum_b.astype(jnp.float32) + own_b[s]).astype(jnp.bfloat16)
    return jnp.concatenate([sum_a, sum_b], axis=1)

def halves_of(value, dim, upper):
    low, high = jnp.split(value, 2, axis=dim)
    return jnp.where(upper, high, low), jnp.where(upper, low, high)


def col_psum(value):
    core = lax.axis_index("col") % 2 == 1
    keep, give = halves_of(value, 1, core)
    count = lax.axis_size("col")
    got = lax.ppermute(give, "col", [(c, c ^ 1) for c in range(count)])
    pair = keep.astype(jnp.float32) + got.astype(jnp.float32)
    total = pair + lax.ppermute(
        pair.astype(jnp.bfloat16), "col", [(c, c ^ 2) for c in range(count)]
    ).astype(jnp.float32)
    other = lax.ppermute(total, "col", [(c, c ^ 1) for c in range(count)])
    return jnp.where(
        core, jnp.concatenate([other, total], axis=1), jnp.concatenate([total, other], axis=1)
    )


def col_psum_scatter(value):
    col = lax.axis_index("col")
    count = lax.axis_size("col")
    quarters = value.reshape(2, 2, value.shape[0] // 4, value.shape[1])
    keep = jnp.take(quarters, col % 2, axis=1)
    give = jnp.take(quarters, 1 - col % 2, axis=1)
    got = lax.ppermute(give, "col", [(c, c ^ 1) for c in range(count)])
    pair = keep.astype(jnp.float32) + got.astype(jnp.float32)
    mine = jnp.take(pair, col // 2, axis=0)
    theirs = jnp.take(pair, 1 - col // 2, axis=0)
    got = lax.ppermute(theirs.astype(jnp.bfloat16), "col", [(c, c ^ 2) for c in range(count)])
    return (mine + got.astype(jnp.float32)).astype(jnp.bfloat16)


def silu_grad(argument):
    sigmoid_v = jax.nn.sigmoid(argument)
    return sigmoid_v * (1.0 + argument * (1.0 - sigmoid_v))


def shards(
    tokens, in_weight, gate_branch, conv_weight, out_weight, target, lang_ids, lang_weight, doc_pos
):
    row_count = tokens.shape[0]
    inner_width = gate_branch.shape[1]
    margin = CONV - 1
    moves_tokens = (
        row_count * lax.axis_size("row") < tokens.shape[1]
        and lax.axis_size("row") % lax.axis_size("col") == 0
    )
    if moves_tokens:
        inner_x = ring_reduce_scatter(fetched_columns(tokens), in_weight, "row")
    else:
        full_in = lax.all_gather(in_weight, "row", axis=0, tiled=True)
        inner_x = jnp.dot(tokens, full_in, preferred_element_type=jnp.float32).astype(jnp.bfloat16)
    from_prev = passed_along(inner_x[row_count - margin :], "row", 1)
    extended = jnp.concatenate([from_prev, inner_x], axis=0).astype(jnp.float32)
    conv_sum = jnp.zeros((row_count, inner_width), jnp.float32)
    for offset in range(CONV):
        keep_mask = (doc_pos >= offset).astype(jnp.float32)[:, None]
        conv_sum = (
            conv_sum
            + conv_weight[offset][None, :]
            * extended[margin - offset : margin - offset + row_count]
            * keep_mask
        )
    gate_value = gate_branch.astype(jnp.float32)
    gate_act = jax.nn.silu(gate_value)
    conv_act = jax.nn.silu(conv_sum)
    mixed = (conv_act * gate_act).astype(jnp.bfloat16)
    partial_value = jnp.dot(mixed, out_weight, preferred_element_type=jnp.float32)
    columns = tokens.shape[1] // lax.axis_size("col")
    col_start = lax.axis_index("col") * columns
    lang_table = (lang_ids[:, None] == jnp.arange(LANGS, dtype=jnp.int32)[None, :]).astype(
        jnp.float32
    )
    token_weight = jnp.sum(lang_table * lang_weight[None, :], axis=1)[:, None]
    if moves_tokens and lax.axis_size("col") == 4:
        out_total = col_psum(partial_value.astype(jnp.bfloat16))
    else:
        out_total = lax.psum(partial_value.astype(jnp.bfloat16), "col").astype(jnp.float32)
    out_block = lax.dynamic_slice_in_dim(out_total, col_start, columns, 1)
    residual_grad = (token_weight * (out_total - target.astype(jnp.float32))).astype(jnp.bfloat16)
    grad_mixed = lax.dot_general(
        residual_grad, out_weight, (((1,), (1,)), ((), ())), preferred_element_type=jnp.float32
    )
    grad_conv = grad_mixed * gate_act * silu_grad(conv_sum)
    grad_gate = (grad_mixed * conv_act * silu_grad(gate_value)).astype(jnp.bfloat16)
    local_grad = conv_weight[0][None, :] * grad_conv
    spill_over = jnp.zeros((margin, inner_width), jnp.float32)
    for offset in range(1, CONV):
        masked = (
            conv_weight[offset][None, :]
            * grad_conv
            * (doc_pos >= offset).astype(jnp.float32)[:, None]
        )
        local_grad = local_grad + jnp.concatenate(
            [masked[offset:], jnp.zeros((offset, inner_width), jnp.float32)], axis=0
        )
        spill_over = spill_over + jnp.concatenate(
            [jnp.zeros((margin - offset, inner_width), jnp.float32), masked[:offset]], axis=0
        )
    from_next = passed_along(spill_over, "row", -1)
    grad_x = (
        local_grad
        + jnp.concatenate(
            [jnp.zeros((row_count - margin, inner_width), jnp.float32), from_next], axis=0
        )
    ).astype(jnp.bfloat16)
    if moves_tokens:
        got_a, got_b, sources = ring_gather(grad_x, "row")
        half = grad_x.shape[1] // 2
        contract = (((2,), (1,)), ((), ()))
        grad_cols = lax.dot_general(
            got_a, in_weight[:, :half], contract, preferred_element_type=jnp.float32
        ) + lax.dot_general(got_b, in_weight[:, half:], contract, preferred_element_type=jnp.float32)
        grad_cols = jnp.take(grad_cols.astype(jnp.bfloat16), jnp.argsort(sources), axis=0)
        grad_cols = grad_cols.reshape(-1, grad_cols.shape[2])
        if lax.axis_size("col") == 4:
            grad_sum = col_psum_scatter(grad_cols)
        else:
            grad_sum = lax.psum_scatter(grad_cols, "col", scatter_dimension=0, tiled=True)
        grad_tokens = placed_blocks(grad_sum, row_count)
    else:
        partial_grad = lax.dot_general(
            grad_x, full_in, (((1,), (1,)), ((), ())), preferred_element_type=jnp.float32
        )
        grad_tokens = lax.psum_scatter(
            partial_grad.astype(jnp.bfloat16), "col", scatter_dimension=1, tiled=True
        )
    return (out_block.astype(jnp.bfloat16), grad_tokens, grad_gate)


def solution(mesh):
    in_specs = (
        P("row", None),
        P("row", "col"),
        P("row", "col"),
        P(None, "col"),
        P("col", None),
        P("row", None),
        P("row"),
        P(),
        P("row"),
    )
    out_specs = (P("row", "col"), P("row", "col"), P("row", "col"))
    return jax.shard_map(shards, mesh=mesh, in_specs=in_specs, out_specs=out_specs, check_vma=False)
```

```python
import jax
import jax.numpy as jnp
from jax import lax
from jax.sharding import PartitionSpec as P

CONV = 4
LANGS = 32


def passed_along(value, axis, steps):
    count = lax.axis_size(axis)
    first, last = (max(0, -steps), min(count, count - steps))
    return lax.ppermute(value, axis, [(source, source + steps) for source in range(first, last)])


def fetched_columns(tokens):
    n_row, n_col = lax.axis_size("row"), lax.axis_size("col")
    width = tokens.shape[1] // n_row
    if n_col % 2:
        return lax.all_to_all(tokens, "row", 1, 0, tiled=True)
    core = lax.axis_index("col") % 2
    halves = tokens.reshape(tokens.shape[0], n_row, 2, width // 2)
    mine = jnp.take(halves, core, axis=2).reshape(tokens.shape[0], n_row * (width // 2))
    mine = lax.all_to_all(mine, "row", 1, 0, tiled=True)
    other = lax.ppermute(mine, "col", [(c, c ^ 1) for c in range(n_col)])
    return jnp.where(
        core == 0, jnp.concatenate([mine, other], axis=1), jnp.concatenate([other, mine], axis=1)
    )


def placed_blocks(grad_sum, row_count):
    n_row, n_col = lax.axis_size("row"), lax.axis_size("col")
    share = n_row // n_col
    row, col = lax.axis_index("row"), lax.axis_index("col")
    pieces = []
    for j in range(share):
        got = []
        for k in range(share):
            pairs = [
                (r * n_col + c, (c * share + k) * n_col + r // share)
                for r in range(n_row)
                if r % share == j
                for c in range(n_col)
            ]
            got.append(lax.ppermute(grad_sum[k * row_count : (k + 1) * row_count], ("row", "col"), pairs))
        piece = got[0]
        for k in range(1, share):
            piece = jnp.where(row % share == k, got[k], piece)
        pieces.append(piece)
    return jnp.concatenate(pieces, axis=1)


def ring_order(count):
    if count % 2:
        return list(range(count))
    return list(range(0, count, 2)) + list(range(count - 1, 0, -2))


def ring_place(axis):
    count = lax.axis_size(axis)
    order = ring_order(count)
    place = jnp.array([order.index(i) for i in range(count)], jnp.int32)[lax.axis_index(axis)]
    ahead = [(order[i], order[(i + 1) % count]) for i in range(count)]
    behind = [(order[(i + 1) % count], order[i]) for i in range(count)]
    return count, jnp.array(order, jnp.int32), place, ahead, behind


def ring_gather(value, axis, chains=2):
    count, order, place, ahead, behind = ring_place(axis)
    parts = jnp.split(value, 2 * chains, axis=1)
    stacks = []
    for number, part in enumerate(parts):
        pairs = ahead if number < chains else behind
        got = [part]
        for _ in range(1, count):
            part = lax.ppermute(part, axis, pairs)
            got.append(part)
        if number >= chains:
            got = [got[(count - s) % count] for s in range(count)]
        stacks.append(jnp.stack(got))
    sources = order[(place - jnp.arange(count)) % count]
    return stacks, sources


def ring_reduce_scatter(token_cols, weight, axis, chains=2):
    count, order, place, ahead, behind = ring_place(axis)
    rows = token_cols.shape[0] // count
    blocks = token_cols.reshape(count, rows, token_cols.shape[1])
    half = weight.shape[1] // 2
    steps = jnp.arange(count)
    first = jnp.take(blocks, order[(place - 1 - steps) % count], axis=0).reshape(token_cols.shape)
    second = jnp.take(blocks, order[(place + 1 + steps) % count], axis=0).reshape(token_cols.shape)
    own_a = jnp.dot(first, weight[:, :half], preferred_element_type=jnp.float32)
    own_b = jnp.dot(second, weight[:, half:], preferred_element_type=jnp.float32)
    owns = jnp.split(own_a.reshape(count, rows, half), chains, axis=2) + jnp.split(
        own_b.reshape(count, rows, weight.shape[1] - half), chains, axis=2
    )
    sums = []
    for number, own in enumerate(owns):
        pairs = ahead if number < chains else behind
        total = own[0].astype(jnp.bfloat16)
        for s in range(1, count):
            total = lax.ppermute(total, axis, pairs)
            total = (total.astype(jnp.float32) + own[s]).astype(jnp.bfloat16)
        sums.append(total)
    return jnp.concatenate(sums, axis=1)

def halves_of(value, dim, upper):
    low, high = jnp.split(value, 2, axis=dim)
    return jnp.where(upper, high, low), jnp.where(upper, low, high)


def col_psum(value):
    core = lax.axis_index("col") % 2 == 1
    keep, give = halves_of(value, 1, core)
    count = lax.axis_size("col")
    got = lax.ppermute(give, "col", [(c, c ^ 1) for c in range(count)])
    pair = keep.astype(jnp.float32) + got.astype(jnp.float32)
    total = pair + lax.ppermute(
        pair.astype(jnp.bfloat16), "col", [(c, c ^ 2) for c in range(count)]
    ).astype(jnp.float32)
    other = lax.ppermute(total, "col", [(c, c ^ 1) for c in range(count)])
    return jnp.where(
        core, jnp.concatenate([other, total], axis=1), jnp.concatenate([total, other], axis=1)
    )


def col_psum_scatter(value):
    col = lax.axis_index("col")
    count = lax.axis_size("col")
    quarters = value.reshape(2, 2, value.shape[0] // 4, value.shape[1])
    keep = jnp.take(quarters, col % 2, axis=1)
    give = jnp.take(quarters, 1 - col % 2, axis=1)
    got = lax.ppermute(give, "col", [(c, c ^ 1) for c in range(count)])
    pair = keep.astype(jnp.float32) + got.astype(jnp.float32)
    mine = jnp.take(pair, col // 2, axis=0)
    theirs = jnp.take(pair, 1 - col // 2, axis=0)
    got = lax.ppermute(theirs.astype(jnp.bfloat16), "col", [(c, c ^ 2) for c in range(count)])
    return (mine + got.astype(jnp.float32)).astype(jnp.bfloat16)


def silu_grad(argument):
    sigmoid_v = jax.nn.sigmoid(argument)
    return sigmoid_v * (1.0 + argument * (1.0 - sigmoid_v))


def shards(
    tokens, in_weight, gate_branch, conv_weight, out_weight, target, lang_ids, lang_weight, doc_pos
):
    row_count = tokens.shape[0]
    inner_width = gate_branch.shape[1]
    margin = CONV - 1
    moves_tokens = (
        row_count * lax.axis_size("row") < tokens.shape[1]
        and lax.axis_size("row") % lax.axis_size("col") == 0
    )
    if moves_tokens:
        inner_x = ring_reduce_scatter(fetched_columns(tokens), in_weight, "row")
    else:
        full_in = lax.all_gather(in_weight, "row", axis=0, tiled=True)
        inner_x = jnp.dot(tokens, full_in, preferred_element_type=jnp.float32).astype(jnp.bfloat16)
    from_prev = passed_along(inner_x[row_count - margin :], "row", 1)
    extended = jnp.concatenate([from_prev, inner_x], axis=0).astype(jnp.float32)
    conv_sum = jnp.zeros((row_count, inner_width), jnp.float32)
    for offset in range(CONV):
        keep_mask = (doc_pos >= offset).astype(jnp.float32)[:, None]
        conv_sum = (
            conv_sum
            + conv_weight[offset][None, :]
            * extended[margin - offset : margin - offset + row_count]
            * keep_mask
        )
    gate_value = gate_branch.astype(jnp.float32)
    gate_act = jax.nn.silu(gate_value)
    conv_act = jax.nn.silu(conv_sum)
    mixed = (conv_act * gate_act).astype(jnp.bfloat16)
    partial_value = jnp.dot(mixed, out_weight, preferred_element_type=jnp.float32)
    columns = tokens.shape[1] // lax.axis_size("col")
    col_start = lax.axis_index("col") * columns
    lang_table = (lang_ids[:, None] == jnp.arange(LANGS, dtype=jnp.int32)[None, :]).astype(
        jnp.float32
    )
    token_weight = jnp.sum(lang_table * lang_weight[None, :], axis=1)[:, None]
    if moves_tokens and lax.axis_size("col") == 4:
        out_total = col_psum(partial_value.astype(jnp.bfloat16))
    else:
        out_total = lax.psum(partial_value.astype(jnp.bfloat16), "col").astype(jnp.float32)
    out_block = lax.dynamic_slice_in_dim(out_total, col_start, columns, 1)
    residual_grad = (token_weight * (out_total - target.astype(jnp.float32))).astype(jnp.bfloat16)
    grad_mixed = lax.dot_general(
        residual_grad, out_weight, (((1,), (1,)), ((), ())), preferred_element_type=jnp.float32
    )
    grad_conv = grad_mixed * gate_act * silu_grad(conv_sum)
    grad_gate = (grad_mixed * conv_act * silu_grad(gate_value)).astype(jnp.bfloat16)
    local_grad = conv_weight[0][None, :] * grad_conv
    spill_over = jnp.zeros((margin, inner_width), jnp.float32)
    for offset in range(1, CONV):
        masked = (
            conv_weight[offset][None, :]
            * grad_conv
            * (doc_pos >= offset).astype(jnp.float32)[:, None]
        )
        local_grad = local_grad + jnp.concatenate(
            [masked[offset:], jnp.zeros((offset, inner_width), jnp.float32)], axis=0
        )
        spill_over = spill_over + jnp.concatenate(
            [jnp.zeros((margin - offset, inner_width), jnp.float32), masked[:offset]], axis=0
        )
    from_next = passed_along(spill_over, "row", -1)
    grad_x = (
        local_grad
        + jnp.concatenate(
            [jnp.zeros((row_count - margin, inner_width), jnp.float32), from_next], axis=0
        )
    ).astype(jnp.bfloat16)
    if moves_tokens:
        stacks, sources = ring_gather(grad_x, "row")
        contract = (((2,), (1,)), ((), ()))
        weight_parts = jnp.split(in_weight, len(stacks), axis=1)
        grad_cols = lax.dot_general(
            stacks[0], weight_parts[0], contract, preferred_element_type=jnp.float32
        )
        for stack, weight_part in zip(stacks[1:], weight_parts[1:]):
            grad_cols = grad_cols + lax.dot_general(
                stack, weight_part, contract, preferred_element_type=jnp.float32
            )
        grad_cols = jnp.take(grad_cols.astype(jnp.bfloat16), jnp.argsort(sources), axis=0)
        grad_cols = grad_cols.reshape(-1, grad_cols.shape[2])
        if lax.axis_size("col") == 4:
            grad_sum = col_psum_scatter(grad_cols)
        else:
            grad_sum = lax.psum_scatter(grad_cols, "col", scatter_dimension=0, tiled=True)
        grad_tokens = placed_blocks(grad_sum, row_count)
    else:
        partial_grad = lax.dot_general(
            grad_x, full_in, (((1,), (1,)), ((), ())), preferred_element_type=jnp.float32
        )
        grad_tokens = lax.psum_scatter(
            partial_grad.astype(jnp.bfloat16), "col", scatter_dimension=1, tiled=True
        )
    return (out_block.astype(jnp.bfloat16), grad_tokens, grad_gate)


def solution(mesh):
    in_specs = (
        P("row", None),
        P("row", "col"),
        P("row", "col"),
        P(None, "col"),
        P("col", None),
        P("row", None),
        P("row"),
        P(),
        P("row"),
    )
    out_specs = (P("row", "col"), P("row", "col"), P("row", "col"))
    return jax.shard_map(shards, mesh=mesh, in_specs=in_specs, out_specs=out_specs, check_vma=False)
```

```python
import jax
import jax.numpy as jnp
from jax import lax
from jax.sharding import PartitionSpec as P

CONV = 4
LANGS = 32


def passed_along(value, axis, steps):
    count = lax.axis_size(axis)
    first, last = (max(0, -steps), min(count, count - steps))
    return lax.ppermute(value, axis, [(source, source + steps) for source in range(first, last)])


def fetched_columns(tokens):
    n_row, n_col = lax.axis_size("row"), lax.axis_size("col")
    width = tokens.shape[1] // n_row
    if n_col % 2:
        return lax.all_to_all(tokens, "row", 1, 0, tiled=True)
    core = lax.axis_index("col") % 2
    halves = tokens.reshape(tokens.shape[0], n_row, 2, width // 2)
    mine = jnp.take(halves, core, axis=2).reshape(tokens.shape[0], n_row * (width // 2))
    mine = lax.all_to_all(mine, "row", 1, 0, tiled=True)
    other = lax.ppermute(mine, "col", [(c, c ^ 1) for c in range(n_col)])
    return jnp.where(
        core == 0, jnp.concatenate([mine, other], axis=1), jnp.concatenate([other, mine], axis=1)
    )


def placed_blocks(grad_sum, row_count):
    n_row, n_col = lax.axis_size("row"), lax.axis_size("col")
    share = n_row // n_col
    row, col = lax.axis_index("row"), lax.axis_index("col")
    pieces = []
    for j in range(share):
        got = []
        for k in range(share):
            pairs = [
                (r * n_col + c, (c * share + k) * n_col + r // share)
                for r in range(n_row)
                if r % share == j
                for c in range(n_col)
            ]
            got.append(lax.ppermute(grad_sum[k * row_count : (k + 1) * row_count], ("row", "col"), pairs))
        piece = got[0]
        for k in range(1, share):
            piece = jnp.where(row % share == k, got[k], piece)
        pieces.append(piece)
    return jnp.concatenate(pieces, axis=1)


def ring_order(count):
    if count % 2:
        return list(range(count))
    return list(range(0, count, 2)) + list(range(count - 1, 0, -2))


def ring_place(axis):
    count = lax.axis_size(axis)
    order = ring_order(count)
    place = jnp.array([order.index(i) for i in range(count)], jnp.int32)[lax.axis_index(axis)]
    ahead = [(order[i], order[(i + 1) % count]) for i in range(count)]
    behind = [(order[(i + 1) % count], order[i]) for i in range(count)]
    return count, jnp.array(order, jnp.int32), place, ahead, behind


def ring_gather(value, axis, chains=2):
    count, order, place, ahead, behind = ring_place(axis)
    parts = jnp.split(value, 2 * chains, axis=1)
    stacks = []
    for number, part in enumerate(parts):
        pairs = ahead if number < chains else behind
        got = [part]
        for _ in range(1, count):
            part = lax.ppermute(part, axis, pairs)
            got.append(part)
        if number >= chains:
            got = [got[(count - s) % count] for s in range(count)]
        stacks.append(jnp.stack(got))
    sources = order[(place - jnp.arange(count)) % count]
    return stacks, sources


def ring_reduce_scatter(tokens, weight, axis, chains=2):
    count, order, place, ahead, behind = ring_place(axis)
    rows = tokens.shape[0]
    width = tokens.shape[1] // count
    columns = tokens.reshape(rows, count, width)
    fetched = {0: jnp.take(columns, order[place], axis=1)}
    for distance in sorted(range(1, count), key=lambda k: min(k, count - k)):
        sent = jnp.take(columns, order[(place + distance) % count], axis=1)
        cycle = ring_order(count)
        fetched[distance] = lax.ppermute(
            sent, axis, [(cycle[i], cycle[(i + distance) % count]) for i in range(count)]
        )
    half = weight.shape[1] // 2
    part = half // chains
    sums = []
    for number in range(2 * chains):
        forward = number < chains
        pairs = ahead if forward else behind
        cols = slice(number * part, (number + 1) * part)
        total = None
        for s in range(count):
            distance = (s + 1) % count if forward else (count - 1 - s) % count
            own = jnp.dot(fetched[distance], weight[:, cols], preferred_element_type=jnp.float32)
            if total is None:
                total = own.astype(jnp.bfloat16)
            else:
                total = lax.ppermute(total, axis, pairs)
                total = (total.astype(jnp.float32) + own).astype(jnp.bfloat16)
        sums.append(total)
    return jnp.concatenate(sums, axis=1)

def halves_of(value, dim, upper):
    low, high = jnp.split(value, 2, axis=dim)
    return jnp.where(upper, high, low), jnp.where(upper, low, high)


def col_psum(value):
    core = lax.axis_index("col") % 2 == 1
    keep, give = halves_of(value, 1, core)
    count = lax.axis_size("col")
    got = lax.ppermute(give, "col", [(c, c ^ 1) for c in range(count)])
    pair = keep.astype(jnp.float32) + got.astype(jnp.float32)
    total = pair + lax.ppermute(
        pair.astype(jnp.bfloat16), "col", [(c, c ^ 2) for c in range(count)]
    ).astype(jnp.float32)
    other = lax.ppermute(total, "col", [(c, c ^ 1) for c in range(count)])
    return jnp.where(
        core, jnp.concatenate([other, total], axis=1), jnp.concatenate([total, other], axis=1)
    )


def col_psum_scatter(value):
    col = lax.axis_index("col")
    count = lax.axis_size("col")
    quarters = value.reshape(2, 2, value.shape[0] // 4, value.shape[1])
    keep = jnp.take(quarters, col % 2, axis=1)
    give = jnp.take(quarters, 1 - col % 2, axis=1)
    got = lax.ppermute(give, "col", [(c, c ^ 1) for c in range(count)])
    pair = keep.astype(jnp.float32) + got.astype(jnp.float32)
    mine = jnp.take(pair, col // 2, axis=0)
    theirs = jnp.take(pair, 1 - col // 2, axis=0)
    got = lax.ppermute(theirs.astype(jnp.bfloat16), "col", [(c, c ^ 2) for c in range(count)])
    return (mine + got.astype(jnp.float32)).astype(jnp.bfloat16)


def silu_grad(argument):
    sigmoid_v = jax.nn.sigmoid(argument)
    return sigmoid_v * (1.0 + argument * (1.0 - sigmoid_v))


def shards(
    tokens, in_weight, gate_branch, conv_weight, out_weight, target, lang_ids, lang_weight, doc_pos
):
    row_count = tokens.shape[0]
    inner_width = gate_branch.shape[1]
    margin = CONV - 1
    moves_tokens = (
        row_count * lax.axis_size("row") < tokens.shape[1]
        and lax.axis_size("row") % lax.axis_size("col") == 0
    )
    if moves_tokens:
        inner_x = ring_reduce_scatter(tokens, in_weight, "row")
    else:
        full_in = lax.all_gather(in_weight, "row", axis=0, tiled=True)
        inner_x = jnp.dot(tokens, full_in, preferred_element_type=jnp.float32).astype(jnp.bfloat16)
    from_prev = passed_along(inner_x[row_count - margin :], "row", 1)
    extended = jnp.concatenate([from_prev, inner_x], axis=0).astype(jnp.float32)
    conv_sum = jnp.zeros((row_count, inner_width), jnp.float32)
    for offset in range(CONV):
        keep_mask = (doc_pos >= offset).astype(jnp.float32)[:, None]
        conv_sum = (
            conv_sum
            + conv_weight[offset][None, :]
            * extended[margin - offset : margin - offset + row_count]
            * keep_mask
        )
    gate_value = gate_branch.astype(jnp.float32)
    gate_act = jax.nn.silu(gate_value)
    conv_act = jax.nn.silu(conv_sum)
    mixed = (conv_act * gate_act).astype(jnp.bfloat16)
    partial_value = jnp.dot(mixed, out_weight, preferred_element_type=jnp.float32)
    columns = tokens.shape[1] // lax.axis_size("col")
    col_start = lax.axis_index("col") * columns
    lang_table = (lang_ids[:, None] == jnp.arange(LANGS, dtype=jnp.int32)[None, :]).astype(
        jnp.float32
    )
    token_weight = jnp.sum(lang_table * lang_weight[None, :], axis=1)[:, None]
    if moves_tokens and lax.axis_size("col") == 4:
        out_total = col_psum(partial_value.astype(jnp.bfloat16))
    else:
        out_total = lax.psum(partial_value.astype(jnp.bfloat16), "col").astype(jnp.float32)
    out_block = lax.dynamic_slice_in_dim(out_total, col_start, columns, 1)
    residual_grad = (token_weight * (out_total - target.astype(jnp.float32))).astype(jnp.bfloat16)
    grad_mixed = lax.dot_general(
        residual_grad, out_weight, (((1,), (1,)), ((), ())), preferred_element_type=jnp.float32
    )
    grad_conv = grad_mixed * gate_act * silu_grad(conv_sum)
    grad_gate = (grad_mixed * conv_act * silu_grad(gate_value)).astype(jnp.bfloat16)
    local_grad = conv_weight[0][None, :] * grad_conv
    spill_over = jnp.zeros((margin, inner_width), jnp.float32)
    for offset in range(1, CONV):
        masked = (
            conv_weight[offset][None, :]
            * grad_conv
            * (doc_pos >= offset).astype(jnp.float32)[:, None]
        )
        local_grad = local_grad + jnp.concatenate(
            [masked[offset:], jnp.zeros((offset, inner_width), jnp.float32)], axis=0
        )
        spill_over = spill_over + jnp.concatenate(
            [jnp.zeros((margin - offset, inner_width), jnp.float32), masked[:offset]], axis=0
        )
    from_next = passed_along(spill_over, "row", -1)
    grad_x = (
        local_grad
        + jnp.concatenate(
            [jnp.zeros((row_count - margin, inner_width), jnp.float32), from_next], axis=0
        )
    ).astype(jnp.bfloat16)
    if moves_tokens:
        stacks, sources = ring_gather(grad_x, "row")
        contract = (((2,), (1,)), ((), ()))
        weight_parts = jnp.split(in_weight, len(stacks), axis=1)
        grad_cols = lax.dot_general(
            stacks[0], weight_parts[0], contract, preferred_element_type=jnp.float32
        )
        for stack, weight_part in zip(stacks[1:], weight_parts[1:]):
            grad_cols = grad_cols + lax.dot_general(
                stack, weight_part, contract, preferred_element_type=jnp.float32
            )
        grad_cols = jnp.take(grad_cols.astype(jnp.bfloat16), jnp.argsort(sources), axis=0)
        grad_cols = grad_cols.reshape(-1, grad_cols.shape[2])
        if lax.axis_size("col") == 4:
            grad_sum = col_psum_scatter(grad_cols)
        else:
            grad_sum = lax.psum_scatter(grad_cols, "col", scatter_dimension=0, tiled=True)
        grad_tokens = placed_blocks(grad_sum, row_count)
    else:
        partial_grad = lax.dot_general(
            grad_x, full_in, (((1,), (1,)), ((), ())), preferred_element_type=jnp.float32
        )
        grad_tokens = lax.psum_scatter(
            partial_grad.astype(jnp.bfloat16), "col", scatter_dimension=1, tiled=True
        )
    return (out_block.astype(jnp.bfloat16), grad_tokens, grad_gate)


def solution(mesh):
    in_specs = (
        P("row", None),
        P("row", "col"),
        P("row", "col"),
        P(None, "col"),
        P("col", None),
        P("row", None),
        P("row"),
        P(),
        P("row"),
    )
    out_specs = (P("row", "col"), P("row", "col"), P("row", "col"))
    return jax.shard_map(shards, mesh=mesh, in_specs=in_specs, out_specs=out_specs, check_vma=False)
```

```python
import jax
import jax.numpy as jnp
from jax import lax
from jax.sharding import PartitionSpec as P

CONV = 4
LANGS = 32


def passed_along(value, axis, steps):
    count = lax.axis_size(axis)
    first, last = (max(0, -steps), min(count, count - steps))
    return lax.ppermute(value, axis, [(source, source + steps) for source in range(first, last)])


def fetched_columns(tokens):
    n_row, n_col = lax.axis_size("row"), lax.axis_size("col")
    width = tokens.shape[1] // n_row
    if n_col % 2:
        return lax.all_to_all(tokens, "row", 1, 0, tiled=True)
    core = lax.axis_index("col") % 2
    halves = tokens.reshape(tokens.shape[0], n_row, 2, width // 2)
    mine = jnp.take(halves, core, axis=2).reshape(tokens.shape[0], n_row * (width // 2))
    mine = lax.all_to_all(mine, "row", 1, 0, tiled=True)
    other = lax.ppermute(mine, "col", [(c, c ^ 1) for c in range(n_col)])
    return jnp.where(
        core == 0, jnp.concatenate([mine, other], axis=1), jnp.concatenate([other, mine], axis=1)
    )


def placed_blocks(grad_sum, row_count):
    n_row, n_col = lax.axis_size("row"), lax.axis_size("col")
    share = n_row // n_col
    row, col = lax.axis_index("row"), lax.axis_index("col")
    pieces = []
    for j in range(share):
        got = []
        for k in range(share):
            pairs = [
                (r * n_col + c, (c * share + k) * n_col + r // share)
                for r in range(n_row)
                if r % share == j
                for c in range(n_col)
            ]
            got.append(lax.ppermute(grad_sum[k * row_count : (k + 1) * row_count], ("row", "col"), pairs))
        piece = got[0]
        for k in range(1, share):
            piece = jnp.where(row % share == k, got[k], piece)
        pieces.append(piece)
    return jnp.concatenate(pieces, axis=1)


def ring_order(count):
    if count % 2:
        return list(range(count))
    return list(range(0, count, 2)) + list(range(count - 1, 0, -2))


def ring_place(axis):
    count = lax.axis_size(axis)
    order = ring_order(count)
    place = jnp.array([order.index(i) for i in range(count)], jnp.int32)[lax.axis_index(axis)]
    ahead = [(order[i], order[(i + 1) % count]) for i in range(count)]
    behind = [(order[(i + 1) % count], order[i]) for i in range(count)]
    return count, jnp.array(order, jnp.int32), place, ahead, behind


def ring_gather(value, axis):
    count, order, place, ahead, behind = ring_place(axis)
    parts = value
    chains = len(parts) // 2
    stacks = []
    for number, part in enumerate(parts):
        pairs = ahead if number < chains else behind
        got = [part]
        for _ in range(1, count):
            part = lax.ppermute(part, axis, pairs)
            got.append(part)
        if number >= chains:
            got = [got[(count - s) % count] for s in range(count)]
        stacks.append(jnp.stack(got))
    sources = order[(place - jnp.arange(count)) % count]
    return stacks, sources


def ring_reduce_scatter(token_cols, weight, axis, chains=2):
    count, order, place, ahead, behind = ring_place(axis)
    rows = token_cols.shape[0] // count
    blocks = token_cols.reshape(count, rows, token_cols.shape[1])
    half = weight.shape[1] // 2
    steps = jnp.arange(count)
    first = jnp.take(blocks, order[(place - 1 - steps) % count], axis=0).reshape(token_cols.shape)
    second = jnp.take(blocks, order[(place + 1 + steps) % count], axis=0).reshape(token_cols.shape)
    own_a = jnp.dot(first, weight[:, :half], preferred_element_type=jnp.float32)
    own_b = jnp.dot(second, weight[:, half:], preferred_element_type=jnp.float32)
    owns = jnp.split(own_a.reshape(count, rows, half), chains, axis=2) + jnp.split(
        own_b.reshape(count, rows, weight.shape[1] - half), chains, axis=2
    )
    sums = []
    for number, own in enumerate(owns):
        pairs = ahead if number < chains else behind
        total = own[0].astype(jnp.bfloat16)
        for s in range(1, count):
            total = lax.ppermute(total, axis, pairs)
            total = (total.astype(jnp.float32) + own[s]).astype(jnp.bfloat16)
        sums.append(total)
    return jnp.concatenate(sums, axis=1)

def halves_of(value, dim, upper):
    low, high = jnp.split(value, 2, axis=dim)
    return jnp.where(upper, high, low), jnp.where(upper, low, high)


def col_psum(value):
    core = lax.axis_index("col") % 2 == 1
    keep, give = halves_of(value, 1, core)
    count = lax.axis_size("col")
    got = lax.ppermute(give, "col", [(c, c ^ 1) for c in range(count)])
    pair = keep.astype(jnp.float32) + got.astype(jnp.float32)
    total = pair + lax.ppermute(
        pair.astype(jnp.bfloat16), "col", [(c, c ^ 2) for c in range(count)]
    ).astype(jnp.float32)
    other = lax.ppermute(total, "col", [(c, c ^ 1) for c in range(count)])
    return jnp.where(
        core, jnp.concatenate([other, total], axis=1), jnp.concatenate([total, other], axis=1)
    )


def col_psum_scatter(value):
    col = lax.axis_index("col")
    count = lax.axis_size("col")
    quarters = value.reshape(2, 2, value.shape[0] // 4, value.shape[1])
    keep = jnp.take(quarters, col % 2, axis=1)
    give = jnp.take(quarters, 1 - col % 2, axis=1)
    got = lax.ppermute(give, "col", [(c, c ^ 1) for c in range(count)])
    pair = keep.astype(jnp.float32) + got.astype(jnp.float32)
    mine = jnp.take(pair, col // 2, axis=0)
    theirs = jnp.take(pair, 1 - col // 2, axis=0)
    got = lax.ppermute(theirs.astype(jnp.bfloat16), "col", [(c, c ^ 2) for c in range(count)])
    return (mine + got.astype(jnp.float32)).astype(jnp.bfloat16)


def silu_grad(argument):
    sigmoid_v = jax.nn.sigmoid(argument)
    return sigmoid_v * (1.0 + argument * (1.0 - sigmoid_v))


def shards(
    tokens, in_weight, gate_branch, conv_weight, out_weight, target, lang_ids, lang_weight, doc_pos
):
    row_count = tokens.shape[0]
    inner_width = gate_branch.shape[1]
    margin = CONV - 1
    moves_tokens = (
        row_count * lax.axis_size("row") < tokens.shape[1]
        and lax.axis_size("row") % lax.axis_size("col") == 0
    )
    if moves_tokens:
        inner_x = ring_reduce_scatter(fetched_columns(tokens), in_weight, "row")
    else:
        full_in = lax.all_gather(in_weight, "row", axis=0, tiled=True)
        inner_x = jnp.dot(tokens, full_in, preferred_element_type=jnp.float32).astype(jnp.bfloat16)
    from_prev = passed_along(inner_x[row_count - margin :], "row", 1)
    extended = jnp.concatenate([from_prev, inner_x], axis=0).astype(jnp.float32)
    conv_sum = jnp.zeros((row_count, inner_width), jnp.float32)
    for offset in range(CONV):
        keep_mask = (doc_pos >= offset).astype(jnp.float32)[:, None]
        conv_sum = (
            conv_sum
            + conv_weight[offset][None, :]
            * extended[margin - offset : margin - offset + row_count]
            * keep_mask
        )
    gate_value = gate_branch.astype(jnp.float32)
    gate_act = jax.nn.silu(gate_value)
    conv_act = jax.nn.silu(conv_sum)
    mixed = (conv_act * gate_act).astype(jnp.bfloat16)
    partial_value = jnp.dot(mixed, out_weight, preferred_element_type=jnp.float32)
    columns = tokens.shape[1] // lax.axis_size("col")
    col_start = lax.axis_index("col") * columns
    lang_table = (lang_ids[:, None] == jnp.arange(LANGS, dtype=jnp.int32)[None, :]).astype(
        jnp.float32
    )
    token_weight = jnp.sum(lang_table * lang_weight[None, :], axis=1)[:, None]
    if moves_tokens and lax.axis_size("col") == 4:
        out_total = col_psum(partial_value.astype(jnp.bfloat16))
    else:
        out_total = lax.psum(partial_value.astype(jnp.bfloat16), "col").astype(jnp.float32)
    out_block = lax.dynamic_slice_in_dim(out_total, col_start, columns, 1)
    residual_grad = (token_weight * (out_total - target.astype(jnp.float32))).astype(jnp.bfloat16)
    def backward_part(cols):
        width = cols.stop - cols.start
        mixed_grad = lax.dot_general(
            residual_grad, out_weight[cols], (((1,), (1,)), ((), ())), preferred_element_type=jnp.float32
        )
        grad_conv = mixed_grad * gate_act[:, cols] * silu_grad(conv_sum[:, cols])
        gate_grad = (mixed_grad * conv_act[:, cols] * silu_grad(gate_value[:, cols])).astype(jnp.bfloat16)
        local_grad = conv_weight[0][None, cols] * grad_conv
        spill_over = jnp.zeros((margin, width), jnp.float32)
        for offset in range(1, CONV):
            masked = (
                conv_weight[offset][None, cols]
                * grad_conv
                * (doc_pos >= offset).astype(jnp.float32)[:, None]
            )
            local_grad = local_grad + jnp.concatenate(
                [masked[offset:], jnp.zeros((offset, width), jnp.float32)], axis=0
            )
            spill_over = spill_over + jnp.concatenate(
                [jnp.zeros((margin - offset, width), jnp.float32), masked[:offset]], axis=0
            )
        from_next = passed_along(spill_over, "row", -1)
        x_grad = (
            local_grad
            + jnp.concatenate([jnp.zeros((row_count - margin, width), jnp.float32), from_next], axis=0)
        ).astype(jnp.bfloat16)
        return x_grad, gate_grad

    part_count = 4 if moves_tokens else 1
    part_width = inner_width // part_count
    outcomes = [
        backward_part(slice(k * part_width, (k + 1) * part_width)) for k in range(part_count)
    ]
    grad_x_parts = [x for x, _ in outcomes]
    grad_gate = jnp.concatenate([g for _, g in outcomes], axis=1)
    grad_x = jnp.concatenate(grad_x_parts, axis=1)
    if moves_tokens:
        stacks, sources = ring_gather(grad_x_parts, "row")
        contract = (((2,), (1,)), ((), ()))
        weight_parts = jnp.split(in_weight, len(stacks), axis=1)
        grad_cols = lax.dot_general(
            stacks[0], weight_parts[0], contract, preferred_element_type=jnp.float32
        )
        for stack, weight_part in zip(stacks[1:], weight_parts[1:]):
            grad_cols = grad_cols + lax.dot_general(
                stack, weight_part, contract, preferred_element_type=jnp.float32
            )
        grad_cols = jnp.take(grad_cols.astype(jnp.bfloat16), jnp.argsort(sources), axis=0)
        grad_cols = grad_cols.reshape(-1, grad_cols.shape[2])
        if lax.axis_size("col") == 4:
            grad_sum = col_psum_scatter(grad_cols)
        else:
            grad_sum = lax.psum_scatter(grad_cols, "col", scatter_dimension=0, tiled=True)
        grad_tokens = placed_blocks(grad_sum, row_count)
    else:
        partial_grad = lax.dot_general(
            grad_x, full_in, (((1,), (1,)), ((), ())), preferred_element_type=jnp.float32
        )
        grad_tokens = lax.psum_scatter(
            partial_grad.astype(jnp.bfloat16), "col", scatter_dimension=1, tiled=True
        )
    return (out_block.astype(jnp.bfloat16), grad_tokens, grad_gate)


def solution(mesh):
    in_specs = (
        P("row", None),
        P("row", "col"),
        P("row", "col"),
        P(None, "col"),
        P("col", None),
        P("row", None),
        P("row"),
        P(),
        P("row"),
    )
    out_specs = (P("row", "col"), P("row", "col"), P("row", "col"))
    return jax.shard_map(shards, mesh=mesh, in_specs=in_specs, out_specs=out_specs, check_vma=False)
```

```python
import jax
import jax.numpy as jnp
from jax import lax
from jax.sharding import PartitionSpec as P

CONV = 4
LANGS = 32


def passed_along(value, axis, steps):
    count = lax.axis_size(axis)
    first, last = (max(0, -steps), min(count, count - steps))
    return lax.ppermute(value, axis, [(source, source + steps) for source in range(first, last)])


def fetched_columns(tokens):
    n_row, n_col = lax.axis_size("row"), lax.axis_size("col")
    width = tokens.shape[1] // n_row
    if n_col % 2:
        return lax.all_to_all(tokens, "row", 1, 0, tiled=True)
    core = lax.axis_index("col") % 2
    halves = tokens.reshape(tokens.shape[0], n_row, 2, width // 2)
    mine = jnp.take(halves, core, axis=2).reshape(tokens.shape[0], n_row * (width // 2))
    mine = lax.all_to_all(mine, "row", 1, 0, tiled=True)
    other = lax.ppermute(mine, "col", [(c, c ^ 1) for c in range(n_col)])
    return jnp.where(
        core == 0, jnp.concatenate([mine, other], axis=1), jnp.concatenate([other, mine], axis=1)
    )


def placed_blocks(grad_sum, row_count):
    n_row, n_col = lax.axis_size("row"), lax.axis_size("col")
    share = n_row // n_col
    row = lax.axis_index("row")
    got = []
    for m in range(share):
        pairs = [
            (r * n_col + c, (c * share + (r % share + m) % share) * n_col + r // share)
            for r in range(n_row)
            for c in range(n_col)
        ]
        start = ((row % share + m) % share) * row_count
        piece = lax.dynamic_slice_in_dim(grad_sum, start, row_count, axis=0)
        got.append(lax.ppermute(piece, ("row", "col"), pairs))
    pieces = []
    for j in range(share):
        want = (row % share - j) % share
        piece = got[0]
        for m in range(1, share):
            piece = jnp.where(want == m, got[m], piece)
        pieces.append(piece)
    return jnp.concatenate(pieces, axis=1)

def ring_order(count):
    if count % 2:
        return list(range(count))
    return list(range(0, count, 2)) + list(range(count - 1, 0, -2))


def ring_place(axis):
    count = lax.axis_size(axis)
    order = ring_order(count)
    place = jnp.array([order.index(i) for i in range(count)], jnp.int32)[lax.axis_index(axis)]
    ahead = [(order[i], order[(i + 1) % count]) for i in range(count)]
    behind = [(order[(i + 1) % count], order[i]) for i in range(count)]
    return count, jnp.array(order, jnp.int32), place, ahead, behind


def ring_gather(value, axis, chains=2):
    count, order, place, ahead, behind = ring_place(axis)
    parts = jnp.split(value, 2 * chains, axis=1)
    stacks = []
    for number, part in enumerate(parts):
        pairs = ahead if number < chains else behind
        got = [part]
        for _ in range(1, count):
            part = lax.ppermute(part, axis, pairs)
            got.append(part)
        if number >= chains:
            got = [got[(count - s) % count] for s in range(count)]
        stacks.append(jnp.stack(got))
    sources = order[(place - jnp.arange(count)) % count]
    return stacks, sources


def ring_reduce_scatter(token_cols, weight, axis, chains=2):
    count, order, place, ahead, behind = ring_place(axis)
    rows = token_cols.shape[0] // count
    blocks = token_cols.reshape(count, rows, token_cols.shape[1])
    half = weight.shape[1] // 2
    steps = jnp.arange(count)
    first = jnp.take(blocks, order[(place - 1 - steps) % count], axis=0).reshape(token_cols.shape)
    second = jnp.take(blocks, order[(place + 1 + steps) % count], axis=0).reshape(token_cols.shape)
    own_a = jnp.dot(first, weight[:, :half], preferred_element_type=jnp.float32)
    own_b = jnp.dot(second, weight[:, half:], preferred_element_type=jnp.float32)
    owns = jnp.split(own_a.reshape(count, rows, half), chains, axis=2) + jnp.split(
        own_b.reshape(count, rows, weight.shape[1] - half), chains, axis=2
    )
    sums = []
    for number, own in enumerate(owns):
        pairs = ahead if number < chains else behind
        total = own[0].astype(jnp.bfloat16)
        for s in range(1, count):
            total = lax.ppermute(total, axis, pairs)
            total = (total.astype(jnp.float32) + own[s]).astype(jnp.bfloat16)
        sums.append(total)
    return jnp.concatenate(sums, axis=1)

def halves_of(value, dim, upper):
    low, high = jnp.split(value, 2, axis=dim)
    return jnp.where(upper, high, low), jnp.where(upper, low, high)


def col_psum(value):
    core = lax.axis_index("col") % 2 == 1
    keep, give = halves_of(value, 1, core)
    count = lax.axis_size("col")
    got = lax.ppermute(give, "col", [(c, c ^ 1) for c in range(count)])
    pair = keep.astype(jnp.float32) + got.astype(jnp.float32)
    total = pair + lax.ppermute(
        pair.astype(jnp.bfloat16), "col", [(c, c ^ 2) for c in range(count)]
    ).astype(jnp.float32)
    other = lax.ppermute(total, "col", [(c, c ^ 1) for c in range(count)])
    return jnp.where(
        core, jnp.concatenate([other, total], axis=1), jnp.concatenate([total, other], axis=1)
    )


def col_psum_scatter(value):
    col = lax.axis_index("col")
    count = lax.axis_size("col")
    quarters = value.reshape(2, 2, value.shape[0] // 4, value.shape[1])
    keep = jnp.take(quarters, col % 2, axis=1)
    give = jnp.take(quarters, 1 - col % 2, axis=1)
    got = lax.ppermute(give, "col", [(c, c ^ 1) for c in range(count)])
    pair = keep.astype(jnp.float32) + got.astype(jnp.float32)
    mine = jnp.take(pair, col // 2, axis=0)
    theirs = jnp.take(pair, 1 - col // 2, axis=0)
    got = lax.ppermute(theirs.astype(jnp.bfloat16), "col", [(c, c ^ 2) for c in range(count)])
    return (mine + got.astype(jnp.float32)).astype(jnp.bfloat16)


def silu_grad(argument):
    sigmoid_v = jax.nn.sigmoid(argument)
    return sigmoid_v * (1.0 + argument * (1.0 - sigmoid_v))


def shards(
    tokens, in_weight, gate_branch, conv_weight, out_weight, target, lang_ids, lang_weight, doc_pos
):
    row_count = tokens.shape[0]
    inner_width = gate_branch.shape[1]
    margin = CONV - 1
    moves_tokens = (
        row_count * lax.axis_size("row") < tokens.shape[1]
        and lax.axis_size("row") % lax.axis_size("col") == 0
    )
    if moves_tokens:
        inner_x = ring_reduce_scatter(fetched_columns(tokens), in_weight, "row")
    else:
        full_in = lax.all_gather(in_weight, "row", axis=0, tiled=True)
        inner_x = jnp.dot(tokens, full_in, preferred_element_type=jnp.float32).astype(jnp.bfloat16)
    from_prev = passed_along(inner_x[row_count - margin :], "row", 1)
    extended = jnp.concatenate([from_prev, inner_x], axis=0).astype(jnp.float32)
    conv_sum = jnp.zeros((row_count, inner_width), jnp.float32)
    for offset in range(CONV):
        keep_mask = (doc_pos >= offset).astype(jnp.float32)[:, None]
        conv_sum = (
            conv_sum
            + conv_weight[offset][None, :]
            * extended[margin - offset : margin - offset + row_count]
            * keep_mask
        )
    gate_value = gate_branch.astype(jnp.float32)
    gate_act = jax.nn.silu(gate_value)
    conv_act = jax.nn.silu(conv_sum)
    mixed = (conv_act * gate_act).astype(jnp.bfloat16)
    partial_value = jnp.dot(mixed, out_weight, preferred_element_type=jnp.float32)
    columns = tokens.shape[1] // lax.axis_size("col")
    col_start = lax.axis_index("col") * columns
    lang_table = (lang_ids[:, None] == jnp.arange(LANGS, dtype=jnp.int32)[None, :]).astype(
        jnp.float32
    )
    token_weight = jnp.sum(lang_table * lang_weight[None, :], axis=1)[:, None]
    if moves_tokens and lax.axis_size("col") == 4:
        out_total = col_psum(partial_value.astype(jnp.bfloat16))
    else:
        out_total = lax.psum(partial_value.astype(jnp.bfloat16), "col").astype(jnp.float32)
    out_block = lax.dynamic_slice_in_dim(out_total, col_start, columns, 1)
    residual_grad = (token_weight * (out_total - target.astype(jnp.float32))).astype(jnp.bfloat16)
    grad_mixed = lax.dot_general(
        residual_grad, out_weight, (((1,), (1,)), ((), ())), preferred_element_type=jnp.float32
    )
    grad_conv = grad_mixed * gate_act * silu_grad(conv_sum)
    grad_gate = (grad_mixed * conv_act * silu_grad(gate_value)).astype(jnp.bfloat16)
    local_grad = conv_weight[0][None, :] * grad_conv
    spill_over = jnp.zeros((margin, inner_width), jnp.float32)
    for offset in range(1, CONV):
        masked = (
            conv_weight[offset][None, :]
            * grad_conv
            * (doc_pos >= offset).astype(jnp.float32)[:, None]
        )
        local_grad = local_grad + jnp.concatenate(
            [masked[offset:], jnp.zeros((offset, inner_width), jnp.float32)], axis=0
        )
        spill_over = spill_over + jnp.concatenate(
            [jnp.zeros((margin - offset, inner_width), jnp.float32), masked[:offset]], axis=0
        )
    from_next = passed_along(spill_over, "row", -1)
    grad_x = (
        local_grad
        + jnp.concatenate(
            [jnp.zeros((row_count - margin, inner_width), jnp.float32), from_next], axis=0
        )
    ).astype(jnp.bfloat16)
    if moves_tokens:
        stacks, sources = ring_gather(grad_x, "row")
        contract = (((2,), (1,)), ((), ()))
        weight_parts = jnp.split(in_weight, len(stacks), axis=1)
        grad_cols = lax.dot_general(
            stacks[0], weight_parts[0], contract, preferred_element_type=jnp.float32
        )
        for stack, weight_part in zip(stacks[1:], weight_parts[1:]):
            grad_cols = grad_cols + lax.dot_general(
                stack, weight_part, contract, preferred_element_type=jnp.float32
            )
        grad_cols = jnp.take(grad_cols.astype(jnp.bfloat16), jnp.argsort(sources), axis=0)
        grad_cols = grad_cols.reshape(-1, grad_cols.shape[2])
        if lax.axis_size("col") == 4:
            grad_sum = col_psum_scatter(grad_cols)
        else:
            grad_sum = lax.psum_scatter(grad_cols, "col", scatter_dimension=0, tiled=True)
        grad_tokens = placed_blocks(grad_sum, row_count)
    else:
        partial_grad = lax.dot_general(
            grad_x, full_in, (((1,), (1,)), ((), ())), preferred_element_type=jnp.float32
        )
        grad_tokens = lax.psum_scatter(
            partial_grad.astype(jnp.bfloat16), "col", scatter_dimension=1, tiled=True
        )
    return (out_block.astype(jnp.bfloat16), grad_tokens, grad_gate)


def solution(mesh):
    in_specs = (
        P("row", None),
        P("row", "col"),
        P("row", "col"),
        P(None, "col"),
        P("col", None),
        P("row", None),
        P("row"),
        P(),
        P("row"),
    )
    out_specs = (P("row", "col"), P("row", "col"), P("row", "col"))
    return jax.shard_map(shards, mesh=mesh, in_specs=in_specs, out_specs=out_specs, check_vma=False)
```

```python
import jax
import jax.numpy as jnp
from jax import lax
from jax.sharding import PartitionSpec as P

CONV = 4
LANGS = 32


def passed_along(value, axis, steps):
    count = lax.axis_size(axis)
    first, last = (max(0, -steps), min(count, count - steps))
    return lax.ppermute(value, axis, [(source, source + steps) for source in range(first, last)])


def fetched_columns(tokens):
    n_row, n_col = lax.axis_size("row"), lax.axis_size("col")
    width = tokens.shape[1] // n_row
    if n_col % 2:
        return lax.all_to_all(tokens, "row", 1, 0, tiled=True)
    core = lax.axis_index("col") % 2
    halves = tokens.reshape(tokens.shape[0], n_row, 2, width // 2)
    mine = jnp.take(halves, core, axis=2).reshape(tokens.shape[0], n_row * (width // 2))
    mine = lax.all_to_all(mine, "row", 1, 0, tiled=True)
    other = lax.ppermute(mine, "col", [(c, c ^ 1) for c in range(n_col)])
    return jnp.where(
        core == 0, jnp.concatenate([mine, other], axis=1), jnp.concatenate([other, mine], axis=1)
    )


def placed_blocks(grad_sum, row_count):
    n_row, n_col = lax.axis_size("row"), lax.axis_size("col")
    share = n_row // n_col
    row = lax.axis_index("row")
    got = []
    for m in range(share):
        pairs = [
            (r * n_col + c, (c * share + (r % share + m) % share) * n_col + r // share)
            for r in range(n_row)
            for c in range(n_col)
        ]
        start = ((row % share + m) % share) * row_count
        piece = lax.dynamic_slice_in_dim(grad_sum, start, row_count, axis=0)
        got.append(lax.ppermute(piece, ("row", "col"), pairs))
    pieces = []
    for j in range(share):
        want = (row % share - j) % share
        piece = got[0]
        for m in range(1, share):
            piece = jnp.where(want == m, got[m], piece)
        pieces.append(piece)
    return jnp.concatenate(pieces, axis=1)

def ring_order(count):
    if count % 2:
        return list(range(count))
    return list(range(0, count, 2)) + list(range(count - 1, 0, -2))


def ring_place(axis):
    count = lax.axis_size(axis)
    order = ring_order(count)
    place = jnp.array([order.index(i) for i in range(count)], jnp.int32)[lax.axis_index(axis)]
    ahead = [(order[i], order[(i + 1) % count]) for i in range(count)]
    behind = [(order[(i + 1) % count], order[i]) for i in range(count)]
    return count, jnp.array(order, jnp.int32), place, ahead, behind


def ring_gather(value, axis, chains=2):
    count, order, place, ahead, behind = ring_place(axis)
    parts = jnp.split(value, 2 * chains, axis=1)
    stacks = []
    for number, part in enumerate(parts):
        pairs = ahead if number < chains else behind
        got = [part]
        for _ in range(1, count):
            part = lax.ppermute(part, axis, pairs)
            got.append(part)
        if number >= chains:
            got = [got[(count - s) % count] for s in range(count)]
        stacks.append(jnp.stack(got))
    sources = order[(place - jnp.arange(count)) % count]
    return stacks, sources


def ring_reduce_scatter(token_cols, weight, axis, chains=2):
    count, order, place, ahead, behind = ring_place(axis)
    rows = token_cols.shape[0] // count
    blocks = token_cols.reshape(count, rows, token_cols.shape[1])
    half = weight.shape[1] // 2
    steps = jnp.arange(count)
    first = jnp.take(blocks, order[(place - 1 - steps) % count], axis=0).reshape(token_cols.shape)
    second = jnp.take(blocks, order[(place + 1 + steps) % count], axis=0).reshape(token_cols.shape)
    own_a = jnp.dot(first, weight[:, :half], preferred_element_type=jnp.float32)
    own_b = jnp.dot(second, weight[:, half:], preferred_element_type=jnp.float32)
    owns = jnp.split(own_a.reshape(count, rows, half), chains, axis=2) + jnp.split(
        own_b.reshape(count, rows, weight.shape[1] - half), chains, axis=2
    )
    sums = []
    for number, own in enumerate(owns):
        pairs = ahead if number < chains else behind
        total = own[0].astype(jnp.bfloat16)
        for s in range(1, count):
            total = lax.ppermute(total, axis, pairs)
            total = (total.astype(jnp.float32) + own[s]).astype(jnp.bfloat16)
        sums.append(total)
    return jnp.concatenate(sums, axis=1)

def halves_of(value, dim, upper):
    low, high = jnp.split(value, 2, axis=dim)
    return jnp.where(upper, high, low), jnp.where(upper, low, high)


def col_psum(value):
    core = lax.axis_index("col") % 2 == 1
    keep, give = halves_of(value, 1, core)
    count = lax.axis_size("col")
    got = lax.ppermute(give, "col", [(c, c ^ 1) for c in range(count)])
    pair = keep.astype(jnp.float32) + got.astype(jnp.float32)
    total = pair + lax.ppermute(
        pair.astype(jnp.bfloat16), "col", [(c, c ^ 2) for c in range(count)]
    ).astype(jnp.float32)
    other = lax.ppermute(total, "col", [(c, c ^ 1) for c in range(count)])
    return jnp.where(
        core, jnp.concatenate([other, total], axis=1), jnp.concatenate([total, other], axis=1)
    )


def col_psum_scatter(value):
    col = lax.axis_index("col")
    count = lax.axis_size("col")
    quarters = value.reshape(2, 2, value.shape[0] // 4, value.shape[1])
    keep = jnp.take(quarters, col % 2, axis=1)
    give = jnp.take(quarters, 1 - col % 2, axis=1)
    got = lax.ppermute(give, "col", [(c, c ^ 1) for c in range(count)])
    pair = keep.astype(jnp.float32) + got.astype(jnp.float32)
    mine = jnp.take(pair, col // 2, axis=0)
    theirs = jnp.take(pair, 1 - col // 2, axis=0)
    got = lax.ppermute(theirs.astype(jnp.bfloat16), "col", [(c, c ^ 2) for c in range(count)])
    return (mine + got.astype(jnp.float32)).astype(jnp.bfloat16)


def silu_grad(argument):
    sigmoid_v = jax.nn.sigmoid(argument)
    return sigmoid_v * (1.0 + argument * (1.0 - sigmoid_v))


def shards(
    tokens, in_weight, gate_branch, conv_weight, out_weight, target, lang_ids, lang_weight, doc_pos
):
    row_count = tokens.shape[0]
    inner_width = gate_branch.shape[1]
    margin = CONV - 1
    moves_tokens = (
        row_count * lax.axis_size("row") < tokens.shape[1]
        and lax.axis_size("row") % lax.axis_size("col") == 0
    )
    if moves_tokens:
        inner_x = ring_reduce_scatter(fetched_columns(tokens), in_weight, "row")
    else:
        full_in = lax.all_gather(in_weight, "row", axis=0, tiled=True)
        inner_x = jnp.dot(tokens, full_in, preferred_element_type=jnp.float32).astype(jnp.bfloat16)
    from_prev = passed_along(inner_x[row_count - margin :], "row", 1)
    extended = jnp.concatenate([from_prev, inner_x], axis=0).astype(jnp.float32)
    conv_sum = jnp.zeros((row_count, inner_width), jnp.float32)
    for offset in range(CONV):
        keep_mask = (doc_pos >= offset).astype(jnp.float32)[:, None]
        conv_sum = (
            conv_sum
            + conv_weight[offset][None, :]
            * extended[margin - offset : margin - offset + row_count]
            * keep_mask
        )
    gate_value = gate_branch.astype(jnp.float32)
    gate_act = jax.nn.silu(gate_value)
    conv_act = jax.nn.silu(conv_sum)
    conv_scale, gate_scale = lax.optimization_barrier(
        (gate_act * silu_grad(conv_sum), conv_act * silu_grad(gate_value))
    )
    mixed = (conv_act * gate_act).astype(jnp.bfloat16)
    partial_value = jnp.dot(mixed, out_weight, preferred_element_type=jnp.float32)
    columns = tokens.shape[1] // lax.axis_size("col")
    col_start = lax.axis_index("col") * columns
    lang_table = (lang_ids[:, None] == jnp.arange(LANGS, dtype=jnp.int32)[None, :]).astype(
        jnp.float32
    )
    token_weight = jnp.sum(lang_table * lang_weight[None, :], axis=1)[:, None]
    if moves_tokens and lax.axis_size("col") == 4:
        out_total = col_psum(partial_value.astype(jnp.bfloat16))
    else:
        out_total = lax.psum(partial_value.astype(jnp.bfloat16), "col").astype(jnp.float32)
    out_block = lax.dynamic_slice_in_dim(out_total, col_start, columns, 1)
    residual_grad = (token_weight * (out_total - target.astype(jnp.float32))).astype(jnp.bfloat16)
    grad_mixed = lax.dot_general(
        residual_grad, out_weight, (((1,), (1,)), ((), ())), preferred_element_type=jnp.float32
    )
    grad_conv = grad_mixed * conv_scale
    grad_gate = (grad_mixed * gate_scale).astype(jnp.bfloat16)
    local_grad = conv_weight[0][None, :] * grad_conv
    spill_over = jnp.zeros((margin, inner_width), jnp.float32)
    for offset in range(1, CONV):
        masked = (
            conv_weight[offset][None, :]
            * grad_conv
            * (doc_pos >= offset).astype(jnp.float32)[:, None]
        )
        local_grad = local_grad + jnp.concatenate(
            [masked[offset:], jnp.zeros((offset, inner_width), jnp.float32)], axis=0
        )
        spill_over = spill_over + jnp.concatenate(
            [jnp.zeros((margin - offset, inner_width), jnp.float32), masked[:offset]], axis=0
        )
    from_next = passed_along(spill_over, "row", -1)
    grad_x = (
        local_grad
        + jnp.concatenate(
            [jnp.zeros((row_count - margin, inner_width), jnp.float32), from_next], axis=0
        )
    ).astype(jnp.bfloat16)
    if moves_tokens:
        stacks, sources = ring_gather(grad_x, "row")
        contract = (((2,), (1,)), ((), ()))
        weight_parts = jnp.split(in_weight, len(stacks), axis=1)
        grad_cols = lax.dot_general(
            stacks[0], weight_parts[0], contract, preferred_element_type=jnp.float32
        )
        for stack, weight_part in zip(stacks[1:], weight_parts[1:]):
            grad_cols = grad_cols + lax.dot_general(
                stack, weight_part, contract, preferred_element_type=jnp.float32
            )
        grad_cols = jnp.take(grad_cols.astype(jnp.bfloat16), jnp.argsort(sources), axis=0)
        grad_cols = grad_cols.reshape(-1, grad_cols.shape[2])
        if lax.axis_size("col") == 4:
            grad_sum = col_psum_scatter(grad_cols)
        else:
            grad_sum = lax.psum_scatter(grad_cols, "col", scatter_dimension=0, tiled=True)
        grad_tokens = placed_blocks(grad_sum, row_count)
    else:
        partial_grad = lax.dot_general(
            grad_x, full_in, (((1,), (1,)), ((), ())), preferred_element_type=jnp.float32
        )
        grad_tokens = lax.psum_scatter(
            partial_grad.astype(jnp.bfloat16), "col", scatter_dimension=1, tiled=True
        )
    return (out_block.astype(jnp.bfloat16), grad_tokens, grad_gate)


def solution(mesh):
    in_specs = (
        P("row", None),
        P("row", "col"),
        P("row", "col"),
        P(None, "col"),
        P("col", None),
        P("row", None),
        P("row"),
        P(),
        P("row"),
    )
    out_specs = (P("row", "col"), P("row", "col"), P("row", "col"))
    return jax.shard_map(shards, mesh=mesh, in_specs=in_specs, out_specs=out_specs, check_vma=False)
```

```python
import jax
import jax.numpy as jnp
from jax import lax
from jax.sharding import PartitionSpec as P

CONV = 4
LANGS = 32


def passed_along(value, axis, steps):
    count = lax.axis_size(axis)
    first, last = (max(0, -steps), min(count, count - steps))
    return lax.ppermute(value, axis, [(source, source + steps) for source in range(first, last)])


def fetched_columns(tokens):
    n_row, n_col = lax.axis_size("row"), lax.axis_size("col")
    width = tokens.shape[1] // n_row
    if n_col % 2:
        return lax.all_to_all(tokens, "row", 1, 0, tiled=True)
    core = lax.axis_index("col") % 2
    halves = tokens.reshape(tokens.shape[0], n_row, 2, width // 2)
    mine = jnp.take(halves, core, axis=2).reshape(tokens.shape[0], n_row * (width // 2))
    mine = lax.all_to_all(mine, "row", 1, 0, tiled=True)
    other = lax.ppermute(mine, "col", [(c, c ^ 1) for c in range(n_col)])
    return jnp.where(
        core == 0, jnp.concatenate([mine, other], axis=1), jnp.concatenate([other, mine], axis=1)
    )


def placed_blocks(grad_sum, row_count):
    n_row, n_col = lax.axis_size("row"), lax.axis_size("col")
    share = n_row // n_col
    row = lax.axis_index("row")
    got = []
    for m in range(share):
        pairs = [
            (r * n_col + c, (c * share + (r % share + m) % share) * n_col + r // share)
            for r in range(n_row)
            for c in range(n_col)
        ]
        start = ((row % share + m) % share) * row_count
        piece = lax.dynamic_slice_in_dim(grad_sum, start, row_count, axis=0)
        got.append(lax.ppermute(piece, ("row", "col"), pairs))
    pieces = []
    for j in range(share):
        want = (row % share - j) % share
        piece = got[0]
        for m in range(1, share):
            piece = jnp.where(want == m, got[m], piece)
        pieces.append(piece)
    return jnp.concatenate(pieces, axis=1)

def ring_order(count):
    if count % 2:
        return list(range(count))
    return list(range(0, count, 2)) + list(range(count - 1, 0, -2))


def ring_place(axis):
    count = lax.axis_size(axis)
    order = ring_order(count)
    place = jnp.array([order.index(i) for i in range(count)], jnp.int32)[lax.axis_index(axis)]
    ahead = [(order[i], order[(i + 1) % count]) for i in range(count)]
    behind = [(order[(i + 1) % count], order[i]) for i in range(count)]
    return count, jnp.array(order, jnp.int32), place, ahead, behind


def ring_gather(value, axis, chains=2):
    count, order, place, ahead, behind = ring_place(axis)
    parts = jnp.split(value, 2 * chains, axis=1)
    stacks = []
    for number, part in enumerate(parts):
        pairs = ahead if number < chains else behind
        got = [part]
        for _ in range(1, count):
            part = lax.ppermute(part, axis, pairs)
            got.append(part)
        if number >= chains:
            got = [got[(count - s) % count] for s in range(count)]
        stacks.append(jnp.stack(got))
    sources = order[(place - jnp.arange(count)) % count]
    return stacks, sources


def ring_reduce_scatter(token_cols, weight, axis, chains=2):
    count, order, place, ahead, behind = ring_place(axis)
    rows = token_cols.shape[0] // count
    blocks = token_cols.reshape(count, rows, token_cols.shape[1])
    half = weight.shape[1] // 2
    steps = jnp.arange(count)
    first = jnp.take(blocks, order[(place - 1 - steps) % count], axis=0).reshape(token_cols.shape)
    second = jnp.take(blocks, order[(place + 1 + steps) % count], axis=0).reshape(token_cols.shape)
    own_a = jnp.dot(first, weight[:, :half], preferred_element_type=jnp.float32)
    own_b = jnp.dot(second, weight[:, half:], preferred_element_type=jnp.float32)
    owns = jnp.split(own_a.reshape(count, rows, half), chains, axis=2) + jnp.split(
        own_b.reshape(count, rows, weight.shape[1] - half), chains, axis=2
    )
    sums = []
    for number, own in enumerate(owns):
        pairs = ahead if number < chains else behind
        total = own[0].astype(jnp.bfloat16)
        for s in range(1, count):
            total = lax.ppermute(total, axis, pairs)
            total = (total.astype(jnp.float32) + own[s]).astype(jnp.bfloat16)
        sums.append(total)
    return jnp.concatenate(sums, axis=1)

def halves_of(value, dim, upper):
    low, high = jnp.split(value, 2, axis=dim)
    return jnp.where(upper, high, low), jnp.where(upper, low, high)


def col_psum(value, alongside, work):
    core = lax.axis_index("col") % 2 == 1
    keep, give = halves_of(value, 1, core)
    count = lax.axis_size("col")
    got = lax.ppermute(give, "col", [(c, c ^ 1) for c in range(count)])
    pair = keep.astype(jnp.float32) + got.astype(jnp.float32)
    sent, alongside = lax.optimization_barrier((pair.astype(jnp.bfloat16), alongside))
    got, done = lax.optimization_barrier(
        (lax.ppermute(sent, "col", [(c, c ^ 2) for c in range(count)]), work(*alongside))
    )
    total = pair + got.astype(jnp.float32)
    other = lax.ppermute(total, "col", [(c, c ^ 1) for c in range(count)])
    return jnp.where(
        core, jnp.concatenate([other, total], axis=1), jnp.concatenate([total, other], axis=1)
    ), done


def col_psum_scatter(value):
    col = lax.axis_index("col")
    count = lax.axis_size("col")
    quarters = value.reshape(2, 2, value.shape[0] // 4, value.shape[1])
    keep = jnp.take(quarters, col % 2, axis=1)
    give = jnp.take(quarters, 1 - col % 2, axis=1)
    got = lax.ppermute(give, "col", [(c, c ^ 1) for c in range(count)])
    pair = keep.astype(jnp.float32) + got.astype(jnp.float32)
    mine = jnp.take(pair, col // 2, axis=0)
    theirs = jnp.take(pair, 1 - col // 2, axis=0)
    got = lax.ppermute(theirs.astype(jnp.bfloat16), "col", [(c, c ^ 2) for c in range(count)])
    return (mine + got.astype(jnp.float32)).astype(jnp.bfloat16)


def silu_grad(argument):
    sigmoid_v = jax.nn.sigmoid(argument)
    return sigmoid_v * (1.0 + argument * (1.0 - sigmoid_v))


def shards(
    tokens, in_weight, gate_branch, conv_weight, out_weight, target, lang_ids, lang_weight, doc_pos
):
    row_count = tokens.shape[0]
    inner_width = gate_branch.shape[1]
    margin = CONV - 1
    moves_tokens = (
        row_count * lax.axis_size("row") < tokens.shape[1]
        and lax.axis_size("row") % lax.axis_size("col") == 0
    )
    if moves_tokens:
        inner_x = ring_reduce_scatter(fetched_columns(tokens), in_weight, "row")
    else:
        full_in = lax.all_gather(in_weight, "row", axis=0, tiled=True)
        inner_x = jnp.dot(tokens, full_in, preferred_element_type=jnp.float32).astype(jnp.bfloat16)
    from_prev = passed_along(inner_x[row_count - margin :], "row", 1)
    extended = jnp.concatenate([from_prev, inner_x], axis=0).astype(jnp.float32)
    conv_sum = jnp.zeros((row_count, inner_width), jnp.float32)
    for offset in range(CONV):
        keep_mask = (doc_pos >= offset).astype(jnp.float32)[:, None]
        conv_sum = (
            conv_sum
            + conv_weight[offset][None, :]
            * extended[margin - offset : margin - offset + row_count]
            * keep_mask
        )
    gate_value = gate_branch.astype(jnp.float32)
    gate_act = jax.nn.silu(gate_value)
    conv_act = jax.nn.silu(conv_sum)
    mixed = (conv_act * gate_act).astype(jnp.bfloat16)
    partial_value = jnp.dot(mixed, out_weight, preferred_element_type=jnp.float32)
    columns = tokens.shape[1] // lax.axis_size("col")
    col_start = lax.axis_index("col") * columns
    lang_table = (lang_ids[:, None] == jnp.arange(LANGS, dtype=jnp.int32)[None, :]).astype(
        jnp.float32
    )
    token_weight = jnp.sum(lang_table * lang_weight[None, :], axis=1)[:, None]
    if moves_tokens and lax.axis_size("col") == 4:
        out_total, (conv_scale, gate_scale) = col_psum(
            partial_value.astype(jnp.bfloat16),
            (gate_value, conv_sum),
            lambda gate, conv: (jax.nn.silu(gate) * silu_grad(conv), jax.nn.silu(conv) * silu_grad(gate)),
        )
    else:
        out_total = lax.psum(partial_value.astype(jnp.bfloat16), "col").astype(jnp.float32)
        conv_scale = gate_act * silu_grad(conv_sum)
        gate_scale = conv_act * silu_grad(gate_value)
    out_block = lax.dynamic_slice_in_dim(out_total, col_start, columns, 1)
    residual_grad = (token_weight * (out_total - target.astype(jnp.float32))).astype(jnp.bfloat16)
    grad_mixed = lax.dot_general(
        residual_grad, out_weight, (((1,), (1,)), ((), ())), preferred_element_type=jnp.float32
    )
    grad_conv = grad_mixed * conv_scale
    grad_gate = (grad_mixed * gate_scale).astype(jnp.bfloat16)
    local_grad = conv_weight[0][None, :] * grad_conv
    spill_over = jnp.zeros((margin, inner_width), jnp.float32)
    for offset in range(1, CONV):
        masked = (
            conv_weight[offset][None, :]
            * grad_conv
            * (doc_pos >= offset).astype(jnp.float32)[:, None]
        )
        local_grad = local_grad + jnp.concatenate(
            [masked[offset:], jnp.zeros((offset, inner_width), jnp.float32)], axis=0
        )
        spill_over = spill_over + jnp.concatenate(
            [jnp.zeros((margin - offset, inner_width), jnp.float32), masked[:offset]], axis=0
        )
    from_next = passed_along(spill_over, "row", -1)
    grad_x = (
        local_grad
        + jnp.concatenate(
            [jnp.zeros((row_count - margin, inner_width), jnp.float32), from_next], axis=0
        )
    ).astype(jnp.bfloat16)
    if moves_tokens:
        stacks, sources = ring_gather(grad_x, "row")
        contract = (((2,), (1,)), ((), ()))
        weight_parts = jnp.split(in_weight, len(stacks), axis=1)
        grad_cols = lax.dot_general(
            stacks[0], weight_parts[0], contract, preferred_element_type=jnp.float32
        )
        for stack, weight_part in zip(stacks[1:], weight_parts[1:]):
            grad_cols = grad_cols + lax.dot_general(
                stack, weight_part, contract, preferred_element_type=jnp.float32
            )
        grad_cols = jnp.take(grad_cols.astype(jnp.bfloat16), jnp.argsort(sources), axis=0)
        grad_cols = grad_cols.reshape(-1, grad_cols.shape[2])
        if lax.axis_size("col") == 4:
            grad_sum = col_psum_scatter(grad_cols)
        else:
            grad_sum = lax.psum_scatter(grad_cols, "col", scatter_dimension=0, tiled=True)
        grad_tokens = placed_blocks(grad_sum, row_count)
    else:
        partial_grad = lax.dot_general(
            grad_x, full_in, (((1,), (1,)), ((), ())), preferred_element_type=jnp.float32
        )
        grad_tokens = lax.psum_scatter(
            partial_grad.astype(jnp.bfloat16), "col", scatter_dimension=1, tiled=True
        )
    return (out_block.astype(jnp.bfloat16), grad_tokens, grad_gate)


def solution(mesh):
    in_specs = (
        P("row", None),
        P("row", "col"),
        P("row", "col"),
        P(None, "col"),
        P("col", None),
        P("row", None),
        P("row"),
        P(),
        P("row"),
    )
    out_specs = (P("row", "col"), P("row", "col"), P("row", "col"))
    return jax.shard_map(shards, mesh=mesh, in_specs=in_specs, out_specs=out_specs, check_vma=False)
```

```python
import jax
import jax.numpy as jnp
from jax import lax
from jax.sharding import PartitionSpec as P

CONV = 4
LANGS = 32


def passed_along(value, axis, steps):
    count = lax.axis_size(axis)
    first, last = (max(0, -steps), min(count, count - steps))
    return lax.ppermute(value, axis, [(source, source + steps) for source in range(first, last)])


def fetched_columns(tokens):
    n_row, n_col = lax.axis_size("row"), lax.axis_size("col")
    width = tokens.shape[1] // n_row
    if n_col % 2:
        return lax.all_to_all(tokens, "row", 1, 0, tiled=True)
    core = lax.axis_index("col") % 2
    halves = tokens.reshape(tokens.shape[0], n_row, 2, width // 2)
    mine = jnp.take(halves, core, axis=2).reshape(tokens.shape[0], n_row * (width // 2))
    mine = lax.all_to_all(mine, "row", 1, 0, tiled=True)
    other = lax.ppermute(mine, "col", [(c, c ^ 1) for c in range(n_col)])
    return jnp.where(
        core == 0, jnp.concatenate([mine, other], axis=1), jnp.concatenate([other, mine], axis=1)
    )


def placed_blocks(grad_sum, row_count):
    n_row, n_col = lax.axis_size("row"), lax.axis_size("col")
    share = n_row // n_col
    row = lax.axis_index("row")
    got = []
    for m in range(share):
        pairs = [
            (r * n_col + c, (c * share + (r % share + m) % share) * n_col + r // share)
            for r in range(n_row)
            for c in range(n_col)
        ]
        start = ((row % share + m) % share) * row_count
        piece = lax.dynamic_slice_in_dim(grad_sum, start, row_count, axis=0)
        got.append(lax.ppermute(piece, ("row", "col"), pairs))
    pieces = []
    for j in range(share):
        want = (row % share - j) % share
        piece = got[0]
        for m in range(1, share):
            piece = jnp.where(want == m, got[m], piece)
        pieces.append(piece)
    return jnp.concatenate(pieces, axis=1)

def ring_order(count):
    if count % 2:
        return list(range(count))
    return list(range(0, count, 2)) + list(range(count - 1, 0, -2))


def ring_place(axis):
    count = lax.axis_size(axis)
    order = ring_order(count)
    place = jnp.array([order.index(i) for i in range(count)], jnp.int32)[lax.axis_index(axis)]
    ahead = [(order[i], order[(i + 1) % count]) for i in range(count)]
    behind = [(order[(i + 1) % count], order[i]) for i in range(count)]
    return count, jnp.array(order, jnp.int32), place, ahead, behind


def ring_gather(value, axis, chains=2):
    count, order, place, ahead, behind = ring_place(axis)
    parts = jnp.split(value, 2 * chains, axis=1)
    stacks = []
    for number, part in enumerate(parts):
        pairs = ahead if number < chains else behind
        got = [part]
        for _ in range(1, count):
            part = lax.ppermute(part, axis, pairs)
            got.append(part)
        if number >= chains:
            got = [got[(count - s) % count] for s in range(count)]
        stacks.append(jnp.stack(got))
    sources = order[(place - jnp.arange(count)) % count]
    return stacks, sources


def ring_reduce_scatter(token_cols, weight, axis, chains=2):
    count, order, place, ahead, behind = ring_place(axis)
    rows = token_cols.shape[0] // count
    blocks = token_cols.reshape(count, rows, token_cols.shape[1])
    half = weight.shape[1] // 2
    steps = jnp.arange(count)
    first = jnp.take(blocks, order[(place - 1 - steps) % count], axis=0).reshape(token_cols.shape)
    second = jnp.take(blocks, order[(place + 1 + steps) % count], axis=0).reshape(token_cols.shape)
    own_a = jnp.dot(first, weight[:, :half], preferred_element_type=jnp.float32)
    own_b = jnp.dot(second, weight[:, half:], preferred_element_type=jnp.float32)
    owns = jnp.split(own_a.reshape(count, rows, half), chains, axis=2) + jnp.split(
        own_b.reshape(count, rows, weight.shape[1] - half), chains, axis=2
    )
    sums = []
    for number, own in enumerate(owns):
        pairs = ahead if number < chains else behind
        total = own[0].astype(jnp.bfloat16)
        for s in range(1, count):
            total = lax.ppermute(total, axis, pairs)
            total = (total.astype(jnp.float32) + own[s]).astype(jnp.bfloat16)
        sums.append(total)
    return jnp.concatenate(sums, axis=1)

def halves_of(value, dim, upper):
    low, high = jnp.split(value, 2, axis=dim)
    return jnp.where(upper, high, low), jnp.where(upper, low, high)


def col_psum(value):
    core = lax.axis_index("col") % 2 == 1
    keep, give = halves_of(value, 1, core)
    count = lax.axis_size("col")
    got = lax.ppermute(give, "col", [(c, c ^ 1) for c in range(count)])
    pair = keep.astype(jnp.float32) + got.astype(jnp.float32)
    total = pair + lax.ppermute(
        pair.astype(jnp.bfloat16), "col", [(c, c ^ 2) for c in range(count)]
    ).astype(jnp.float32)
    other = lax.ppermute(total, "col", [(c, c ^ 1) for c in range(count)])
    return jnp.where(
        core, jnp.concatenate([other, total], axis=1), jnp.concatenate([total, other], axis=1)
    )


def col_psum_scatter(value):
    col = lax.axis_index("col")
    count = lax.axis_size("col")
    quarters = value.reshape(2, 2, value.shape[0] // 4, value.shape[1])
    keep = jnp.take(quarters, col % 2, axis=1)
    give = jnp.take(quarters, 1 - col % 2, axis=1)
    got = lax.ppermute(give, "col", [(c, c ^ 1) for c in range(count)])
    pair = keep.astype(jnp.float32) + got.astype(jnp.float32)
    mine = jnp.take(pair, col // 2, axis=0)
    theirs = jnp.take(pair, 1 - col // 2, axis=0)
    got = lax.ppermute(theirs.astype(jnp.bfloat16), "col", [(c, c ^ 2) for c in range(count)])
    return (mine + got.astype(jnp.float32)).astype(jnp.bfloat16)


def silu_grad(argument):
    sigmoid_v = jax.nn.sigmoid(argument)
    return sigmoid_v * (1.0 + argument * (1.0 - sigmoid_v))


def shards(
    tokens, in_weight, gate_branch, conv_weight, out_weight, target, lang_ids, lang_weight, doc_pos
):
    row_count = tokens.shape[0]
    inner_width = gate_branch.shape[1]
    margin = CONV - 1
    moves_tokens = (
        row_count * lax.axis_size("row") < tokens.shape[1]
        and lax.axis_size("row") % lax.axis_size("col") == 0
    )
    if moves_tokens:
        inner_x = ring_reduce_scatter(fetched_columns(tokens), in_weight, "row")
    else:
        full_in = lax.all_gather(in_weight, "row", axis=0, tiled=True)
        inner_x = jnp.dot(tokens, full_in, preferred_element_type=jnp.float32).astype(jnp.bfloat16)
    from_prev = passed_along(inner_x[row_count - margin :], "row", 1)
    extended = jnp.concatenate([from_prev, inner_x], axis=0).astype(jnp.float32)
    conv_sum = jnp.zeros((row_count, inner_width), jnp.float32)
    for offset in range(CONV):
        keep_mask = (doc_pos >= offset).astype(jnp.float32)[:, None]
        conv_sum = (
            conv_sum
            + conv_weight[offset][None, :]
            * extended[margin - offset : margin - offset + row_count]
            * keep_mask
        )
    gate_value = gate_branch.astype(jnp.float32)
    gate_act = jax.nn.silu(gate_value)
    conv_act = jax.nn.silu(conv_sum)
    mixed = (conv_act * gate_act).astype(jnp.bfloat16)
    partial_value = jnp.dot(mixed, out_weight, preferred_element_type=jnp.float32)
    columns = tokens.shape[1] // lax.axis_size("col")
    col_start = lax.axis_index("col") * columns
    lang_table = (lang_ids[:, None] == jnp.arange(LANGS, dtype=jnp.int32)[None, :]).astype(
        jnp.float32
    )
    token_weight = jnp.sum(lang_table * lang_weight[None, :], axis=1)[:, None]
    if moves_tokens and lax.axis_size("col") == 4:
        out_total = col_psum(partial_value.astype(jnp.bfloat16))
    else:
        out_total = lax.psum(partial_value.astype(jnp.bfloat16), "col").astype(jnp.float32)
    out_block = lax.dynamic_slice_in_dim(out_total, col_start, columns, 1)
    residual_grad = (token_weight * (out_total - target.astype(jnp.float32))).astype(jnp.bfloat16)
    grad_mixed = lax.dot_general(
        residual_grad, out_weight, (((1,), (1,)), ((), ())), preferred_element_type=jnp.float32
    )
    grad_conv = grad_mixed * gate_act * silu_grad(conv_sum)
    grad_gate = (grad_mixed * conv_act * silu_grad(gate_value)).astype(jnp.bfloat16)
    local_grad = conv_weight[0][None, :] * grad_conv
    spill_over = jnp.zeros((margin, inner_width), jnp.float32)
    for offset in range(1, CONV):
        masked = (
            conv_weight[offset][None, :]
            * grad_conv
            * (doc_pos >= offset).astype(jnp.float32)[:, None]
        )
        local_grad = local_grad + jnp.concatenate(
            [masked[offset:], jnp.zeros((offset, inner_width), jnp.float32)], axis=0
        )
        spill_over = spill_over + jnp.concatenate(
            [jnp.zeros((margin - offset, inner_width), jnp.float32), masked[:offset]], axis=0
        )
    if moves_tokens:
        carried = jnp.concatenate(
            [local_grad.astype(jnp.bfloat16), spill_over.astype(jnp.bfloat16)], axis=0
        )
        carried_stacks, sources = ring_gather(carried, "row")
        count = lax.axis_size("row")
        position = jnp.argsort(sources)
        after = jnp.where(sources + 1 < count, position[jnp.minimum(sources + 1, count - 1)], count)
        stacks = []
        for stack in carried_stacks:
            spills = jnp.concatenate(
                [stack[:, row_count:], jnp.zeros((1, margin, stack.shape[2]), jnp.bfloat16)], axis=0
            )
            last = (
                stack[:, row_count - margin : row_count].astype(jnp.float32)
                + jnp.take(spills, after, axis=0).astype(jnp.float32)
            ).astype(jnp.bfloat16)
            stacks.append(jnp.concatenate([stack[:, : row_count - margin], last], axis=1))
        contract = (((2,), (1,)), ((), ()))
        weight_parts = jnp.split(in_weight, len(stacks), axis=1)
        grad_cols = lax.dot_general(
            stacks[0], weight_parts[0], contract, preferred_element_type=jnp.float32
        )
        for stack, weight_part in zip(stacks[1:], weight_parts[1:]):
            grad_cols = grad_cols + lax.dot_general(
                stack, weight_part, contract, preferred_element_type=jnp.float32
            )
        grad_cols = jnp.take(grad_cols.astype(jnp.bfloat16), jnp.argsort(sources), axis=0)
        grad_cols = grad_cols.reshape(-1, grad_cols.shape[2])
        if lax.axis_size("col") == 4:
            grad_sum = col_psum_scatter(grad_cols)
        else:
            grad_sum = lax.psum_scatter(grad_cols, "col", scatter_dimension=0, tiled=True)
        grad_tokens = placed_blocks(grad_sum, row_count)
    else:
        from_next = passed_along(spill_over, "row", -1)
        grad_x = (
            local_grad
            + jnp.concatenate(
                [jnp.zeros((row_count - margin, inner_width), jnp.float32), from_next], axis=0
            )
        ).astype(jnp.bfloat16)
        partial_grad = lax.dot_general(
            grad_x, full_in, (((1,), (1,)), ((), ())), preferred_element_type=jnp.float32
        )
        grad_tokens = lax.psum_scatter(
            partial_grad.astype(jnp.bfloat16), "col", scatter_dimension=1, tiled=True
        )
    return (out_block.astype(jnp.bfloat16), grad_tokens, grad_gate)


def solution(mesh):
    in_specs = (
        P("row", None),
        P("row", "col"),
        P("row", "col"),
        P(None, "col"),
        P("col", None),
        P("row", None),
        P("row"),
        P(),
        P("row"),
    )
    out_specs = (P("row", "col"), P("row", "col"), P("row", "col"))
    return jax.shard_map(shards, mesh=mesh, in_specs=in_specs, out_specs=out_specs, check_vma=False)
```

```python
import jax
import jax.numpy as jnp
from jax import lax
from jax.sharding import PartitionSpec as P

CONV = 4
LANGS = 32


def passed_along(value, axis, steps):
    count = lax.axis_size(axis)
    first, last = (max(0, -steps), min(count, count - steps))
    return lax.ppermute(value, axis, [(source, source + steps) for source in range(first, last)])


def fetched_columns(tokens):
    n_row, n_col = lax.axis_size("row"), lax.axis_size("col")
    width = tokens.shape[1] // n_row
    if n_col % 2:
        return lax.all_to_all(tokens, "row", 1, 0, tiled=True)
    core = lax.axis_index("col") % 2
    halves = tokens.reshape(tokens.shape[0], n_row, 2, width // 2)
    mine = jnp.take(halves, core, axis=2).reshape(tokens.shape[0], n_row * (width // 2))
    mine = lax.all_to_all(mine, "row", 1, 0, tiled=True)
    other = lax.ppermute(mine, "col", [(c, c ^ 1) for c in range(n_col)])
    return jnp.where(
        core == 0, jnp.concatenate([mine, other], axis=1), jnp.concatenate([other, mine], axis=1)
    )


def placed_blocks(grad_sum, row_count):
    n_row, n_col = lax.axis_size("row"), lax.axis_size("col")
    share = n_row // n_col
    row = lax.axis_index("row")
    got = []
    for m in range(share):
        pairs = [
            (r * n_col + c, (c * share + (r % share + m) % share) * n_col + r // share)
            for r in range(n_row)
            for c in range(n_col)
        ]
        start = ((row % share + m) % share) * row_count
        piece = lax.dynamic_slice_in_dim(grad_sum, start, row_count, axis=0)
        got.append(lax.ppermute(piece, ("row", "col"), pairs))
    pieces = []
    for j in range(share):
        want = (row % share - j) % share
        piece = got[0]
        for m in range(1, share):
            piece = jnp.where(want == m, got[m], piece)
        pieces.append(piece)
    return jnp.concatenate(pieces, axis=1)

def ring_order(count):
    if count % 2:
        return list(range(count))
    return list(range(0, count, 2)) + list(range(count - 1, 0, -2))


def ring_place(axis):
    count = lax.axis_size(axis)
    order = ring_order(count)
    place = jnp.array([order.index(i) for i in range(count)], jnp.int32)[lax.axis_index(axis)]
    ahead = [(order[i], order[(i + 1) % count]) for i in range(count)]
    behind = [(order[(i + 1) % count], order[i]) for i in range(count)]
    return count, jnp.array(order, jnp.int32), place, ahead, behind


def ring_gather(value, axis, chains=2):
    count, order, place, ahead, behind = ring_place(axis)
    parts = jnp.split(value, 2 * chains, axis=1)
    stacks = []
    for number, part in enumerate(parts):
        pairs = ahead if number < chains else behind
        got = [part]
        for _ in range(1, count):
            part = lax.ppermute(part, axis, pairs)
            got.append(part)
        if number >= chains:
            got = [got[(count - s) % count] for s in range(count)]
        stacks.append(jnp.stack(got))
    sources = order[(place - jnp.arange(count)) % count]
    return stacks, sources


def ring_reduce_scatter(token_cols, weight, axis, chains=2):
    count, order, place, ahead, behind = ring_place(axis)
    rows = token_cols.shape[0] // count
    blocks = token_cols.reshape(count, rows, token_cols.shape[1])
    half = weight.shape[1] // 2
    steps = jnp.arange(1, count)
    later = (count - 1) * rows
    first_0 = jnp.take(blocks, order[(place - 1) % count], axis=0)
    second_0 = jnp.take(blocks, order[(place + 1) % count], axis=0)
    start_a = jnp.dot(first_0, weight[:, :half], preferred_element_type=jnp.float32)
    start_b = jnp.dot(second_0, weight[:, half:], preferred_element_type=jnp.float32)
    first = jnp.take(blocks, order[(place - 1 - steps) % count], axis=0).reshape(later, -1)
    second = jnp.take(blocks, order[(place + 1 + steps) % count], axis=0).reshape(later, -1)
    own_a = jnp.dot(first, weight[:, :half], preferred_element_type=jnp.float32)
    own_b = jnp.dot(second, weight[:, half:], preferred_element_type=jnp.float32)
    own_a = own_a.reshape(count - 1, rows, half)
    own_b = own_b.reshape(count - 1, rows, weight.shape[1] - half)
    starts = jnp.split(start_a, chains, axis=1) + jnp.split(start_b, chains, axis=1)
    owns = jnp.split(own_a, chains, axis=2) + jnp.split(own_b, chains, axis=2)
    sums = []
    for number, (start, own) in enumerate(zip(starts, owns)):
        pairs = ahead if number < chains else behind
        total = start.astype(jnp.bfloat16)
        for s in range(1, count):
            total = lax.ppermute(total, axis, pairs)
            total = (total.astype(jnp.float32) + own[s - 1]).astype(jnp.bfloat16)
        sums.append(total)
    return jnp.concatenate(sums, axis=1)

def halves_of(value, dim, upper):
    low, high = jnp.split(value, 2, axis=dim)
    return jnp.where(upper, high, low), jnp.where(upper, low, high)


def col_psum(value):
    core = lax.axis_index("col") % 2 == 1
    keep, give = halves_of(value, 1, core)
    count = lax.axis_size("col")
    got = lax.ppermute(give, "col", [(c, c ^ 1) for c in range(count)])
    pair = keep.astype(jnp.float32) + got.astype(jnp.float32)
    total = pair + lax.ppermute(
        pair.astype(jnp.bfloat16), "col", [(c, c ^ 2) for c in range(count)]
    ).astype(jnp.float32)
    other = lax.ppermute(total, "col", [(c, c ^ 1) for c in range(count)])
    return jnp.where(
        core, jnp.concatenate([other, total], axis=1), jnp.concatenate([total, other], axis=1)
    )


def col_psum_scatter(value):
    col = lax.axis_index("col")
    count = lax.axis_size("col")
    quarters = value.reshape(2, 2, value.shape[0] // 4, value.shape[1])
    keep = jnp.take(quarters, col % 2, axis=1)
    give = jnp.take(quarters, 1 - col % 2, axis=1)
    got = lax.ppermute(give, "col", [(c, c ^ 1) for c in range(count)])
    pair = keep.astype(jnp.float32) + got.astype(jnp.float32)
    mine = jnp.take(pair, col // 2, axis=0)
    theirs = jnp.take(pair, 1 - col // 2, axis=0)
    got = lax.ppermute(theirs.astype(jnp.bfloat16), "col", [(c, c ^ 2) for c in range(count)])
    return (mine + got.astype(jnp.float32)).astype(jnp.bfloat16)


def silu_grad(argument):
    sigmoid_v = jax.nn.sigmoid(argument)
    return sigmoid_v * (1.0 + argument * (1.0 - sigmoid_v))


def shards(
    tokens, in_weight, gate_branch, conv_weight, out_weight, target, lang_ids, lang_weight, doc_pos
):
    row_count = tokens.shape[0]
    inner_width = gate_branch.shape[1]
    margin = CONV - 1
    moves_tokens = (
        row_count * lax.axis_size("row") < tokens.shape[1]
        and lax.axis_size("row") % lax.axis_size("col") == 0
    )
    if moves_tokens:
        inner_x = ring_reduce_scatter(fetched_columns(tokens), in_weight, "row")
    else:
        full_in = lax.all_gather(in_weight, "row", axis=0, tiled=True)
        inner_x = jnp.dot(tokens, full_in, preferred_element_type=jnp.float32).astype(jnp.bfloat16)
    from_prev = passed_along(inner_x[row_count - margin :], "row", 1)
    extended = jnp.concatenate([from_prev, inner_x], axis=0).astype(jnp.float32)
    conv_sum = jnp.zeros((row_count, inner_width), jnp.float32)
    for offset in range(CONV):
        keep_mask = (doc_pos >= offset).astype(jnp.float32)[:, None]
        conv_sum = (
            conv_sum
            + conv_weight[offset][None, :]
            * extended[margin - offset : margin - offset + row_count]
            * keep_mask
        )
    gate_value = gate_branch.astype(jnp.float32)
    gate_act = jax.nn.silu(gate_value)
    conv_act = jax.nn.silu(conv_sum)
    mixed = (conv_act * gate_act).astype(jnp.bfloat16)
    partial_value = jnp.dot(mixed, out_weight, preferred_element_type=jnp.float32)
    columns = tokens.shape[1] // lax.axis_size("col")
    col_start = lax.axis_index("col") * columns
    lang_table = (lang_ids[:, None] == jnp.arange(LANGS, dtype=jnp.int32)[None, :]).astype(
        jnp.float32
    )
    token_weight = jnp.sum(lang_table * lang_weight[None, :], axis=1)[:, None]
    if moves_tokens and lax.axis_size("col") == 4:
        out_total = col_psum(partial_value.astype(jnp.bfloat16))
    else:
        out_total = lax.psum(partial_value.astype(jnp.bfloat16), "col").astype(jnp.float32)
    out_block = lax.dynamic_slice_in_dim(out_total, col_start, columns, 1)
    residual_grad = (token_weight * (out_total - target.astype(jnp.float32))).astype(jnp.bfloat16)
    grad_mixed = lax.dot_general(
        residual_grad, out_weight, (((1,), (1,)), ((), ())), preferred_element_type=jnp.float32
    )
    grad_conv = grad_mixed * gate_act * silu_grad(conv_sum)
    grad_gate = (grad_mixed * conv_act * silu_grad(gate_value)).astype(jnp.bfloat16)
    local_grad = conv_weight[0][None, :] * grad_conv
    spill_over = jnp.zeros((margin, inner_width), jnp.float32)
    for offset in range(1, CONV):
        masked = (
            conv_weight[offset][None, :]
            * grad_conv
            * (doc_pos >= offset).astype(jnp.float32)[:, None]
        )
        local_grad = local_grad + jnp.concatenate(
            [masked[offset:], jnp.zeros((offset, inner_width), jnp.float32)], axis=0
        )
        spill_over = spill_over + jnp.concatenate(
            [jnp.zeros((margin - offset, inner_width), jnp.float32), masked[:offset]], axis=0
        )
    from_next = passed_along(spill_over, "row", -1)
    grad_x = (
        local_grad
        + jnp.concatenate(
            [jnp.zeros((row_count - margin, inner_width), jnp.float32), from_next], axis=0
        )
    ).astype(jnp.bfloat16)
    if moves_tokens:
        stacks, sources = ring_gather(grad_x, "row")
        contract = (((2,), (1,)), ((), ()))
        weight_parts = jnp.split(in_weight, len(stacks), axis=1)
        grad_cols = lax.dot_general(
            stacks[0], weight_parts[0], contract, preferred_element_type=jnp.float32
        )
        for stack, weight_part in zip(stacks[1:], weight_parts[1:]):
            grad_cols = grad_cols + lax.dot_general(
                stack, weight_part, contract, preferred_element_type=jnp.float32
            )
        grad_cols = jnp.take(grad_cols.astype(jnp.bfloat16), jnp.argsort(sources), axis=0)
        grad_cols = grad_cols.reshape(-1, grad_cols.shape[2])
        if lax.axis_size("col") == 4:
            grad_sum = col_psum_scatter(grad_cols)
        else:
            grad_sum = lax.psum_scatter(grad_cols, "col", scatter_dimension=0, tiled=True)
        grad_tokens = placed_blocks(grad_sum, row_count)
    else:
        partial_grad = lax.dot_general(
            grad_x, full_in, (((1,), (1,)), ((), ())), preferred_element_type=jnp.float32
        )
        grad_tokens = lax.psum_scatter(
            partial_grad.astype(jnp.bfloat16), "col", scatter_dimension=1, tiled=True
        )
    return (out_block.astype(jnp.bfloat16), grad_tokens, grad_gate)


def solution(mesh):
    in_specs = (
        P("row", None),
        P("row", "col"),
        P("row", "col"),
        P(None, "col"),
        P("col", None),
        P("row", None),
        P("row"),
        P(),
        P("row"),
    )
    out_specs = (P("row", "col"), P("row", "col"), P("row", "col"))
    return jax.shard_map(shards, mesh=mesh, in_specs=in_specs, out_specs=out_specs, check_vma=False)
```

```python
import jax
import jax.numpy as jnp
from jax import lax
from jax.sharding import PartitionSpec as P

CONV = 4
LANGS = 32


def passed_along(value, axis, steps):
    count = lax.axis_size(axis)
    first, last = (max(0, -steps), min(count, count - steps))
    return lax.ppermute(value, axis, [(source, source + steps) for source in range(first, last)])


def fetched_columns(tokens):
    n_row, n_col = lax.axis_size("row"), lax.axis_size("col")
    width = tokens.shape[1] // n_row
    if n_col % 2:
        return lax.all_to_all(tokens, "row", 1, 0, tiled=True)
    core = lax.axis_index("col") % 2
    halves = tokens.reshape(tokens.shape[0], n_row, 2, width // 2)
    mine = jnp.take(halves, core, axis=2).reshape(tokens.shape[0], n_row * (width // 2))
    mine = lax.all_to_all(mine, "row", 1, 0, tiled=True)
    other = lax.ppermute(mine, "col", [(c, c ^ 1) for c in range(n_col)])
    return jnp.where(
        core == 0, jnp.concatenate([mine, other], axis=1), jnp.concatenate([other, mine], axis=1)
    )


def placed_blocks(grad_sum, row_count):
    n_row, n_col = lax.axis_size("row"), lax.axis_size("col")
    share = n_row // n_col
    row = lax.axis_index("row")
    got = []
    for m in range(share):
        pairs = [
            (r * n_col + c, (c * share + (r % share + m) % share) * n_col + r // share)
            for r in range(n_row)
            for c in range(n_col)
        ]
        start = ((row % share + m) % share) * row_count
        piece = lax.dynamic_slice_in_dim(grad_sum, start, row_count, axis=0)
        got.append(lax.ppermute(piece, ("row", "col"), pairs))
    pieces = []
    for j in range(share):
        want = (row % share - j) % share
        piece = got[0]
        for m in range(1, share):
            piece = jnp.where(want == m, got[m], piece)
        pieces.append(piece)
    return jnp.concatenate(pieces, axis=1)

def placed_sums(grad_cols, row_count):
    n_row, n_col = lax.axis_size("row"), lax.axis_size("col")
    row, col = lax.axis_index("row"), lax.axis_index("col")
    core, chip = col % 2, col // 2
    quarters = grad_cols.reshape(2, 2, grad_cols.shape[0] // 4, grad_cols.shape[1])
    keep = jnp.take(quarters, core, axis=1)
    give = jnp.take(quarters, 1 - core, axis=1)
    got = lax.ppermute(give, "col", [(c, c ^ 1) for c in range(n_col)])
    pair = (keep.astype(jnp.float32) + got.astype(jnp.float32)).astype(jnp.bfloat16)
    pieces = pair.reshape(2, 2, row_count, grad_cols.shape[1])
    arrived = {}
    for a in range(2):
        for b in range(2):
            pairs = [
                (r * n_col + c, (2 * (((c // 2) ^ b) * 2 + c % 2) + ((r % 2) ^ a)) * n_col + r // 2)
                for r in range(n_row)
                for c in range(n_col)
            ]
            piece = jnp.take(jnp.take(pieces, chip ^ b, axis=0), (row % 2) ^ a, axis=0)
            arrived[a, b] = lax.ppermute(piece, ("row", "col"), pairs).astype(jnp.float32)
    sums = [arrived[a, 0] + arrived[a, 1] for a in range(2)]
    return jnp.concatenate(
        [jnp.where((row % 2) ^ j == 0, sums[0], sums[1]).astype(jnp.bfloat16) for j in range(2)], axis=1
    )


def ring_order(count):
    if count % 2:
        return list(range(count))
    return list(range(0, count, 2)) + list(range(count - 1, 0, -2))


def ring_place(axis):
    count = lax.axis_size(axis)
    order = ring_order(count)
    place = jnp.array([order.index(i) for i in range(count)], jnp.int32)[lax.axis_index(axis)]
    ahead = [(order[i], order[(i + 1) % count]) for i in range(count)]
    behind = [(order[(i + 1) % count], order[i]) for i in range(count)]
    return count, jnp.array(order, jnp.int32), place, ahead, behind


def ring_gather(value, axis, chains=2):
    count, order, place, ahead, behind = ring_place(axis)
    parts = jnp.split(value, 2 * chains, axis=1)
    stacks = []
    for number, part in enumerate(parts):
        pairs = ahead if number < chains else behind
        got = [part]
        for _ in range(1, count):
            part = lax.ppermute(part, axis, pairs)
            got.append(part)
        if number >= chains:
            got = [got[(count - s) % count] for s in range(count)]
        stacks.append(jnp.stack(got))
    sources = order[(place - jnp.arange(count)) % count]
    return stacks, sources


def ring_reduce_scatter(token_cols, weight, axis, chains=2):
    count, order, place, ahead, behind = ring_place(axis)
    rows = token_cols.shape[0] // count
    blocks = token_cols.reshape(count, rows, token_cols.shape[1])
    half = weight.shape[1] // 2
    steps = jnp.arange(1, count)
    later = (count - 1) * rows
    first_0 = jnp.take(blocks, order[(place - 1) % count], axis=0)
    second_0 = jnp.take(blocks, order[(place + 1) % count], axis=0)
    start_a = jnp.dot(first_0, weight[:, :half], preferred_element_type=jnp.float32)
    start_b = jnp.dot(second_0, weight[:, half:], preferred_element_type=jnp.float32)
    first = jnp.take(blocks, order[(place - 1 - steps) % count], axis=0).reshape(later, -1)
    second = jnp.take(blocks, order[(place + 1 + steps) % count], axis=0).reshape(later, -1)
    own_a = jnp.dot(first, weight[:, :half], preferred_element_type=jnp.float32)
    own_b = jnp.dot(second, weight[:, half:], preferred_element_type=jnp.float32)
    own_a = own_a.reshape(count - 1, rows, half)
    own_b = own_b.reshape(count - 1, rows, weight.shape[1] - half)
    starts = jnp.split(start_a, chains, axis=1) + jnp.split(start_b, chains, axis=1)
    owns = jnp.split(own_a, chains, axis=2) + jnp.split(own_b, chains, axis=2)
    sums = []
    for number, (start, own) in enumerate(zip(starts, owns)):
        pairs = ahead if number < chains else behind
        total = start.astype(jnp.bfloat16)
        for s in range(1, count):
            total = lax.ppermute(total, axis, pairs)
            total = (total.astype(jnp.float32) + own[s - 1]).astype(jnp.bfloat16)
        sums.append(total)
    return jnp.concatenate(sums, axis=1)

def halves_of(value, dim, upper):
    low, high = jnp.split(value, 2, axis=dim)
    return jnp.where(upper, high, low), jnp.where(upper, low, high)


def col_psum(value):
    core = lax.axis_index("col") % 2 == 1
    keep, give = halves_of(value, 1, core)
    count = lax.axis_size("col")
    got = lax.ppermute(give, "col", [(c, c ^ 1) for c in range(count)])
    pair = keep.astype(jnp.float32) + got.astype(jnp.float32)
    total = pair + lax.ppermute(
        pair.astype(jnp.bfloat16), "col", [(c, c ^ 2) for c in range(count)]
    ).astype(jnp.float32)
    other = lax.ppermute(total, "col", [(c, c ^ 1) for c in range(count)])
    return jnp.where(
        core, jnp.concatenate([other, total], axis=1), jnp.concatenate([total, other], axis=1)
    )


def col_psum_scatter(value):
    col = lax.axis_index("col")
    count = lax.axis_size("col")
    quarters = value.reshape(2, 2, value.shape[0] // 4, value.shape[1])
    keep = jnp.take(quarters, col % 2, axis=1)
    give = jnp.take(quarters, 1 - col % 2, axis=1)
    got = lax.ppermute(give, "col", [(c, c ^ 1) for c in range(count)])
    pair = keep.astype(jnp.float32) + got.astype(jnp.float32)
    mine = jnp.take(pair, col // 2, axis=0)
    theirs = jnp.take(pair, 1 - col // 2, axis=0)
    got = lax.ppermute(theirs.astype(jnp.bfloat16), "col", [(c, c ^ 2) for c in range(count)])
    return (mine + got.astype(jnp.float32)).astype(jnp.bfloat16)


def silu_grad(argument):
    sigmoid_v = jax.nn.sigmoid(argument)
    return sigmoid_v * (1.0 + argument * (1.0 - sigmoid_v))


def shards(
    tokens, in_weight, gate_branch, conv_weight, out_weight, target, lang_ids, lang_weight, doc_pos
):
    row_count = tokens.shape[0]
    inner_width = gate_branch.shape[1]
    margin = CONV - 1
    moves_tokens = (
        row_count * lax.axis_size("row") < tokens.shape[1]
        and lax.axis_size("row") % lax.axis_size("col") == 0
    )
    if moves_tokens:
        inner_x = ring_reduce_scatter(fetched_columns(tokens), in_weight, "row")
    else:
        full_in = lax.all_gather(in_weight, "row", axis=0, tiled=True)
        inner_x = jnp.dot(tokens, full_in, preferred_element_type=jnp.float32).astype(jnp.bfloat16)
    from_prev = passed_along(inner_x[row_count - margin :], "row", 1)
    extended = jnp.concatenate([from_prev, inner_x], axis=0).astype(jnp.float32)
    conv_sum = jnp.zeros((row_count, inner_width), jnp.float32)
    for offset in range(CONV):
        keep_mask = (doc_pos >= offset).astype(jnp.float32)[:, None]
        conv_sum = (
            conv_sum
            + conv_weight[offset][None, :]
            * extended[margin - offset : margin - offset + row_count]
            * keep_mask
        )
    gate_value = gate_branch.astype(jnp.float32)
    gate_act = jax.nn.silu(gate_value)
    conv_act = jax.nn.silu(conv_sum)
    mixed = (conv_act * gate_act).astype(jnp.bfloat16)
    partial_value = jnp.dot(mixed, out_weight, preferred_element_type=jnp.float32)
    columns = tokens.shape[1] // lax.axis_size("col")
    col_start = lax.axis_index("col") * columns
    lang_table = (lang_ids[:, None] == jnp.arange(LANGS, dtype=jnp.int32)[None, :]).astype(
        jnp.float32
    )
    token_weight = jnp.sum(lang_table * lang_weight[None, :], axis=1)[:, None]
    if moves_tokens and lax.axis_size("col") == 4:
        out_total = col_psum(partial_value.astype(jnp.bfloat16))
    else:
        out_total = lax.psum(partial_value.astype(jnp.bfloat16), "col").astype(jnp.float32)
    out_block = lax.dynamic_slice_in_dim(out_total, col_start, columns, 1)
    residual_grad = (token_weight * (out_total - target.astype(jnp.float32))).astype(jnp.bfloat16)
    grad_mixed = lax.dot_general(
        residual_grad, out_weight, (((1,), (1,)), ((), ())), preferred_element_type=jnp.float32
    )
    grad_conv = grad_mixed * gate_act * silu_grad(conv_sum)
    grad_gate = (grad_mixed * conv_act * silu_grad(gate_value)).astype(jnp.bfloat16)
    local_grad = conv_weight[0][None, :] * grad_conv
    spill_over = jnp.zeros((margin, inner_width), jnp.float32)
    for offset in range(1, CONV):
        masked = (
            conv_weight[offset][None, :]
            * grad_conv
            * (doc_pos >= offset).astype(jnp.float32)[:, None]
        )
        local_grad = local_grad + jnp.concatenate(
            [masked[offset:], jnp.zeros((offset, inner_width), jnp.float32)], axis=0
        )
        spill_over = spill_over + jnp.concatenate(
            [jnp.zeros((margin - offset, inner_width), jnp.float32), masked[:offset]], axis=0
        )
    from_next = passed_along(spill_over, "row", -1)
    grad_x = (
        local_grad
        + jnp.concatenate(
            [jnp.zeros((row_count - margin, inner_width), jnp.float32), from_next], axis=0
        )
    ).astype(jnp.bfloat16)
    if moves_tokens:
        stacks, sources = ring_gather(grad_x, "row")
        contract = (((2,), (1,)), ((), ()))
        weight_parts = jnp.split(in_weight, len(stacks), axis=1)
        grad_cols = lax.dot_general(
            stacks[0], weight_parts[0], contract, preferred_element_type=jnp.float32
        )
        for stack, weight_part in zip(stacks[1:], weight_parts[1:]):
            grad_cols = grad_cols + lax.dot_general(
                stack, weight_part, contract, preferred_element_type=jnp.float32
            )
        grad_cols = jnp.take(grad_cols.astype(jnp.bfloat16), jnp.argsort(sources), axis=0)
        grad_cols = grad_cols.reshape(-1, grad_cols.shape[2])
        if lax.axis_size("col") == 4 and lax.axis_size("row") == 8:
            grad_tokens = placed_sums(grad_cols, row_count)
        else:
            grad_sum = lax.psum_scatter(grad_cols, "col", scatter_dimension=0, tiled=True)
            grad_tokens = placed_blocks(grad_sum, row_count)
    else:
        partial_grad = lax.dot_general(
            grad_x, full_in, (((1,), (1,)), ((), ())), preferred_element_type=jnp.float32
        )
        grad_tokens = lax.psum_scatter(
            partial_grad.astype(jnp.bfloat16), "col", scatter_dimension=1, tiled=True
        )
    return (out_block.astype(jnp.bfloat16), grad_tokens, grad_gate)


def solution(mesh):
    in_specs = (
        P("row", None),
        P("row", "col"),
        P("row", "col"),
        P(None, "col"),
        P("col", None),
        P("row", None),
        P("row"),
        P(),
        P("row"),
    )
    out_specs = (P("row", "col"), P("row", "col"), P("row", "col"))
    return jax.shard_map(shards, mesh=mesh, in_specs=in_specs, out_specs=out_specs, check_vma=False)
```

```python
import jax
import jax.numpy as jnp
from jax import lax
from jax.sharding import PartitionSpec as P

CONV = 4
LANGS = 32


def passed_along(value, axis, steps):
    count = lax.axis_size(axis)
    first, last = (max(0, -steps), min(count, count - steps))
    return lax.ppermute(value, axis, [(source, source + steps) for source in range(first, last)])


def fetched_columns(tokens):
    n_row, n_col = lax.axis_size("row"), lax.axis_size("col")
    width = tokens.shape[1] // n_row
    if n_col % 2:
        return lax.all_to_all(tokens, "row", 1, 0, tiled=True)
    core = lax.axis_index("col") % 2
    halves = tokens.reshape(tokens.shape[0], n_row, 2, width // 2)
    mine = jnp.take(halves, core, axis=2).reshape(tokens.shape[0], n_row * (width // 2))
    mine = lax.all_to_all(mine, "row", 1, 0, tiled=True)
    other = lax.ppermute(mine, "col", [(c, c ^ 1) for c in range(n_col)])
    return jnp.where(
        core == 0, jnp.concatenate([mine, other], axis=1), jnp.concatenate([other, mine], axis=1)
    )


def placed_blocks(grad_sum, row_count):
    n_row, n_col = lax.axis_size("row"), lax.axis_size("col")
    share = n_row // n_col
    row = lax.axis_index("row")
    got = []
    for m in range(share):
        pairs = [
            (r * n_col + c, (c * share + (r % share + m) % share) * n_col + r // share)
            for r in range(n_row)
            for c in range(n_col)
        ]
        start = ((row % share + m) % share) * row_count
        piece = lax.dynamic_slice_in_dim(grad_sum, start, row_count, axis=0)
        got.append(lax.ppermute(piece, ("row", "col"), pairs))
    pieces = []
    for j in range(share):
        want = (row % share - j) % share
        piece = got[0]
        for m in range(1, share):
            piece = jnp.where(want == m, got[m], piece)
        pieces.append(piece)
    return jnp.concatenate(pieces, axis=1)

def placed_sums(grad_cols, row_count):
    n_row, n_col = lax.axis_size("row"), lax.axis_size("col")
    row, col = lax.axis_index("row"), lax.axis_index("col")
    core, chip = col % 2, col // 2
    quarters = grad_cols.reshape(2, 2, grad_cols.shape[0] // 4, grad_cols.shape[1])
    keep = jnp.take(quarters, core, axis=1)
    give = jnp.take(quarters, 1 - core, axis=1)
    got = lax.ppermute(give, "col", [(c, c ^ 1) for c in range(n_col)])
    pair = (keep.astype(jnp.float32) + got.astype(jnp.float32)).astype(jnp.bfloat16)
    pieces = pair.reshape(2, 2, row_count, grad_cols.shape[1])
    arrived = {}
    for a in range(2):
        for b in range(2):
            pairs = [
                (r * n_col + c, (2 * (((c // 2) ^ b) * 2 + c % 2) + ((r % 2) ^ a)) * n_col + r // 2)
                for r in range(n_row)
                for c in range(n_col)
            ]
            piece = jnp.take(jnp.take(pieces, chip ^ b, axis=0), (row % 2) ^ a, axis=0)
            arrived[a, b] = lax.ppermute(piece, ("row", "col"), pairs).astype(jnp.float32)
    sums = [arrived[a, 0] + arrived[a, 1] for a in range(2)]
    return jnp.concatenate(
        [jnp.where((row % 2) ^ j == 0, sums[0], sums[1]).astype(jnp.bfloat16) for j in range(2)], axis=1
    )


def ring_order(count):
    if count % 2:
        return list(range(count))
    return list(range(0, count, 2)) + list(range(count - 1, 0, -2))


def ring_place(axis):
    count = lax.axis_size(axis)
    order = ring_order(count)
    place = jnp.array([order.index(i) for i in range(count)], jnp.int32)[lax.axis_index(axis)]
    ahead = [(order[i], order[(i + 1) % count]) for i in range(count)]
    behind = [(order[(i + 1) % count], order[i]) for i in range(count)]
    return count, jnp.array(order, jnp.int32), place, ahead, behind


def ring_gather(value, axis, chains=2):
    count, order, place, ahead, behind = ring_place(axis)
    parts = jnp.split(value, 2 * chains, axis=1)
    stacks = []
    for number, part in enumerate(parts):
        pairs = ahead if number < chains else behind
        got = [part]
        for _ in range(1, count):
            part = lax.ppermute(part, axis, pairs)
            got.append(part)
        if number >= chains:
            got = [got[(count - s) % count] for s in range(count)]
        stacks.append(jnp.stack(got))
    sources = order[(place - jnp.arange(count)) % count]
    return stacks, sources


def ring_reduce_scatter(token_cols, weight, axis, chains=2):
    count, order, place, ahead, behind = ring_place(axis)
    rows = token_cols.shape[0] // count
    blocks = token_cols.reshape(count, rows, token_cols.shape[1])
    half = weight.shape[1] // 2
    steps = jnp.arange(1, count)
    later = (count - 1) * rows
    first_0 = jnp.take(blocks, order[(place - 1) % count], axis=0)
    second_0 = jnp.take(blocks, order[(place + 1) % count], axis=0)
    start_a = jnp.dot(first_0, weight[:, :half], preferred_element_type=jnp.float32)
    start_b = jnp.dot(second_0, weight[:, half:], preferred_element_type=jnp.float32)
    first = jnp.take(blocks, order[(place - 1 - steps) % count], axis=0).reshape(later, -1)
    second = jnp.take(blocks, order[(place + 1 + steps) % count], axis=0).reshape(later, -1)
    own_a = jnp.dot(first, weight[:, :half], preferred_element_type=jnp.float32)
    own_b = jnp.dot(second, weight[:, half:], preferred_element_type=jnp.float32)
    own_a = own_a.reshape(count - 1, rows, half)
    own_b = own_b.reshape(count - 1, rows, weight.shape[1] - half)
    starts = jnp.split(start_a, chains, axis=1) + jnp.split(start_b, chains, axis=1)
    owns = jnp.split(own_a, chains, axis=2) + jnp.split(own_b, chains, axis=2)
    sums = []
    for number, (start, own) in enumerate(zip(starts, owns)):
        pairs = ahead if number < chains else behind
        total = start.astype(jnp.bfloat16)
        for s in range(1, count):
            total = lax.ppermute(total, axis, pairs)
            total = (total.astype(jnp.float32) + own[s - 1]).astype(jnp.bfloat16)
        sums.append(total)
    return jnp.concatenate(sums, axis=1)

def halves_of(value, dim, upper):
    low, high = jnp.split(value, 2, axis=dim)
    return jnp.where(upper, high, low), jnp.where(upper, low, high)


def col_psum(value):
    core = lax.axis_index("col") % 2 == 1
    keep, give = halves_of(value, 1, core)
    count = lax.axis_size("col")
    got = lax.ppermute(give, "col", [(c, c ^ 1) for c in range(count)])
    pair = keep.astype(jnp.float32) + got.astype(jnp.float32)
    totals, others = [], []
    for chunk in jnp.split(pair, 2, axis=1):
        total = chunk + lax.ppermute(
            chunk.astype(jnp.bfloat16), "col", [(c, c ^ 2) for c in range(count)]
        ).astype(jnp.float32)
        totals.append(total)
        others.append(lax.ppermute(total, "col", [(c, c ^ 1) for c in range(count)]))
    total, other = jnp.concatenate(totals, axis=1), jnp.concatenate(others, axis=1)
    return jnp.where(
        core, jnp.concatenate([other, total], axis=1), jnp.concatenate([total, other], axis=1)
    )


def col_psum_scatter(value):
    col = lax.axis_index("col")
    count = lax.axis_size("col")
    quarters = value.reshape(2, 2, value.shape[0] // 4, value.shape[1])
    keep = jnp.take(quarters, col % 2, axis=1)
    give = jnp.take(quarters, 1 - col % 2, axis=1)
    got = lax.ppermute(give, "col", [(c, c ^ 1) for c in range(count)])
    pair = keep.astype(jnp.float32) + got.astype(jnp.float32)
    mine = jnp.take(pair, col // 2, axis=0)
    theirs = jnp.take(pair, 1 - col // 2, axis=0)
    got = lax.ppermute(theirs.astype(jnp.bfloat16), "col", [(c, c ^ 2) for c in range(count)])
    return (mine + got.astype(jnp.float32)).astype(jnp.bfloat16)


def silu_grad(argument):
    sigmoid_v = jax.nn.sigmoid(argument)
    return sigmoid_v * (1.0 + argument * (1.0 - sigmoid_v))


def shards(
    tokens, in_weight, gate_branch, conv_weight, out_weight, target, lang_ids, lang_weight, doc_pos
):
    row_count = tokens.shape[0]
    inner_width = gate_branch.shape[1]
    margin = CONV - 1
    moves_tokens = (
        row_count * lax.axis_size("row") < tokens.shape[1]
        and lax.axis_size("row") % lax.axis_size("col") == 0
    )
    if moves_tokens:
        inner_x = ring_reduce_scatter(fetched_columns(tokens), in_weight, "row")
    else:
        full_in = lax.all_gather(in_weight, "row", axis=0, tiled=True)
        inner_x = jnp.dot(tokens, full_in, preferred_element_type=jnp.float32).astype(jnp.bfloat16)
    from_prev = passed_along(inner_x[row_count - margin :], "row", 1)
    extended = jnp.concatenate([from_prev, inner_x], axis=0).astype(jnp.float32)
    conv_sum = jnp.zeros((row_count, inner_width), jnp.float32)
    for offset in range(CONV):
        keep_mask = (doc_pos >= offset).astype(jnp.float32)[:, None]
        conv_sum = (
            conv_sum
            + conv_weight[offset][None, :]
            * extended[margin - offset : margin - offset + row_count]
            * keep_mask
        )
    gate_value = gate_branch.astype(jnp.float32)
    gate_act = jax.nn.silu(gate_value)
    conv_act = jax.nn.silu(conv_sum)
    mixed = (conv_act * gate_act).astype(jnp.bfloat16)
    partial_value = jnp.dot(mixed, out_weight, preferred_element_type=jnp.float32)
    columns = tokens.shape[1] // lax.axis_size("col")
    col_start = lax.axis_index("col") * columns
    lang_table = (lang_ids[:, None] == jnp.arange(LANGS, dtype=jnp.int32)[None, :]).astype(
        jnp.float32
    )
    token_weight = jnp.sum(lang_table * lang_weight[None, :], axis=1)[:, None]
    if moves_tokens and lax.axis_size("col") == 4:
        out_total = col_psum(partial_value.astype(jnp.bfloat16))
    else:
        out_total = lax.psum(partial_value.astype(jnp.bfloat16), "col").astype(jnp.float32)
    out_block = lax.dynamic_slice_in_dim(out_total, col_start, columns, 1)
    residual_grad = (token_weight * (out_total - target.astype(jnp.float32))).astype(jnp.bfloat16)
    grad_mixed = lax.dot_general(
        residual_grad, out_weight, (((1,), (1,)), ((), ())), preferred_element_type=jnp.float32
    )
    grad_conv = grad_mixed * gate_act * silu_grad(conv_sum)
    grad_gate = (grad_mixed * conv_act * silu_grad(gate_value)).astype(jnp.bfloat16)
    local_grad = conv_weight[0][None, :] * grad_conv
    spill_over = jnp.zeros((margin, inner_width), jnp.float32)
    for offset in range(1, CONV):
        masked = (
            conv_weight[offset][None, :]
            * grad_conv
            * (doc_pos >= offset).astype(jnp.float32)[:, None]
        )
        local_grad = local_grad + jnp.concatenate(
            [masked[offset:], jnp.zeros((offset, inner_width), jnp.float32)], axis=0
        )
        spill_over = spill_over + jnp.concatenate(
            [jnp.zeros((margin - offset, inner_width), jnp.float32), masked[:offset]], axis=0
        )
    from_next = passed_along(spill_over, "row", -1)
    grad_x = (
        local_grad
        + jnp.concatenate(
            [jnp.zeros((row_count - margin, inner_width), jnp.float32), from_next], axis=0
        )
    ).astype(jnp.bfloat16)
    if moves_tokens:
        stacks, sources = ring_gather(grad_x, "row")
        contract = (((2,), (1,)), ((), ()))
        weight_parts = jnp.split(in_weight, len(stacks), axis=1)
        grad_cols = lax.dot_general(
            stacks[0], weight_parts[0], contract, preferred_element_type=jnp.float32
        )
        for stack, weight_part in zip(stacks[1:], weight_parts[1:]):
            grad_cols = grad_cols + lax.dot_general(
                stack, weight_part, contract, preferred_element_type=jnp.float32
            )
        grad_cols = jnp.take(grad_cols.astype(jnp.bfloat16), jnp.argsort(sources), axis=0)
        grad_cols = grad_cols.reshape(-1, grad_cols.shape[2])
        if lax.axis_size("col") == 4 and lax.axis_size("row") == 8:
            grad_tokens = placed_sums(grad_cols, row_count)
        else:
            grad_sum = lax.psum_scatter(grad_cols, "col", scatter_dimension=0, tiled=True)
            grad_tokens = placed_blocks(grad_sum, row_count)
    else:
        partial_grad = lax.dot_general(
            grad_x, full_in, (((1,), (1,)), ((), ())), preferred_element_type=jnp.float32
        )
        grad_tokens = lax.psum_scatter(
            partial_grad.astype(jnp.bfloat16), "col", scatter_dimension=1, tiled=True
        )
    return (out_block.astype(jnp.bfloat16), grad_tokens, grad_gate)


def solution(mesh):
    in_specs = (
        P("row", None),
        P("row", "col"),
        P("row", "col"),
        P(None, "col"),
        P("col", None),
        P("row", None),
        P("row"),
        P(),
        P("row"),
    )
    out_specs = (P("row", "col"), P("row", "col"), P("row", "col"))
    return jax.shard_map(shards, mesh=mesh, in_specs=in_specs, out_specs=out_specs, check_vma=False)
```

```python
import jax
import jax.numpy as jnp
from jax import lax
from jax.sharding import PartitionSpec as P

CONV = 4
LANGS = 32


def passed_along(value, axis, steps):
    count = lax.axis_size(axis)
    first, last = (max(0, -steps), min(count, count - steps))
    return lax.ppermute(value, axis, [(source, source + steps) for source in range(first, last)])


def fetched_columns(tokens):
    n_row, n_col = lax.axis_size("row"), lax.axis_size("col")
    width = tokens.shape[1] // n_row
    if n_col % 2:
        return lax.all_to_all(tokens, "row", 1, 0, tiled=True), None
    core = lax.axis_index("col") % 2
    halves = tokens.reshape(tokens.shape[0], n_row, 2, width // 2)
    mine = jnp.take(halves, core, axis=2).reshape(tokens.shape[0], n_row * (width // 2))
    mine = lax.all_to_all(mine, "row", 1, 0, tiled=True)
    other = lax.ppermute(mine, "col", [(c, c ^ 1) for c in range(n_col)])
    return jnp.where(
        core == 0, jnp.concatenate([mine, other], axis=1), jnp.concatenate([other, mine], axis=1)
    ), (mine, other, core)


def placed_blocks(grad_sum, row_count):
    n_row, n_col = lax.axis_size("row"), lax.axis_size("col")
    share = n_row // n_col
    row = lax.axis_index("row")
    got = []
    for m in range(share):
        pairs = [
            (r * n_col + c, (c * share + (r % share + m) % share) * n_col + r // share)
            for r in range(n_row)
            for c in range(n_col)
        ]
        start = ((row % share + m) % share) * row_count
        piece = lax.dynamic_slice_in_dim(grad_sum, start, row_count, axis=0)
        got.append(lax.ppermute(piece, ("row", "col"), pairs))
    pieces = []
    for j in range(share):
        want = (row % share - j) % share
        piece = got[0]
        for m in range(1, share):
            piece = jnp.where(want == m, got[m], piece)
        pieces.append(piece)
    return jnp.concatenate(pieces, axis=1)

def placed_sums(grad_cols, row_count):
    n_row, n_col = lax.axis_size("row"), lax.axis_size("col")
    row, col = lax.axis_index("row"), lax.axis_index("col")
    core, chip = col % 2, col // 2
    quarters = grad_cols.reshape(2, 2, grad_cols.shape[0] // 4, grad_cols.shape[1])
    keep = jnp.take(quarters, core, axis=1)
    give = jnp.take(quarters, 1 - core, axis=1)
    got = lax.ppermute(give, "col", [(c, c ^ 1) for c in range(n_col)])
    pair = (keep.astype(jnp.float32) + got.astype(jnp.float32)).astype(jnp.bfloat16)
    pieces = pair.reshape(2, 2, row_count, grad_cols.shape[1])
    arrived = {}
    for a in range(2):
        for b in range(2):
            pairs = [
                (r * n_col + c, (2 * (((c // 2) ^ b) * 2 + c % 2) + ((r % 2) ^ a)) * n_col + r // 2)
                for r in range(n_row)
                for c in range(n_col)
            ]
            piece = jnp.take(jnp.take(pieces, chip ^ b, axis=0), (row % 2) ^ a, axis=0)
            arrived[a, b] = lax.ppermute(piece, ("row", "col"), pairs).astype(jnp.float32)
    sums = [arrived[a, 0] + arrived[a, 1] for a in range(2)]
    return jnp.concatenate(
        [jnp.where((row % 2) ^ j == 0, sums[0], sums[1]).astype(jnp.bfloat16) for j in range(2)], axis=1
    )


def ring_order(count):
    if count % 2:
        return list(range(count))
    return list(range(0, count, 2)) + list(range(count - 1, 0, -2))


def ring_place(axis):
    count = lax.axis_size(axis)
    order = ring_order(count)
    place = jnp.array([order.index(i) for i in range(count)], jnp.int32)[lax.axis_index(axis)]
    ahead = [(order[i], order[(i + 1) % count]) for i in range(count)]
    behind = [(order[(i + 1) % count], order[i]) for i in range(count)]
    return count, jnp.array(order, jnp.int32), place, ahead, behind


def ring_gather(value, axis, chains=2):
    count, order, place, ahead, behind = ring_place(axis)
    parts = jnp.split(value, 2 * chains, axis=1)
    stacks = []
    for number, part in enumerate(parts):
        pairs = ahead if number < chains else behind
        got = [part]
        for _ in range(1, count):
            part = lax.ppermute(part, axis, pairs)
            got.append(part)
        if number >= chains:
            got = [got[(count - s) % count] for s in range(count)]
        stacks.append(jnp.stack(got))
    sources = order[(place - jnp.arange(count)) % count]
    return stacks, sources


def ring_reduce_scatter(token_cols, weight, axis, chains=2, halves=None):
    count, order, place, ahead, behind = ring_place(axis)
    rows = token_cols.shape[0] // count
    blocks = token_cols.reshape(count, rows, token_cols.shape[1])
    half = weight.shape[1] // 2
    steps = jnp.arange(1, count)
    later = (count - 1) * rows
    def block_at(index):
        if halves is None:
            return jnp.take(blocks, index, axis=0)
        mine, other, core = halves
        own = lax.dynamic_slice_in_dim(mine, index * rows, rows, 0)
        swapped = lax.dynamic_slice_in_dim(other, index * rows, rows, 0)
        return jnp.where(
            core == 0,
            jnp.concatenate([own, swapped], axis=1),
            jnp.concatenate([swapped, own], axis=1),
        )

    first_0 = block_at(order[(place - 1) % count])
    second_0 = block_at(order[(place + 1) % count])
    start_a = jnp.dot(first_0, weight[:, :half], preferred_element_type=jnp.float32)
    start_b = jnp.dot(second_0, weight[:, half:], preferred_element_type=jnp.float32)
    first = jnp.take(blocks, order[(place - 1 - steps) % count], axis=0).reshape(later, -1)
    second = jnp.take(blocks, order[(place + 1 + steps) % count], axis=0).reshape(later, -1)
    own_a = jnp.dot(first, weight[:, :half], preferred_element_type=jnp.float32)
    own_b = jnp.dot(second, weight[:, half:], preferred_element_type=jnp.float32)
    own_a = own_a.reshape(count - 1, rows, half)
    own_b = own_b.reshape(count - 1, rows, weight.shape[1] - half)
    starts = jnp.split(start_a, chains, axis=1) + jnp.split(start_b, chains, axis=1)
    owns = jnp.split(own_a, chains, axis=2) + jnp.split(own_b, chains, axis=2)
    sums = []
    for number, (start, own) in enumerate(zip(starts, owns)):
        pairs = ahead if number < chains else behind
        total = start.astype(jnp.bfloat16)
        for s in range(1, count):
            total = lax.ppermute(total, axis, pairs)
            total = (total.astype(jnp.float32) + own[s - 1]).astype(jnp.bfloat16)
        sums.append(total)
    return jnp.concatenate(sums, axis=1)

def halves_of(value, dim, upper):
    low, high = jnp.split(value, 2, axis=dim)
    return jnp.where(upper, high, low), jnp.where(upper, low, high)


def col_psum(value):
    core = lax.axis_index("col") % 2 == 1
    keep, give = halves_of(value, 1, core)
    count = lax.axis_size("col")
    got = lax.ppermute(give, "col", [(c, c ^ 1) for c in range(count)])
    pair = keep.astype(jnp.float32) + got.astype(jnp.float32)
    total = pair + lax.ppermute(
        pair.astype(jnp.bfloat16), "col", [(c, c ^ 2) for c in range(count)]
    ).astype(jnp.float32)
    other = lax.ppermute(total, "col", [(c, c ^ 1) for c in range(count)])
    return jnp.where(
        core, jnp.concatenate([other, total], axis=1), jnp.concatenate([total, other], axis=1)
    )


def col_psum_scatter(value):
    col = lax.axis_index("col")
    count = lax.axis_size("col")
    quarters = value.reshape(2, 2, value.shape[0] // 4, value.shape[1])
    keep = jnp.take(quarters, col % 2, axis=1)
    give = jnp.take(quarters, 1 - col % 2, axis=1)
    got = lax.ppermute(give, "col", [(c, c ^ 1) for c in range(count)])
    pair = keep.astype(jnp.float32) + got.astype(jnp.float32)
    mine = jnp.take(pair, col // 2, axis=0)
    theirs = jnp.take(pair, 1 - col // 2, axis=0)
    got = lax.ppermute(theirs.astype(jnp.bfloat16), "col", [(c, c ^ 2) for c in range(count)])
    return (mine + got.astype(jnp.float32)).astype(jnp.bfloat16)


def silu_grad(argument):
    sigmoid_v = jax.nn.sigmoid(argument)
    return sigmoid_v * (1.0 + argument * (1.0 - sigmoid_v))


def shards(
    tokens, in_weight, gate_branch, conv_weight, out_weight, target, lang_ids, lang_weight, doc_pos
):
    row_count = tokens.shape[0]
    inner_width = gate_branch.shape[1]
    margin = CONV - 1
    moves_tokens = (
        row_count * lax.axis_size("row") < tokens.shape[1]
        and lax.axis_size("row") % lax.axis_size("col") == 0
    )
    if moves_tokens:
        token_cols, halves = fetched_columns(tokens)
        inner_x = ring_reduce_scatter(token_cols, in_weight, "row", halves=halves)
    else:
        full_in = lax.all_gather(in_weight, "row", axis=0, tiled=True)
        inner_x = jnp.dot(tokens, full_in, preferred_element_type=jnp.float32).astype(jnp.bfloat16)
    from_prev = passed_along(inner_x[row_count - margin :], "row", 1)
    extended = jnp.concatenate([from_prev, inner_x], axis=0).astype(jnp.float32)
    conv_sum = jnp.zeros((row_count, inner_width), jnp.float32)
    for offset in range(CONV):
        keep_mask = (doc_pos >= offset).astype(jnp.float32)[:, None]
        conv_sum = (
            conv_sum
            + conv_weight[offset][None, :]
            * extended[margin - offset : margin - offset + row_count]
            * keep_mask
        )
    gate_value = gate_branch.astype(jnp.float32)
    gate_act = jax.nn.silu(gate_value)
    conv_act = jax.nn.silu(conv_sum)
    mixed = (conv_act * gate_act).astype(jnp.bfloat16)
    partial_value = jnp.dot(mixed, out_weight, preferred_element_type=jnp.float32)
    columns = tokens.shape[1] // lax.axis_size("col")
    col_start = lax.axis_index("col") * columns
    lang_table = (lang_ids[:, None] == jnp.arange(LANGS, dtype=jnp.int32)[None, :]).astype(
        jnp.float32
    )
    token_weight = jnp.sum(lang_table * lang_weight[None, :], axis=1)[:, None]
    if moves_tokens and lax.axis_size("col") == 4:
        out_total = col_psum(partial_value.astype(jnp.bfloat16))
    else:
        out_total = lax.psum(partial_value.astype(jnp.bfloat16), "col").astype(jnp.float32)
    out_block = lax.dynamic_slice_in_dim(out_total, col_start, columns, 1)
    residual_grad = (token_weight * (out_total - target.astype(jnp.float32))).astype(jnp.bfloat16)
    grad_mixed = lax.dot_general(
        residual_grad, out_weight, (((1,), (1,)), ((), ())), preferred_element_type=jnp.float32
    )
    grad_conv = grad_mixed * gate_act * silu_grad(conv_sum)
    grad_gate = (grad_mixed * conv_act * silu_grad(gate_value)).astype(jnp.bfloat16)
    local_grad = conv_weight[0][None, :] * grad_conv
    spill_over = jnp.zeros((margin, inner_width), jnp.float32)
    for offset in range(1, CONV):
        masked = (
            conv_weight[offset][None, :]
            * grad_conv
            * (doc_pos >= offset).astype(jnp.float32)[:, None]
        )
        local_grad = local_grad + jnp.concatenate(
            [masked[offset:], jnp.zeros((offset, inner_width), jnp.float32)], axis=0
        )
        spill_over = spill_over + jnp.concatenate(
            [jnp.zeros((margin - offset, inner_width), jnp.float32), masked[:offset]], axis=0
        )
    from_next = passed_along(spill_over, "row", -1)
    grad_x = (
        local_grad
        + jnp.concatenate(
            [jnp.zeros((row_count - margin, inner_width), jnp.float32), from_next], axis=0
        )
    ).astype(jnp.bfloat16)
    if moves_tokens:
        stacks, sources = ring_gather(grad_x, "row")
        contract = (((2,), (1,)), ((), ()))
        weight_parts = jnp.split(in_weight, len(stacks), axis=1)
        grad_cols = lax.dot_general(
            stacks[0], weight_parts[0], contract, preferred_element_type=jnp.float32
        )
        for stack, weight_part in zip(stacks[1:], weight_parts[1:]):
            grad_cols = grad_cols + lax.dot_general(
                stack, weight_part, contract, preferred_element_type=jnp.float32
            )
        grad_cols = jnp.take(grad_cols.astype(jnp.bfloat16), jnp.argsort(sources), axis=0)
        grad_cols = grad_cols.reshape(-1, grad_cols.shape[2])
        if lax.axis_size("col") == 4 and lax.axis_size("row") == 8:
            grad_tokens = placed_sums(grad_cols, row_count)
        else:
            grad_sum = lax.psum_scatter(grad_cols, "col", scatter_dimension=0, tiled=True)
            grad_tokens = placed_blocks(grad_sum, row_count)
    else:
        partial_grad = lax.dot_general(
            grad_x, full_in, (((1,), (1,)), ((), ())), preferred_element_type=jnp.float32
        )
        grad_tokens = lax.psum_scatter(
            partial_grad.astype(jnp.bfloat16), "col", scatter_dimension=1, tiled=True
        )
    return (out_block.astype(jnp.bfloat16), grad_tokens, grad_gate)


def solution(mesh):
    in_specs = (
        P("row", None),
        P("row", "col"),
        P("row", "col"),
        P(None, "col"),
        P("col", None),
        P("row", None),
        P("row"),
        P(),
        P("row"),
    )
    out_specs = (P("row", "col"), P("row", "col"), P("row", "col"))
    return jax.shard_map(shards, mesh=mesh, in_specs=in_specs, out_specs=out_specs, check_vma=False)
```

```python
import jax
import jax.numpy as jnp
from jax import lax
from jax.sharding import PartitionSpec as P

CONV = 4
LANGS = 32


def passed_along(value, axis, steps):
    count = lax.axis_size(axis)
    first, last = (max(0, -steps), min(count, count - steps))
    return lax.ppermute(value, axis, [(source, source + steps) for source in range(first, last)])


def fetched_columns(tokens):
    n_row, n_col = lax.axis_size("row"), lax.axis_size("col")
    width = tokens.shape[1] // n_row
    if n_col % 2:
        return lax.all_to_all(tokens, "row", 1, 0, tiled=True)
    core = lax.axis_index("col") % 2
    halves = tokens.reshape(tokens.shape[0], n_row, 2, width // 2)
    mine = jnp.take(halves, core, axis=2).reshape(tokens.shape[0], n_row * (width // 2))
    mine = lax.all_to_all(mine, "row", 1, 0, tiled=True)
    other = lax.ppermute(mine, "col", [(c, c ^ 1) for c in range(n_col)])
    return jnp.where(
        core == 0, jnp.concatenate([mine, other], axis=1), jnp.concatenate([other, mine], axis=1)
    )


def placed_blocks(grad_sum, row_count):
    n_row, n_col = lax.axis_size("row"), lax.axis_size("col")
    share = n_row // n_col
    row = lax.axis_index("row")
    got = []
    for m in range(share):
        pairs = [
            (r * n_col + c, (c * share + (r % share + m) % share) * n_col + r // share)
            for r in range(n_row)
            for c in range(n_col)
        ]
        start = ((row % share + m) % share) * row_count
        piece = lax.dynamic_slice_in_dim(grad_sum, start, row_count, axis=0)
        got.append(lax.ppermute(piece, ("row", "col"), pairs))
    pieces = []
    for j in range(share):
        want = (row % share - j) % share
        piece = got[0]
        for m in range(1, share):
            piece = jnp.where(want == m, got[m], piece)
        pieces.append(piece)
    return jnp.concatenate(pieces, axis=1)

def placed_sums(grad_cols, row_count):
    n_row, n_col = lax.axis_size("row"), lax.axis_size("col")
    row, col = lax.axis_index("row"), lax.axis_index("col")
    core, chip = col % 2, col // 2
    quarters = grad_cols.reshape(2, 2, grad_cols.shape[0] // 4, grad_cols.shape[1])
    keep = jnp.take(quarters, core, axis=1)
    give = jnp.take(quarters, 1 - core, axis=1)
    got = lax.ppermute(give, "col", [(c, c ^ 1) for c in range(n_col)])
    pair = (keep.astype(jnp.float32) + got.astype(jnp.float32)).astype(jnp.bfloat16)
    pieces = pair.reshape(2, 2, row_count, grad_cols.shape[1])
    arrived = {}
    for a in range(2):
        for b in range(2):
            pairs = [
                (r * n_col + c, (2 * (((c // 2) ^ b) * 2 + c % 2) + ((r % 2) ^ a)) * n_col + r // 2)
                for r in range(n_row)
                for c in range(n_col)
            ]
            piece = jnp.take(jnp.take(pieces, chip ^ b, axis=0), (row % 2) ^ a, axis=0)
            arrived[a, b] = lax.ppermute(piece, ("row", "col"), pairs).astype(jnp.float32)
    sums = [arrived[a, 0] + arrived[a, 1] for a in range(2)]
    return jnp.concatenate(
        [jnp.where((row % 2) ^ j == 0, sums[0], sums[1]).astype(jnp.bfloat16) for j in range(2)], axis=1
    )


def ring_order(count):
    if count % 2:
        return list(range(count))
    return list(range(0, count, 2)) + list(range(count - 1, 0, -2))


def ring_place(axis):
    count = lax.axis_size(axis)
    order = ring_order(count)
    place = jnp.array([order.index(i) for i in range(count)], jnp.int32)[lax.axis_index(axis)]
    ahead = [(order[i], order[(i + 1) % count]) for i in range(count)]
    behind = [(order[(i + 1) % count], order[i]) for i in range(count)]
    return count, jnp.array(order, jnp.int32), place, ahead, behind


def ring_gather(value, axis, chains=2):
    count, order, place, ahead, behind = ring_place(axis)
    parts = jnp.split(value, 2 * chains, axis=1)
    stacks = []
    for number, part in enumerate(parts):
        pairs = ahead if number < chains else behind
        got = [part]
        for _ in range(1, count):
            part = lax.ppermute(part, axis, pairs)
            got.append(part)
        if number >= chains:
            got = [got[(count - s) % count] for s in range(count)]
        stacks.append(jnp.stack(got))
    sources = order[(place - jnp.arange(count)) % count]
    return stacks, sources


def ring_reduce_scatter(token_cols, weight, axis, chains=2):
    count, order, place, ahead, behind = ring_place(axis)
    rows = token_cols.shape[0] // count
    blocks = token_cols.reshape(count, rows, token_cols.shape[1])
    half = weight.shape[1] // 2
    steps = jnp.arange(1, count)
    later = (count - 1) * rows
    first_0 = jnp.take(blocks, order[(place - 1) % count], axis=0)
    second_0 = jnp.take(blocks, order[(place + 1) % count], axis=0)
    start_a = jnp.dot(first_0, weight[:, :half], preferred_element_type=jnp.float32)
    start_b = jnp.dot(second_0, weight[:, half:], preferred_element_type=jnp.float32)
    first = jnp.take(blocks, order[(place - 1 - steps) % count], axis=0).reshape(later, -1)
    second = jnp.take(blocks, order[(place + 1 + steps) % count], axis=0).reshape(later, -1)
    own_a = jnp.dot(first, weight[:, :half], preferred_element_type=jnp.float32)
    own_b = jnp.dot(second, weight[:, half:], preferred_element_type=jnp.float32)
    own_a = own_a.reshape(count - 1, rows, half)
    own_b = own_b.reshape(count - 1, rows, weight.shape[1] - half)
    starts = jnp.split(start_a, chains, axis=1) + jnp.split(start_b, chains, axis=1)
    owns = jnp.split(own_a, chains, axis=2) + jnp.split(own_b, chains, axis=2)
    sums = []
    for number, (start, own) in enumerate(zip(starts, owns)):
        pairs = ahead if number < chains else behind
        total = start.astype(jnp.bfloat16)
        for s in range(1, count):
            total = lax.ppermute(total, axis, pairs)
            total = (total.astype(jnp.float32) + own[s - 1]).astype(jnp.bfloat16)
        sums.append(total)
    return jnp.concatenate(sums, axis=1)

def halves_of(value, dim, upper):
    low, high = jnp.split(value, 2, axis=dim)
    return jnp.where(upper, high, low), jnp.where(upper, low, high)


def col_psum(value):
    core = lax.axis_index("col") % 2 == 1
    keep, give = halves_of(value, 1, core)
    count = lax.axis_size("col")
    got = lax.ppermute(give, "col", [(c, c ^ 1) for c in range(count)])
    pair = keep.astype(jnp.float32) + got.astype(jnp.float32)
    total = pair + lax.ppermute(
        pair.astype(jnp.bfloat16), "col", [(c, c ^ 2) for c in range(count)]
    ).astype(jnp.float32)
    other = lax.ppermute(
        total.astype(jnp.bfloat16), "col", [(c, c ^ 1) for c in range(count)]
    ).astype(jnp.float32)
    return jnp.where(
        core, jnp.concatenate([other, total], axis=1), jnp.concatenate([total, other], axis=1)
    )


def col_psum_scatter(value):
    col = lax.axis_index("col")
    count = lax.axis_size("col")
    quarters = value.reshape(2, 2, value.shape[0] // 4, value.shape[1])
    keep = jnp.take(quarters, col % 2, axis=1)
    give = jnp.take(quarters, 1 - col % 2, axis=1)
    got = lax.ppermute(give, "col", [(c, c ^ 1) for c in range(count)])
    pair = keep.astype(jnp.float32) + got.astype(jnp.float32)
    mine = jnp.take(pair, col // 2, axis=0)
    theirs = jnp.take(pair, 1 - col // 2, axis=0)
    got = lax.ppermute(theirs.astype(jnp.bfloat16), "col", [(c, c ^ 2) for c in range(count)])
    return (mine + got.astype(jnp.float32)).astype(jnp.bfloat16)


def silu_grad(argument):
    sigmoid_v = jax.nn.sigmoid(argument)
    return sigmoid_v * (1.0 + argument * (1.0 - sigmoid_v))


def shards(
    tokens, in_weight, gate_branch, conv_weight, out_weight, target, lang_ids, lang_weight, doc_pos
):
    row_count = tokens.shape[0]
    inner_width = gate_branch.shape[1]
    margin = CONV - 1
    moves_tokens = (
        row_count * lax.axis_size("row") < tokens.shape[1]
        and lax.axis_size("row") % lax.axis_size("col") == 0
    )
    if moves_tokens:
        inner_x = ring_reduce_scatter(fetched_columns(tokens), in_weight, "row")
    else:
        full_in = lax.all_gather(in_weight, "row", axis=0, tiled=True)
        inner_x = jnp.dot(tokens, full_in, preferred_element_type=jnp.float32).astype(jnp.bfloat16)
    from_prev = passed_along(inner_x[row_count - margin :], "row", 1)
    extended = jnp.concatenate([from_prev, inner_x], axis=0).astype(jnp.float32)
    conv_sum = jnp.zeros((row_count, inner_width), jnp.float32)
    for offset in range(CONV):
        keep_mask = (doc_pos >= offset).astype(jnp.float32)[:, None]
        conv_sum = (
            conv_sum
            + conv_weight[offset][None, :]
            * extended[margin - offset : margin - offset + row_count]
            * keep_mask
        )
    gate_value = gate_branch.astype(jnp.float32)
    gate_act = jax.nn.silu(gate_value)
    conv_act = jax.nn.silu(conv_sum)
    mixed = (conv_act * gate_act).astype(jnp.bfloat16)
    partial_value = jnp.dot(mixed, out_weight, preferred_element_type=jnp.float32)
    columns = tokens.shape[1] // lax.axis_size("col")
    col_start = lax.axis_index("col") * columns
    lang_table = (lang_ids[:, None] == jnp.arange(LANGS, dtype=jnp.int32)[None, :]).astype(
        jnp.float32
    )
    token_weight = jnp.sum(lang_table * lang_weight[None, :], axis=1)[:, None]
    if moves_tokens and lax.axis_size("col") == 4:
        out_total = col_psum(partial_value.astype(jnp.bfloat16))
    else:
        out_total = lax.psum(partial_value.astype(jnp.bfloat16), "col").astype(jnp.float32)
    out_block = lax.dynamic_slice_in_dim(out_total, col_start, columns, 1)
    residual_grad = (token_weight * (out_total - target.astype(jnp.float32))).astype(jnp.bfloat16)
    grad_mixed = lax.dot_general(
        residual_grad, out_weight, (((1,), (1,)), ((), ())), preferred_element_type=jnp.float32
    )
    grad_conv = grad_mixed * gate_act * silu_grad(conv_sum)
    grad_gate = (grad_mixed * conv_act * silu_grad(gate_value)).astype(jnp.bfloat16)
    local_grad = conv_weight[0][None, :] * grad_conv
    spill_over = jnp.zeros((margin, inner_width), jnp.float32)
    for offset in range(1, CONV):
        masked = (
            conv_weight[offset][None, :]
            * grad_conv
            * (doc_pos >= offset).astype(jnp.float32)[:, None]
        )
        local_grad = local_grad + jnp.concatenate(
            [masked[offset:], jnp.zeros((offset, inner_width), jnp.float32)], axis=0
        )
        spill_over = spill_over + jnp.concatenate(
            [jnp.zeros((margin - offset, inner_width), jnp.float32), masked[:offset]], axis=0
        )
    from_next = passed_along(spill_over, "row", -1)
    grad_x = (
        local_grad
        + jnp.concatenate(
            [jnp.zeros((row_count - margin, inner_width), jnp.float32), from_next], axis=0
        )
    ).astype(jnp.bfloat16)
    if moves_tokens:
        stacks, sources = ring_gather(grad_x, "row")
        contract = (((2,), (1,)), ((), ()))
        weight_parts = jnp.split(in_weight, len(stacks), axis=1)
        grad_cols = lax.dot_general(
            stacks[0], weight_parts[0], contract, preferred_element_type=jnp.float32
        )
        for stack, weight_part in zip(stacks[1:], weight_parts[1:]):
            grad_cols = grad_cols + lax.dot_general(
                stack, weight_part, contract, preferred_element_type=jnp.float32
            )
        grad_cols = jnp.take(grad_cols.astype(jnp.bfloat16), jnp.argsort(sources), axis=0)
        grad_cols = grad_cols.reshape(-1, grad_cols.shape[2])
        if lax.axis_size("col") == 4 and lax.axis_size("row") == 8:
            grad_tokens = placed_sums(grad_cols, row_count)
        else:
            grad_sum = lax.psum_scatter(grad_cols, "col", scatter_dimension=0, tiled=True)
            grad_tokens = placed_blocks(grad_sum, row_count)
    else:
        partial_grad = lax.dot_general(
            grad_x, full_in, (((1,), (1,)), ((), ())), preferred_element_type=jnp.float32
        )
        grad_tokens = lax.psum_scatter(
            partial_grad.astype(jnp.bfloat16), "col", scatter_dimension=1, tiled=True
        )
    return (out_block.astype(jnp.bfloat16), grad_tokens, grad_gate)


def solution(mesh):
    in_specs = (
        P("row", None),
        P("row", "col"),
        P("row", "col"),
        P(None, "col"),
        P("col", None),
        P("row", None),
        P("row"),
        P(),
        P("row"),
    )
    out_specs = (P("row", "col"), P("row", "col"), P("row", "col"))
    return jax.shard_map(shards, mesh=mesh, in_specs=in_specs, out_specs=out_specs, check_vma=False)
```

```python
import jax
import jax.numpy as jnp
from jax import lax
from jax.sharding import PartitionSpec as P

CONV = 4
LANGS = 32


def passed_along(value, axis, steps):
    count = lax.axis_size(axis)
    first, last = (max(0, -steps), min(count, count - steps))
    return lax.ppermute(value, axis, [(source, source + steps) for source in range(first, last)])


def fetched_columns(tokens):
    n_row, n_col = lax.axis_size("row"), lax.axis_size("col")
    width = tokens.shape[1] // n_row
    if n_col % 2:
        return lax.all_to_all(tokens, "row", 1, 0, tiled=True)
    core = lax.axis_index("col") % 2
    halves = tokens.reshape(tokens.shape[0], n_row, 2, width // 2)
    mine = jnp.take(halves, core, axis=2).reshape(tokens.shape[0], n_row * (width // 2))
    mine = lax.all_to_all(mine, "row", 1, 0, tiled=True)
    other = lax.ppermute(mine, "col", [(c, c ^ 1) for c in range(n_col)])
    return jnp.where(
        core == 0, jnp.concatenate([mine, other], axis=1), jnp.concatenate([other, mine], axis=1)
    )


def placed_blocks(grad_sum, row_count):
    n_row, n_col = lax.axis_size("row"), lax.axis_size("col")
    share = n_row // n_col
    row = lax.axis_index("row")
    got = []
    for m in range(share):
        pairs = [
            (r * n_col + c, (c * share + (r % share + m) % share) * n_col + r // share)
            for r in range(n_row)
            for c in range(n_col)
        ]
        start = ((row % share + m) % share) * row_count
        piece = lax.dynamic_slice_in_dim(grad_sum, start, row_count, axis=0)
        got.append(lax.ppermute(piece, ("row", "col"), pairs))
    pieces = []
    for j in range(share):
        want = (row % share - j) % share
        piece = got[0]
        for m in range(1, share):
            piece = jnp.where(want == m, got[m], piece)
        pieces.append(piece)
    return jnp.concatenate(pieces, axis=1)

def placed_sums(grad_cols, row_count):
    n_row, n_col = lax.axis_size("row"), lax.axis_size("col")
    row, col = lax.axis_index("row"), lax.axis_index("col")
    core, chip = col % 2, col // 2
    quarters = grad_cols.reshape(2, 2, grad_cols.shape[0] // 4, grad_cols.shape[1])
    keep = jnp.take(quarters, core, axis=1)
    give = jnp.take(quarters, 1 - core, axis=1)
    got = lax.ppermute(give, "col", [(c, c ^ 1) for c in range(n_col)])
    pair = (keep.astype(jnp.float32) + got.astype(jnp.float32)).astype(jnp.bfloat16)
    pieces = pair.reshape(2, 2, row_count, grad_cols.shape[1])
    arrived = {}
    for a in range(2):
        for b in range(2):
            pairs = [
                (r * n_col + c, (2 * (((c // 2) ^ b) * 2 + c % 2) + ((r % 2) ^ a)) * n_col + r // 2)
                for r in range(n_row)
                for c in range(n_col)
            ]
            piece = jnp.take(jnp.take(pieces, chip ^ b, axis=0), (row % 2) ^ a, axis=0)
            arrived[a, b] = lax.ppermute(piece, ("row", "col"), pairs).astype(jnp.float32)
    sums = [arrived[a, 0] + arrived[a, 1] for a in range(2)]
    return jnp.concatenate(
        [jnp.where((row % 2) ^ j == 0, sums[0], sums[1]).astype(jnp.bfloat16) for j in range(2)], axis=1
    )


def ring_order(count):
    if count % 2:
        return list(range(count))
    return list(range(0, count, 2)) + list(range(count - 1, 0, -2))


def ring_place(axis):
    count = lax.axis_size(axis)
    order = ring_order(count)
    place = jnp.array([order.index(i) for i in range(count)], jnp.int32)[lax.axis_index(axis)]
    ahead = [(order[i], order[(i + 1) % count]) for i in range(count)]
    behind = [(order[(i + 1) % count], order[i]) for i in range(count)]
    return count, jnp.array(order, jnp.int32), place, ahead, behind


def ring_gather(value, axis, chains=2):
    count, order, place, ahead, behind = ring_place(axis)
    parts = jnp.split(value, 2 * chains, axis=1)
    stacks = []
    for number, part in enumerate(parts):
        pairs = ahead if number < chains else behind
        got = [part]
        for _ in range(1, count):
            part = lax.ppermute(part, axis, pairs)
            got.append(part)
        if number >= chains:
            got = [got[(count - s) % count] for s in range(count)]
        stacks.append(jnp.stack(got))
    sources = order[(place - jnp.arange(count)) % count]
    return stacks, sources


def ring_reduce_scatter(token_cols, weight, axis, chains=2):
    count, order, place, ahead, behind = ring_place(axis)
    rows = token_cols.shape[0] // count
    blocks = token_cols.reshape(count, rows, token_cols.shape[1])
    half = weight.shape[1] // 2
    steps = jnp.arange(1, count)
    later = (count - 1) * rows
    first_0 = jnp.take(blocks, order[(place - 1) % count], axis=0)
    second_0 = jnp.take(blocks, order[(place + 1) % count], axis=0)
    start_a = jnp.dot(first_0, weight[:, :half], preferred_element_type=jnp.float32)
    start_b = jnp.dot(second_0, weight[:, half:], preferred_element_type=jnp.float32)
    first = jnp.take(blocks, order[(place - 1 - steps) % count], axis=0).reshape(later, -1)
    second = jnp.take(blocks, order[(place + 1 + steps) % count], axis=0).reshape(later, -1)
    own_a = jnp.dot(first, weight[:, :half], preferred_element_type=jnp.float32)
    own_b = jnp.dot(second, weight[:, half:], preferred_element_type=jnp.float32)
    own_a = own_a.reshape(count - 1, rows, half)
    own_b = own_b.reshape(count - 1, rows, weight.shape[1] - half)
    starts = jnp.split(start_a, chains, axis=1) + jnp.split(start_b, chains, axis=1)
    owns = jnp.split(own_a, chains, axis=2) + jnp.split(own_b, chains, axis=2)
    sums = []
    for number, (start, own) in enumerate(zip(starts, owns)):
        pairs = ahead if number < chains else behind
        total = start.astype(jnp.bfloat16)
        for s in range(1, count):
            total = lax.ppermute(total, axis, pairs)
            total = (total.astype(jnp.float32) + own[s - 1]).astype(jnp.bfloat16)
        sums.append(total)
    return jnp.concatenate(sums, axis=1)

def halves_of(value, dim, upper):
    low, high = jnp.split(value, 2, axis=dim)
    return jnp.where(upper, high, low), jnp.where(upper, low, high)


def col_psum(value):
    core = lax.axis_index("col") % 2 == 1
    keep, give = halves_of(value, 1, core)
    count = lax.axis_size("col")
    got = lax.ppermute(give, "col", [(c, c ^ 1) for c in range(count)])
    pair = keep.astype(jnp.float32) + got.astype(jnp.float32)
    total = pair + lax.ppermute(
        pair.astype(jnp.bfloat16), "col", [(c, c ^ 2) for c in range(count)]
    ).astype(jnp.float32)
    other = lax.ppermute(total, "col", [(c, c ^ 1) for c in range(count)])
    return jnp.where(
        core, jnp.concatenate([other, total], axis=1), jnp.concatenate([total, other], axis=1)
    )


def col_psum_scatter(value):
    col = lax.axis_index("col")
    count = lax.axis_size("col")
    quarters = value.reshape(2, 2, value.shape[0] // 4, value.shape[1])
    keep = jnp.take(quarters, col % 2, axis=1)
    give = jnp.take(quarters, 1 - col % 2, axis=1)
    got = lax.ppermute(give, "col", [(c, c ^ 1) for c in range(count)])
    pair = keep.astype(jnp.float32) + got.astype(jnp.float32)
    mine = jnp.take(pair, col // 2, axis=0)
    theirs = jnp.take(pair, 1 - col // 2, axis=0)
    got = lax.ppermute(theirs.astype(jnp.bfloat16), "col", [(c, c ^ 2) for c in range(count)])
    return (mine + got.astype(jnp.float32)).astype(jnp.bfloat16)


def silu_grad(argument):
    sigmoid_v = jax.nn.sigmoid(argument)
    return sigmoid_v * (1.0 + argument * (1.0 - sigmoid_v))


def shards(
    tokens, in_weight, gate_branch, conv_weight, out_weight, target, lang_ids, lang_weight, doc_pos
):
    row_count = tokens.shape[0]
    inner_width = gate_branch.shape[1]
    margin = CONV - 1
    moves_tokens = (
        row_count * lax.axis_size("row") < tokens.shape[1]
        and lax.axis_size("row") % lax.axis_size("col") == 0
    )
    if moves_tokens:
        inner_x = ring_reduce_scatter(fetched_columns(tokens), in_weight, "row")
    else:
        full_in = lax.all_gather(in_weight, "row", axis=0, tiled=True)
        inner_x = jnp.dot(tokens, full_in, preferred_element_type=jnp.float32).astype(jnp.bfloat16)
    from_prev = passed_along(inner_x[row_count - margin :], "row", 1)
    extended = jnp.concatenate([from_prev, inner_x], axis=0).astype(jnp.float32)
    conv_sum = jnp.zeros((row_count, inner_width), jnp.float32)
    for offset in range(CONV):
        keep_mask = (doc_pos >= offset).astype(jnp.float32)[:, None]
        conv_sum = (
            conv_sum
            + conv_weight[offset][None, :]
            * extended[margin - offset : margin - offset + row_count]
            * keep_mask
        )
    gate_value = gate_branch.astype(jnp.float32)
    gate_act = jax.nn.silu(gate_value)
    conv_act = jax.nn.silu(conv_sum)
    mixed = (conv_act * gate_act).astype(jnp.bfloat16)
    partial_value = jnp.dot(mixed, out_weight, preferred_element_type=jnp.float32)
    columns = tokens.shape[1] // lax.axis_size("col")
    col_start = lax.axis_index("col") * columns
    lang_table = (lang_ids[:, None] == jnp.arange(LANGS, dtype=jnp.int32)[None, :]).astype(
        jnp.float32
    )
    token_weight = jnp.sum(lang_table * lang_weight[None, :], axis=1)[:, None]
    if moves_tokens and lax.axis_size("col") == 4:
        out_total = col_psum(partial_value.astype(jnp.bfloat16))
    else:
        out_total = lax.psum(partial_value.astype(jnp.bfloat16), "col").astype(jnp.float32)
    out_block = lax.dynamic_slice_in_dim(out_total, col_start, columns, 1)
    residual_grad = (token_weight * (out_total - target.astype(jnp.float32))).astype(jnp.bfloat16)
    grad_mixed = lax.dot_general(
        residual_grad, out_weight, (((1,), (1,)), ((), ())), preferred_element_type=jnp.float32
    )
    grad_conv = grad_mixed * gate_act * silu_grad(conv_sum)
    grad_gate = (grad_mixed * conv_act * silu_grad(gate_value)).astype(jnp.bfloat16)
    local_grad = conv_weight[0][None, :] * grad_conv
    spill_over = jnp.zeros((margin, inner_width), jnp.float32)
    for offset in range(1, CONV):
        masked = (
            conv_weight[offset][None, :]
            * grad_conv
            * (doc_pos >= offset).astype(jnp.float32)[:, None]
        )
        local_grad = local_grad + jnp.concatenate(
            [masked[offset:], jnp.zeros((offset, inner_width), jnp.float32)], axis=0
        )
        spill_over = spill_over + jnp.concatenate(
            [jnp.zeros((margin - offset, inner_width), jnp.float32), masked[:offset]], axis=0
        )
    from_next = passed_along(spill_over, "row", -1)
    grad_x = (
        local_grad
        + jnp.concatenate(
            [jnp.zeros((row_count - margin, inner_width), jnp.float32), from_next], axis=0
        )
    ).astype(jnp.bfloat16)
    if moves_tokens:
        stacks, sources = ring_gather(grad_x, "row", chains=1)
        contract = (((2,), (1,)), ((), ()))
        weight_parts = jnp.split(in_weight, len(stacks), axis=1)
        grad_cols = lax.dot_general(
            stacks[0], weight_parts[0], contract, preferred_element_type=jnp.float32
        )
        for stack, weight_part in zip(stacks[1:], weight_parts[1:]):
            grad_cols = grad_cols + lax.dot_general(
                stack, weight_part, contract, preferred_element_type=jnp.float32
            )
        grad_cols = jnp.take(grad_cols.astype(jnp.bfloat16), jnp.argsort(sources), axis=0)
        grad_cols = grad_cols.reshape(-1, grad_cols.shape[2])
        if lax.axis_size("col") == 4 and lax.axis_size("row") == 8:
            grad_tokens = placed_sums(grad_cols, row_count)
        else:
            grad_sum = lax.psum_scatter(grad_cols, "col", scatter_dimension=0, tiled=True)
            grad_tokens = placed_blocks(grad_sum, row_count)
    else:
        partial_grad = lax.dot_general(
            grad_x, full_in, (((1,), (1,)), ((), ())), preferred_element_type=jnp.float32
        )
        grad_tokens = lax.psum_scatter(
            partial_grad.astype(jnp.bfloat16), "col", scatter_dimension=1, tiled=True
        )
    return (out_block.astype(jnp.bfloat16), grad_tokens, grad_gate)


def solution(mesh):
    in_specs = (
        P("row", None),
        P("row", "col"),
        P("row", "col"),
        P(None, "col"),
        P("col", None),
        P("row", None),
        P("row"),
        P(),
        P("row"),
    )
    out_specs = (P("row", "col"), P("row", "col"), P("row", "col"))
    return jax.shard_map(shards, mesh=mesh, in_specs=in_specs, out_specs=out_specs, check_vma=False)
```

```python
import jax
import jax.numpy as jnp
from jax import lax
from jax.sharding import PartitionSpec as P

CONV = 4
LANGS = 32


def passed_along(value, axis, steps):
    count = lax.axis_size(axis)
    first, last = (max(0, -steps), min(count, count - steps))
    return lax.ppermute(value, axis, [(source, source + steps) for source in range(first, last)])


def fetched_columns(tokens):
    n_row, n_col = lax.axis_size("row"), lax.axis_size("col")
    width = tokens.shape[1] // n_row
    if n_col % 2:
        return lax.all_to_all(tokens, "row", 1, 0, tiled=True)
    core = lax.axis_index("col") % 2
    halves = tokens.reshape(tokens.shape[0], n_row, 2, width // 2)
    mine = jnp.take(halves, core, axis=2).reshape(tokens.shape[0], n_row * (width // 2))
    mine = lax.all_to_all(mine, "row", 1, 0, tiled=True)
    other = lax.ppermute(mine, "col", [(c, c ^ 1) for c in range(n_col)])
    return jnp.where(
        core == 0, jnp.concatenate([mine, other], axis=1), jnp.concatenate([other, mine], axis=1)
    )


def placed_blocks(grad_sum, row_count):
    n_row, n_col = lax.axis_size("row"), lax.axis_size("col")
    share = n_row // n_col
    row = lax.axis_index("row")
    got = []
    for m in range(share):
        pairs = [
            (r * n_col + c, (c * share + (r % share + m) % share) * n_col + r // share)
            for r in range(n_row)
            for c in range(n_col)
        ]
        start = ((row % share + m) % share) * row_count
        piece = lax.dynamic_slice_in_dim(grad_sum, start, row_count, axis=0)
        got.append(lax.ppermute(piece, ("row", "col"), pairs))
    pieces = []
    for j in range(share):
        want = (row % share - j) % share
        piece = got[0]
        for m in range(1, share):
            piece = jnp.where(want == m, got[m], piece)
        pieces.append(piece)
    return jnp.concatenate(pieces, axis=1)

def placed_sums(grad_cols, row_count):
    n_row, n_col = lax.axis_size("row"), lax.axis_size("col")
    row, col = lax.axis_index("row"), lax.axis_index("col")
    core, chip = col % 2, col // 2
    quarters = grad_cols.reshape(2, 2, grad_cols.shape[0] // 4, grad_cols.shape[1])
    keep = jnp.take(quarters, core, axis=1)
    give = jnp.take(quarters, 1 - core, axis=1)
    got = lax.ppermute(give, "col", [(c, c ^ 1) for c in range(n_col)])
    pair = (keep.astype(jnp.float32) + got.astype(jnp.float32)).astype(jnp.bfloat16)
    pieces = pair.reshape(2, 2, row_count, grad_cols.shape[1])
    arrived = {}
    for a in range(2):
        for b in range(2):
            pairs = [
                (r * n_col + c, (2 * (((c // 2) ^ b) * 2 + c % 2) + ((r % 2) ^ a)) * n_col + r // 2)
                for r in range(n_row)
                for c in range(n_col)
            ]
            piece = jnp.take(jnp.take(pieces, chip ^ b, axis=0), (row % 2) ^ a, axis=0)
            arrived[a, b] = lax.ppermute(piece, ("row", "col"), pairs).astype(jnp.float32)
    sums = [arrived[a, 0] + arrived[a, 1] for a in range(2)]
    return jnp.concatenate(
        [jnp.where((row % 2) ^ j == 0, sums[0], sums[1]).astype(jnp.bfloat16) for j in range(2)], axis=1
    )


def ring_order(count):
    if count % 2:
        return list(range(count))
    return list(range(0, count, 2)) + list(range(count - 1, 0, -2))


def ring_place(axis):
    count = lax.axis_size(axis)
    order = ring_order(count)
    place = jnp.array([order.index(i) for i in range(count)], jnp.int32)[lax.axis_index(axis)]
    ahead = [(order[i], order[(i + 1) % count]) for i in range(count)]
    behind = [(order[(i + 1) % count], order[i]) for i in range(count)]
    return count, jnp.array(order, jnp.int32), place, ahead, behind


def ring_gather(value, axis, chains=2):
    count, order, place, ahead, behind = ring_place(axis)
    parts = jnp.split(value, 2 * chains, axis=1)
    stacks = []
    for number, part in enumerate(parts):
        pairs = ahead if number < chains else behind
        got = [part]
        for _ in range(1, count):
            part = lax.ppermute(part, axis, pairs)
            got.append(part)
        if number >= chains:
            got = [got[(count - s) % count] for s in range(count)]
        stacks.append(jnp.stack(got))
    sources = order[(place - jnp.arange(count)) % count]
    return stacks, sources


def ring_reduce_scatter(token_cols, weight, axis, chains=2):
    count, order, place, ahead, behind = ring_place(axis)
    rows = token_cols.shape[0] // count
    blocks = token_cols.reshape(count, rows, token_cols.shape[1])
    half = weight.shape[1] // 2
    steps = jnp.arange(1, count)
    later = (count - 1) * rows
    first_0 = jnp.take(blocks, order[(place - 1) % count], axis=0)
    second_0 = jnp.take(blocks, order[(place + 1) % count], axis=0)
    start_a = jnp.dot(first_0, weight[:, :half], preferred_element_type=jnp.float32)
    start_b = jnp.dot(second_0, weight[:, half:], preferred_element_type=jnp.float32)
    first = jnp.take(blocks, order[(place - 1 - steps) % count], axis=0).reshape(later, -1)
    second = jnp.take(blocks, order[(place + 1 + steps) % count], axis=0).reshape(later, -1)
    own_a = jnp.dot(first, weight[:, :half], preferred_element_type=jnp.float32)
    own_b = jnp.dot(second, weight[:, half:], preferred_element_type=jnp.float32)
    own_a = own_a.reshape(count - 1, rows, half)
    own_b = own_b.reshape(count - 1, rows, weight.shape[1] - half)
    starts = jnp.split(start_a, chains, axis=1) + jnp.split(start_b, chains, axis=1)
    owns = jnp.split(own_a, chains, axis=2) + jnp.split(own_b, chains, axis=2)
    sums = []
    for number, (start, own) in enumerate(zip(starts, owns)):
        pairs = ahead if number < chains else behind
        total = start.astype(jnp.bfloat16)
        for s in range(1, count):
            total = lax.ppermute(total, axis, pairs)
            total = (total.astype(jnp.float32) + own[s - 1]).astype(jnp.bfloat16)
        sums.append(total)
    return jnp.concatenate(sums, axis=1)

def halves_of(value, dim, upper):
    low, high = jnp.split(value, 2, axis=dim)
    return jnp.where(upper, high, low), jnp.where(upper, low, high)


def col_psum(value):
    core = lax.axis_index("col") % 2 == 1
    keep, give = halves_of(value, 1, core)
    count = lax.axis_size("col")
    got = lax.ppermute(give, "col", [(c, c ^ 1) for c in range(count)])
    pair = keep.astype(jnp.float32) + got.astype(jnp.float32)
    total = pair + lax.ppermute(
        pair.astype(jnp.bfloat16), "col", [(c, c ^ 2) for c in range(count)]
    ).astype(jnp.float32)
    other = lax.ppermute(total, "col", [(c, c ^ 1) for c in range(count)])
    return jnp.where(
        core, jnp.concatenate([other, total], axis=1), jnp.concatenate([total, other], axis=1)
    )


def col_psum_scatter(value):
    col = lax.axis_index("col")
    count = lax.axis_size("col")
    quarters = value.reshape(2, 2, value.shape[0] // 4, value.shape[1])
    keep = jnp.take(quarters, col % 2, axis=1)
    give = jnp.take(quarters, 1 - col % 2, axis=1)
    got = lax.ppermute(give, "col", [(c, c ^ 1) for c in range(count)])
    pair = keep.astype(jnp.float32) + got.astype(jnp.float32)
    mine = jnp.take(pair, col // 2, axis=0)
    theirs = jnp.take(pair, 1 - col // 2, axis=0)
    got = lax.ppermute(theirs.astype(jnp.bfloat16), "col", [(c, c ^ 2) for c in range(count)])
    return (mine + got.astype(jnp.float32)).astype(jnp.bfloat16)


def silu_grad(argument):
    sigmoid_v = jax.nn.sigmoid(argument)
    return sigmoid_v * (1.0 + argument * (1.0 - sigmoid_v))


def shards(
    tokens, in_weight, gate_branch, conv_weight, out_weight, target, lang_ids, lang_weight, doc_pos
):
    row_count = tokens.shape[0]
    inner_width = gate_branch.shape[1]
    margin = CONV - 1
    moves_tokens = (
        row_count * lax.axis_size("row") < tokens.shape[1]
        and lax.axis_size("row") % lax.axis_size("col") == 0
    )
    if moves_tokens:
        inner_x = ring_reduce_scatter(fetched_columns(tokens), in_weight, "row", chains=4)
    else:
        full_in = lax.all_gather(in_weight, "row", axis=0, tiled=True)
        inner_x = jnp.dot(tokens, full_in, preferred_element_type=jnp.float32).astype(jnp.bfloat16)
    from_prev = passed_along(inner_x[row_count - margin :], "row", 1)
    extended = jnp.concatenate([from_prev, inner_x], axis=0).astype(jnp.float32)
    conv_sum = jnp.zeros((row_count, inner_width), jnp.float32)
    for offset in range(CONV):
        keep_mask = (doc_pos >= offset).astype(jnp.float32)[:, None]
        conv_sum = (
            conv_sum
            + conv_weight[offset][None, :]
            * extended[margin - offset : margin - offset + row_count]
            * keep_mask
        )
    gate_value = gate_branch.astype(jnp.float32)
    gate_act = jax.nn.silu(gate_value)
    conv_act = jax.nn.silu(conv_sum)
    mixed = (conv_act * gate_act).astype(jnp.bfloat16)
    partial_value = jnp.dot(mixed, out_weight, preferred_element_type=jnp.float32)
    columns = tokens.shape[1] // lax.axis_size("col")
    col_start = lax.axis_index("col") * columns
    lang_table = (lang_ids[:, None] == jnp.arange(LANGS, dtype=jnp.int32)[None, :]).astype(
        jnp.float32
    )
    token_weight = jnp.sum(lang_table * lang_weight[None, :], axis=1)[:, None]
    if moves_tokens and lax.axis_size("col") == 4:
        out_total = col_psum(partial_value.astype(jnp.bfloat16))
    else:
        out_total = lax.psum(partial_value.astype(jnp.bfloat16), "col").astype(jnp.float32)
    out_block = lax.dynamic_slice_in_dim(out_total, col_start, columns, 1)
    residual_grad = (token_weight * (out_total - target.astype(jnp.float32))).astype(jnp.bfloat16)
    grad_mixed = lax.dot_general(
        residual_grad, out_weight, (((1,), (1,)), ((), ())), preferred_element_type=jnp.float32
    )
    grad_conv = grad_mixed * gate_act * silu_grad(conv_sum)
    grad_gate = (grad_mixed * conv_act * silu_grad(gate_value)).astype(jnp.bfloat16)
    local_grad = conv_weight[0][None, :] * grad_conv
    spill_over = jnp.zeros((margin, inner_width), jnp.float32)
    for offset in range(1, CONV):
        masked = (
            conv_weight[offset][None, :]
            * grad_conv
            * (doc_pos >= offset).astype(jnp.float32)[:, None]
        )
        local_grad = local_grad + jnp.concatenate(
            [masked[offset:], jnp.zeros((offset, inner_width), jnp.float32)], axis=0
        )
        spill_over = spill_over + jnp.concatenate(
            [jnp.zeros((margin - offset, inner_width), jnp.float32), masked[:offset]], axis=0
        )
    from_next = passed_along(spill_over, "row", -1)
    grad_x = (
        local_grad
        + jnp.concatenate(
            [jnp.zeros((row_count - margin, inner_width), jnp.float32), from_next], axis=0
        )
    ).astype(jnp.bfloat16)
    if moves_tokens:
        stacks, sources = ring_gather(grad_x, "row")
        contract = (((2,), (1,)), ((), ()))
        weight_parts = jnp.split(in_weight, len(stacks), axis=1)
        grad_cols = lax.dot_general(
            stacks[0], weight_parts[0], contract, preferred_element_type=jnp.float32
        )
        for stack, weight_part in zip(stacks[1:], weight_parts[1:]):
            grad_cols = grad_cols + lax.dot_general(
                stack, weight_part, contract, preferred_element_type=jnp.float32
            )
        grad_cols = jnp.take(grad_cols.astype(jnp.bfloat16), jnp.argsort(sources), axis=0)
        grad_cols = grad_cols.reshape(-1, grad_cols.shape[2])
        if lax.axis_size("col") == 4 and lax.axis_size("row") == 8:
            grad_tokens = placed_sums(grad_cols, row_count)
        else:
            grad_sum = lax.psum_scatter(grad_cols, "col", scatter_dimension=0, tiled=True)
            grad_tokens = placed_blocks(grad_sum, row_count)
    else:
        partial_grad = lax.dot_general(
            grad_x, full_in, (((1,), (1,)), ((), ())), preferred_element_type=jnp.float32
        )
        grad_tokens = lax.psum_scatter(
            partial_grad.astype(jnp.bfloat16), "col", scatter_dimension=1, tiled=True
        )
    return (out_block.astype(jnp.bfloat16), grad_tokens, grad_gate)


def solution(mesh):
    in_specs = (
        P("row", None),
        P("row", "col"),
        P("row", "col"),
        P(None, "col"),
        P("col", None),
        P("row", None),
        P("row"),
        P(),
        P("row"),
    )
    out_specs = (P("row", "col"), P("row", "col"), P("row", "col"))
    return jax.shard_map(shards, mesh=mesh, in_specs=in_specs, out_specs=out_specs, check_vma=False)
```
